32 devices in a mesh: groups: 2 (over y), ctx: 4 (over x, core), head: 4 (over z).
Axes of the slice: x: 2, y: 2, z: 4, core: 2. Of those that a mesh axis runs over, the one named last changes fastest.
Arguments:
- span_query: bfloat16 [4, 128, 64, 128], P('groups', 'ctx', 'head'), parts along dimension 0, may hold values from -5 to 5
- span_key: bfloat16 [4, 128, 8, 128], P('groups', 'ctx', 'head'), parts along dimension 0, may hold values from -15 to 15
- span_value: bfloat16 [4, 128, 8, 128], P('groups', 'ctx', 'head'), parts along dimension 0, may hold values from -6 to 6
- prefix_key: bfloat16 [64, 128, 8, 128], P(('groups', 'ctx'), None, 'head'), parts along dimension 0, may hold values from -15 to 15
- prefix_value: bfloat16 [64, 128, 8, 128], P(('groups', 'ctx'), None, 'head'), parts along dimension 0, may hold values from -6 to 6
- page_table: int32 [4, 16], P('groups', 'ctx'), parts along dimension 0, may hold values from 0 to 7, as said below
- decode_query: bfloat16 [8, 32, 64, 128], P('groups', 'ctx', 'head'), parts along dimension 0, may hold values from -5 to 5
- decode_key: bfloat16 [8, 32, 8, 128], P('groups', 'ctx', 'head'), parts along dimension 0, may hold values from -15 to 15
- decode_value: bfloat16 [8, 32, 8, 128], P('groups', 'ctx', 'head'), parts along dimension 0, may hold values from -6 to 6
- sample_prompt: int32 [64], P('groups'), parts along dimension 0, may hold values from 0 to 1, as said below
- out_weight: bfloat16 [8192, 8192], P('head', 'ctx'), may hold values from -0.25 to 0.25
Outputs:
- span_out: bfloat16 [4, 128, 8192], P('groups', None, 'ctx'), parts along dimension 0
- decode_out: bfloat16 [8, 32, 8192], P('groups', None, 'ctx'), parts along dimension 0
The draws below stay inside these ranges and needn't reach their ends.
There are 2 independent parts, one for each index of `groups`. The reference program is written for one: setup_inputs(seed, part) draws one part's arguments, and reference() takes and returns one part's arrays. A program takes and returns all parts, laid end to end along the dimension named above; an argument that names none is the same for every part. Nothing has to cross between parts.
Inputs may be any that keep to these rules, and one draw needn't show every extreme that they name: `page_table`: within each block of 4 columns (one index of ctx) the entries of both prompts together are a permutation of 0 to 7. `sample_prompt`: every prompt has exactly 16 samples.
All inputs are finite; a program needn't handle non-finite values.
Results may differ from the reference program's by a relative error of at most 0.0075.
Values may be sent and summed in bfloat16 or wider, within the bound.
No kernel may reach another device: no remote copies, remote signals or barrier semaphores. Data moves between devices by JAX's collectives and lax.ppermute only.
A program may use at most 64 MiB of HBM per device.

```python
import jax
import jax.numpy as jnp
from jax import lax

D = 8192
HQ = 64
KVH = 8
HD = 128
PROMPTS = 2
STEPS = 4
PAGE = 128
PAGES_DEV = 4
SPAN = 128
PAGES = 16
PREFIX = 2048
SLOTS = 32
SAMPLES = 32


def base_rows(key, dims):
    return jnp.clip(jax.random.normal(key, dims, jnp.float32), -4.0, 4.0)


def drawn_keys(key, drawn, lead_one, lead_two, salt):
    summed = drawn.reshape(lead_one, lead_two, KVH, HQ // KVH, HD).sum(axis=3)
    jitter = jax.random.normal(jax.random.fold_in(key, salt), (lead_one, lead_two, KVH, HD), jnp.float32)
    return jnp.clip(0.9 * summed + jitter, -15.0, 15.0)


def draw_span_query(key, part):
    drawn = base_rows(jax.random.fold_in(key, 101), (PROMPTS, SPAN, HQ, HD))
    return drawn.astype(jnp.bfloat16)


def draw_span_key(key, part):
    drawn = base_rows(jax.random.fold_in(key, 101), (PROMPTS, SPAN, HQ, HD))
    return drawn_keys(key, drawn, PROMPTS, SPAN, 102).astype(jnp.bfloat16)


def draw_decode_query(key, part):
    drawn = base_rows(jax.random.fold_in(key, 201), (STEPS, SAMPLES, HQ, HD))
    return drawn.astype(jnp.bfloat16)


def draw_decode_key(key, part):
    drawn = base_rows(jax.random.fold_in(key, 201), (STEPS, SAMPLES, HQ, HD))
    return drawn_keys(key, drawn, STEPS, SAMPLES, 202).astype(jnp.bfloat16)


def draw_prefix_key(key, part):
    dims = (SLOTS, PAGE, KVH, HD)
    drawn = jnp.clip(2.5 * jax.random.normal(jax.random.fold_in(key, 501), dims, jnp.float32), -15.0, 15.0)
    return drawn.astype(jnp.bfloat16)


def draw_page_table(key, part):
    shards = PAGES // PAGES_DEV

    def one_shard(shard_id):
        return jax.random.permutation(jax.random.fold_in(key, shard_id + 301), PROMPTS * PAGES_DEV).reshape(PROMPTS, PAGES_DEV)
    blocks = jax.vmap(one_shard)(jnp.arange(shards))
    return blocks.transpose(1, 0, 2).reshape(PROMPTS, PAGES).astype(jnp.int32)


def draw_sample_prompt(key, part):
    return (jax.random.permutation(jax.random.fold_in(key, 401), SAMPLES) % PROMPTS).astype(jnp.int32)


def block_scale(stream_key, shape, pieces, smallest, largest):
    level, own = 1.0, jax.random.fold_in(stream_key, 6)
    for dim, parts in pieces:
        draws = jnp.exp(jax.random.uniform(jax.random.fold_in(own, dim), (parts,), jnp.float32, smallest / len(pieces), largest / len(pieces)))
        level = level * jnp.repeat(draws, shape[dim] // parts).reshape([-1 if axis == dim else 1 for axis in range(len(shape))])
    return level


def bell_draw(stream_key, shape, width, limit, pieces=(), kind=jnp.bfloat16):
    values = width * jax.random.normal(stream_key, shape, jnp.float32)
    if pieces:
        values = values * block_scale(stream_key, shape, pieces, -0.22, 0.18)
    return jnp.clip(values, -limit, limit).astype(kind)


def setup_inputs(seed: int = 0, part: int = 0) -> dict:
    key_list = jax.random.split(jax.random.key(seed), 12)
    part_splits = jax.random.split(jax.random.fold_in(key_list[11], part), 12)
    span_query = draw_span_query(jax.random.fold_in(jax.random.fold_in(key_list[11], part), 71), part)
    span_key = draw_span_key(jax.random.fold_in(jax.random.fold_in(key_list[11], part), 71), part)
    span_value = bell_draw(part_splits[2], (PROMPTS, SPAN, KVH, HD), 1.0, 6.0, ((1, 4), (2, 4)))
    prefix_key = draw_prefix_key(jax.random.fold_in(jax.random.fold_in(key_list[11], part), 71), part)
    prefix_value = bell_draw(part_splits[4], (SLOTS, PAGE, KVH, HD), 1.0, 6.0, ((0, 4), (2, 4)))
    page_table = draw_page_table(jax.random.fold_in(jax.random.fold_in(key_list[11], part), 71), part)
    decode_query = draw_decode_query(jax.random.fold_in(jax.random.fold_in(key_list[11], part), 71), part)
    decode_key = draw_decode_key(jax.random.fold_in(jax.random.fold_in(key_list[11], part), 71), part)
    decode_value = bell_draw(part_splits[8], (STEPS, SAMPLES, KVH, HD), 1.0, 6.0, ((1, 4), (2, 4)))
    sample_prompt = draw_sample_prompt(jax.random.fold_in(jax.random.fold_in(key_list[11], part), 71), part)
    out_weight = bell_draw(key_list[10], (HQ * HD, D), (HQ * HD // 16) ** -0.5, 0.25, ((0, 4), (1, 4)))
    return dict(span_query=span_query, span_key=span_key, span_value=span_value, prefix_key=prefix_key, prefix_value=prefix_value, page_table=page_table, decode_query=decode_query, decode_key=decode_key, decode_value=decode_value, sample_prompt=sample_prompt, out_weight=out_weight)


negative_floor = -1e30


def softmax_rows(scores, allowed, values_here):
    masked = jnp.where(allowed, scores, negative_floor)
    row_max = jnp.max(masked, axis=-1, keepdims=True)
    weights = jnp.exp(masked - row_max)
    weight_sum = jnp.sum(weights, axis=-1, keepdims=True)
    mixed_rows = jnp.dot(weights.astype(jnp.bfloat16), values_here, preferred_element_type=jnp.float32)
    return mixed_rows / weight_sum


def reference(span_query, span_key, span_value, prefix_key, prefix_value, page_table, decode_query, decode_key, decode_value, sample_prompt, out_weight):
    group_size = HQ // KVH
    score_scale = 1.0 / (HD ** 0.5)
    page_index = jnp.arange(PAGES, dtype=jnp.int32)
    slot_index = (page_index // PAGES_DEV * (PROMPTS * PAGES_DEV))[None, :] + page_table
    flat_slots = slot_index.reshape(-1).astype(jnp.int32)
    prompt_keys = jnp.take(prefix_key, flat_slots, axis=0).reshape(PROMPTS, PREFIX, KVH, HD)
    prompt_values = jnp.take(prefix_value, flat_slots, axis=0).reshape(PROMPTS, PREFIX, KVH, HD)
    all_keys = jnp.concatenate([prompt_keys, span_key], axis=1)
    all_values = jnp.concatenate([prompt_values, span_value], axis=1)
    length = PREFIX + SPAN
    key_pos = jnp.arange(length, dtype=jnp.int32)

    head_keys = all_keys.transpose(0, 2, 1, 3).reshape(PROMPTS * KVH, length, HD)
    head_values = all_values.transpose(0, 2, 1, 3).reshape(PROMPTS * KVH, length, HD)
    head_queries = span_query.reshape(PROMPTS, SPAN, KVH, group_size, HD).transpose(0, 2, 1, 3, 4).reshape(PROMPTS * KVH, SPAN * group_size, HD)
    query_pos = jnp.arange(SPAN * group_size, dtype=jnp.int32) // group_size
    allowed = (key_pos[None, :] < PREFIX) | (key_pos[None, :] - PREFIX <= query_pos[:, None])

    def prefill_head(operands):
        queries, keys_here, values_here = operands
        scores = jnp.dot(queries, keys_here.T, preferred_element_type=jnp.float32) * score_scale
        return softmax_rows(scores, allowed, values_here).astype(jnp.bfloat16)

    mixed_heads = lax.map(prefill_head, (head_queries, head_keys, head_values))
    span_attn = mixed_heads.reshape(PROMPTS, KVH, SPAN, group_size, HD).transpose(0, 2, 1, 3, 4).reshape(PROMPTS * SPAN, HQ * HD)

    step_pos = jnp.arange(STEPS * group_size, dtype=jnp.int32) // group_size
    own_allowed = jnp.concatenate([jnp.ones((STEPS * group_size, length), dtype=bool), jnp.arange(STEPS, dtype=jnp.int32)[None, :] <= step_pos[:, None]], axis=1)

    def decode_sample(operands):
        queries, own_keys, own_values, prompt = operands
        keys_here = jnp.concatenate([lax.dynamic_index_in_dim(all_keys, prompt, 0, keepdims=False), own_keys], axis=0)
        values_here = jnp.concatenate([lax.dynamic_index_in_dim(all_values, prompt, 0, keepdims=False), own_values], axis=0)
        grouped = queries.reshape(STEPS, KVH, group_size, HD).transpose(1, 0, 2, 3).reshape(KVH, STEPS * group_size, HD)

        def decode_head(inner_ops):
            one_queries, one_keys, one_values = inner_ops
            scores = jnp.dot(one_queries, one_keys.T, preferred_element_type=jnp.float32) * score_scale
            return softmax_rows(scores, own_allowed, one_values).astype(jnp.bfloat16)

        result = lax.map(decode_head, (grouped, keys_here.transpose(1, 0, 2), values_here.transpose(1, 0, 2)))
        return result.reshape(KVH, STEPS, group_size, HD).transpose(1, 0, 2, 3).reshape(STEPS, HQ * HD)

    decoded = lax.map(decode_sample, (decode_query.transpose(1, 0, 2, 3), decode_key.transpose(1, 0, 2, 3), decode_value.transpose(1, 0, 2, 3), sample_prompt))
    decode_attn = decoded.transpose(1, 0, 2).reshape(STEPS * SAMPLES, HQ * HD)
    span_out = jnp.dot(span_attn, out_weight, preferred_element_type=jnp.float32).astype(jnp.bfloat16).reshape(PROMPTS, SPAN, D)
    decode_out = jnp.dot(decode_attn, out_weight, preferred_element_type=jnp.float32).astype(jnp.bfloat16).reshape(STEPS, SAMPLES, D)
    return span_out, decode_out
```

```python
import math

import jax
import jax.numpy as jnp
from jax import lax
from jax.sharding import PartitionSpec as P

negative_floor = -1e30


def absorb(softmax_state, queries, key_rows, value_rows, allowed):
    running_max, running_sum, weighted = softmax_state
    scores = jnp.einsum("brd,bnd->brn", queries, key_rows, preferred_element_type=jnp.float32) * (
        1.0 / math.sqrt(queries.shape[-1])
    )
    if allowed is not None:
        scores = jnp.where(allowed, scores, negative_floor)
    new_max = jnp.maximum(running_max, jnp.max(scores, axis=-1))
    factor = jnp.exp(running_max - new_max)
    weights = jnp.exp(scores - new_max[..., None])
    running_sum = running_sum * factor + jnp.sum(weights, axis=-1)
    weighted = weighted * factor[..., None] + jnp.einsum(
        "brn,bnd->brd", weights.astype(jnp.bfloat16), value_rows, preferred_element_type=jnp.float32
    )
    return (new_max, running_sum, weighted)


def sweep(softmax_state, queries, key_rows, value_rows, block_width):
    total_keys = key_rows.shape[1]
    block_width = math.gcd(total_keys, block_width)

    def one_block(state_in, block_start):
        key_block = lax.dynamic_slice_in_dim(key_rows, block_start, block_width, 1)
        value_block = lax.dynamic_slice_in_dim(value_rows, block_start, block_width, 1)
        return (absorb(state_in, queries, key_block, value_block, None), None)

    starts = jnp.arange(total_keys // block_width, dtype=jnp.int32) * block_width
    softmax_state, unused = lax.scan(one_block, softmax_state, starts)
    return softmax_state


def empty_state(head_batch, row_count, head_depth):
    return (
        jnp.full((head_batch, row_count), negative_floor, jnp.float32),
        jnp.zeros((head_batch, row_count), jnp.float32),
        jnp.zeros((head_batch, row_count, head_depth), jnp.float32),
    )


def own_steps(softmax_state, queries_five, own_key, own_value):
    running_max, running_sum, weighted = softmax_state
    key_rows = own_key.transpose(2, 1, 0, 3)
    value_rows = own_value.transpose(2, 1, 0, 3)
    scores = jnp.einsum(
        "ktsgd,ksud->ktsgu", queries_five, key_rows, preferred_element_type=jnp.float32
    ) * (1.0 / math.sqrt(queries_five.shape[-1]))
    step_total = queries_five.shape[1]
    step_ids = jnp.arange(step_total, dtype=jnp.int32)
    allowed = (step_ids[None, :] <= step_ids[:, None])[None, :, None, None, :]
    scores = jnp.where(allowed, scores, negative_floor)
    new_max = jnp.maximum(running_max, jnp.max(scores, axis=-1))
    factor = jnp.exp(running_max - new_max)
    weights = jnp.exp(scores - new_max[..., None])
    running_sum = running_sum * factor + jnp.sum(weights, axis=-1)
    weighted = weighted * factor[..., None] + jnp.einsum(
        "ktsgu,ksud->ktsgd",
        weights.astype(jnp.bfloat16),
        value_rows,
        preferred_element_type=jnp.float32,
    )
    return (weighted / running_sum[..., None]).astype(jnp.bfloat16)


def shards(
    span_query,
    span_key,
    span_value,
    prefix_key,
    prefix_value,
    page_table,
    decode_query,
    decode_key,
    decode_value,
    sample_prompt,
    out_weight,
):
    prompts, span_dev, heads_dev, head_depth = span_query.shape
    kv_heads = span_key.shape[2]
    group_size = heads_dev // kv_heads
    steps_count = decode_query.shape[0]
    samples_dev = decode_query.shape[1]
    head_batch = prompts * kv_heads
    ctx_index = lax.axis_index("ctx")
    slot_rows = page_table.reshape(-1)
    local_keys = (
        jnp.take(prefix_key, slot_rows, axis=0)
        .reshape(prompts, -1, kv_heads, head_depth)
        .transpose(0, 2, 1, 3)
    )
    local_values = (
        jnp.take(prefix_value, slot_rows, axis=0)
        .reshape(prompts, -1, kv_heads, head_depth)
        .transpose(0, 2, 1, 3)
    )
    span_rows = (
        span_query.reshape(prompts, span_dev, kv_heads, group_size, head_depth)
        .transpose(0, 2, 1, 3, 4)
        .reshape(head_batch, span_dev * group_size, head_depth)
    )
    span_keys_all, span_values_all = (
        lax.all_gather(span_key, "ctx", axis=1, tiled=True),
        lax.all_gather(span_value, "ctx", axis=1, tiled=True),
    )
    span_total = span_keys_all.shape[1]
    span_key_rows = span_keys_all.transpose(0, 2, 1, 3).reshape(head_batch, span_total, head_depth)
    span_value_rows = span_values_all.transpose(0, 2, 1, 3).reshape(
        head_batch, span_total, head_depth
    )
    query_pos = (
        ctx_index * span_dev + jnp.arange(span_dev * group_size, dtype=jnp.int32) // group_size
    )
    causal = (jnp.arange(span_total, dtype=jnp.int32)[None, :] <= query_pos[:, None])[None]
    decode_five = decode_query.reshape(
        steps_count, samples_dev, kv_heads, group_size, head_depth
    ).transpose(2, 0, 1, 3, 4)
    prefill_state = empty_state(head_batch, span_dev * group_size, head_depth)
    prompt_keys_all, prompt_values_all = (
        lax.all_gather(local_keys, "ctx", axis=2, tiled=True),
        lax.all_gather(local_values, "ctx", axis=2, tiled=True),
    )
    prefix_len = prompt_keys_all.shape[2]
    key_rows = prompt_keys_all.reshape(head_batch, prefix_len, head_depth)
    value_rows = prompt_values_all.reshape(head_batch, prefix_len, head_depth)
    prefill_state = sweep(prefill_state, span_rows, key_rows, value_rows, 2048)
    decode_flat = decode_five.reshape(kv_heads, -1, head_depth)
    decode_batch = jnp.broadcast_to(decode_flat[None], (prompts,) + decode_flat.shape).reshape(
        head_batch, -1, head_depth
    )
    decode_state = empty_state(head_batch, decode_flat.shape[1], head_depth)
    decode_state = sweep(decode_state, decode_batch, key_rows, value_rows, 2048)
    decode_state = sweep(decode_state, decode_batch, span_key_rows, span_value_rows, span_total)
    own_prompts = lax.dynamic_slice_in_dim(sample_prompt, ctx_index * samples_dev, samples_dev)
    chosen = (
        own_prompts[None, None, None, :, None]
        == jnp.arange(prompts, dtype=jnp.int32)[:, None, None, None, None]
    )

    def select_prompt(member):
        shaped = member.reshape(
            (prompts, kv_heads, steps_count, samples_dev, group_size) + member.shape[2:]
        )
        select_mask = chosen.reshape(chosen.shape + (1,) * (shaped.ndim - 5))
        return jnp.sum(jnp.where(select_mask, shaped, 0.0), axis=0)

    decode_state = tuple((select_prompt(member) for member in decode_state))
    prefill_state = absorb(prefill_state, span_rows, span_key_rows, span_value_rows, causal)
    span_mixed = (prefill_state[2] / prefill_state[1][..., None]).astype(jnp.bfloat16)
    span_attn = (
        span_mixed.reshape(prompts, kv_heads, span_dev, group_size, head_depth)
        .transpose(0, 2, 1, 3, 4)
        .reshape(prompts * span_dev, heads_dev * head_depth)
    )
    decode_mixed = own_steps(decode_state, decode_five, decode_key, decode_value)
    decode_attn = decode_mixed.transpose(1, 2, 0, 3, 4).reshape(
        steps_count * samples_dev, heads_dev * head_depth
    )
    rows_local = jnp.concatenate([span_attn, decode_attn], axis=0)
    projected = jnp.dot(
        lax.all_gather(rows_local, "ctx", axis=0, tiled=True),
        out_weight,
        preferred_element_type=jnp.float32,
    )
    share = lax.psum_scatter(
        projected.astype(jnp.bfloat16), "head", scatter_dimension=0, tiled=True
    )
    summed = lax.all_gather(share, "head", axis=0, tiled=True)
    rows_dev = rows_local.shape[0]
    blocks_by_ctx = summed.reshape(-1, rows_dev, summed.shape[-1])
    ctx_count = blocks_by_ctx.shape[0]
    span_out = (
        blocks_by_ctx[:, : prompts * span_dev]
        .reshape(ctx_count, prompts, span_dev, -1)
        .transpose(1, 0, 2, 3)
        .reshape(prompts, ctx_count * span_dev, -1)
    )
    decode_out = (
        blocks_by_ctx[:, prompts * span_dev :]
        .reshape(ctx_count, steps_count, samples_dev, -1)
        .transpose(1, 0, 2, 3)
        .reshape(steps_count, ctx_count * samples_dev, -1)
    )
    return (span_out, decode_out)


def solution(mesh):
    return jax.shard_map(
        shards,
        mesh=mesh,
        in_specs=(
            P("groups", "ctx", "head", None),
            P("groups", "ctx", "head", None),
            P("groups", "ctx", "head", None),
            P(("groups", "ctx"), None, "head", None),
            P(("groups", "ctx"), None, "head", None),
            P("groups", "ctx"),
            P("groups", "ctx", "head", None),
            P("groups", "ctx", "head", None),
            P("groups", "ctx", "head", None),
            P("groups"),
            P("head", "ctx"),
        ),
        out_specs=(P("groups", None, "ctx"), P("groups", None, "ctx")),
        check_vma=False,
    )
```

```python
import math

import jax
import jax.numpy as jnp
from jax import lax
from jax.sharding import PartitionSpec as P

negative_floor = -1e30


def absorb(softmax_state, queries, key_rows, value_rows, allowed):
    running_max, running_sum, weighted = softmax_state
    scores = jnp.einsum("brd,bnd->brn", queries, key_rows, preferred_element_type=jnp.float32) * (
        1.0 / math.sqrt(queries.shape[-1])
    )
    if allowed is not None:
        scores = jnp.where(allowed, scores, negative_floor)
    new_max = jnp.maximum(running_max, jnp.max(scores, axis=-1))
    factor = jnp.exp(running_max - new_max)
    weights = jnp.exp(scores - new_max[..., None])
    running_sum = running_sum * factor + jnp.sum(weights, axis=-1)
    weighted = weighted * factor[..., None] + jnp.einsum(
        "brn,bnd->brd", weights.astype(jnp.bfloat16), value_rows, preferred_element_type=jnp.float32
    )
    return (new_max, running_sum, weighted)


def sweep(softmax_state, queries, key_rows, value_rows, block_width):
    total_keys = key_rows.shape[1]
    block_width = math.gcd(total_keys, block_width)

    def one_block(state_in, block_start):
        key_block = lax.dynamic_slice_in_dim(key_rows, block_start, block_width, 1)
        value_block = lax.dynamic_slice_in_dim(value_rows, block_start, block_width, 1)
        return (absorb(state_in, queries, key_block, value_block, None), None)

    starts = jnp.arange(total_keys // block_width, dtype=jnp.int32) * block_width
    softmax_state, unused = lax.scan(one_block, softmax_state, starts)
    return softmax_state


def empty_state(head_batch, row_count, head_depth):
    return (
        jnp.full((head_batch, row_count), negative_floor, jnp.float32),
        jnp.zeros((head_batch, row_count), jnp.float32),
        jnp.zeros((head_batch, row_count, head_depth), jnp.float32),
    )


def own_steps(softmax_state, queries_five, own_key, own_value):
    running_max, running_sum, weighted = softmax_state
    key_rows = own_key.transpose(2, 1, 0, 3)
    value_rows = own_value.transpose(2, 1, 0, 3)
    scores = jnp.einsum(
        "ktsgd,ksud->ktsgu", queries_five, key_rows, preferred_element_type=jnp.float32
    ) * (1.0 / math.sqrt(queries_five.shape[-1]))
    step_total = queries_five.shape[1]
    step_ids = jnp.arange(step_total, dtype=jnp.int32)
    allowed = (step_ids[None, :] <= step_ids[:, None])[None, :, None, None, :]
    scores = jnp.where(allowed, scores, negative_floor)
    new_max = jnp.maximum(running_max, jnp.max(scores, axis=-1))
    factor = jnp.exp(running_max - new_max)
    weights = jnp.exp(scores - new_max[..., None])
    running_sum = running_sum * factor + jnp.sum(weights, axis=-1)
    weighted = weighted * factor[..., None] + jnp.einsum(
        "ktsgu,ksud->ktsgd",
        weights.astype(jnp.bfloat16),
        value_rows,
        preferred_element_type=jnp.float32,
    )
    return (weighted / running_sum[..., None]).astype(jnp.bfloat16)


def ctx_shards(block, ctx_count):
    chips = ctx_count // 2
    received = [block]
    for shift in range(1, chips):
        pairs = [(dev, (dev - 2 * shift) % ctx_count) for dev in range(ctx_count)]
        received.append(lax.ppermute(block, "ctx", pairs))
    along_x = jnp.stack(received)
    other_core = lax.ppermute(along_x, "ctx", [(dev, dev ^ 1) for dev in range(ctx_count)])
    return along_x, other_core


def ctx_gather(block, ctx_count):
    ctx_index = lax.axis_index("ctx")
    chip, core = ctx_index // 2, ctx_index % 2
    along_x, other_core = ctx_shards(block, ctx_count)
    along_x = jnp.roll(along_x, chip, axis=0)
    other_core = jnp.roll(other_core, chip, axis=0)
    core_zero = jnp.where(core == 0, along_x, other_core)
    core_one = jnp.where(core == 0, other_core, along_x)
    return jnp.stack([core_zero, core_one], axis=1).reshape((ctx_count,) + block.shape)


def shards(
    span_query,
    span_key,
    span_value,
    prefix_key,
    prefix_value,
    page_table,
    decode_query,
    decode_key,
    decode_value,
    sample_prompt,
    out_weight,
):
    prompts, span_dev, heads_dev, head_depth = span_query.shape
    kv_heads = span_key.shape[2]
    group_size = heads_dev // kv_heads
    steps_count = decode_query.shape[0]
    samples_dev = decode_query.shape[1]
    head_batch = prompts * kv_heads
    ctx_index = lax.axis_index("ctx")
    slot_rows = page_table.reshape(-1)
    local_keys = (
        jnp.take(prefix_key, slot_rows, axis=0)
        .reshape(prompts, -1, kv_heads, head_depth)
        .transpose(0, 2, 1, 3)
    )
    local_values = (
        jnp.take(prefix_value, slot_rows, axis=0)
        .reshape(prompts, -1, kv_heads, head_depth)
        .transpose(0, 2, 1, 3)
    )
    span_rows = (
        span_query.reshape(prompts, span_dev, kv_heads, group_size, head_depth)
        .transpose(0, 2, 1, 3, 4)
        .reshape(head_batch, span_dev * group_size, head_depth)
    )
    ctx_count = sample_prompt.shape[0] // samples_dev
    span_pair = ctx_gather(jnp.stack([span_key, span_value]), ctx_count)
    span_keys_all, span_values_all = (
        span_pair[:, member].transpose(1, 0, 2, 3, 4).reshape(
            (prompts, ctx_count * span_dev) + span_key.shape[2:]
        )
        for member in range(2)
    )
    span_total = span_keys_all.shape[1]
    span_key_rows = span_keys_all.transpose(0, 2, 1, 3).reshape(head_batch, span_total, head_depth)
    span_value_rows = span_values_all.transpose(0, 2, 1, 3).reshape(
        head_batch, span_total, head_depth
    )
    query_pos = (
        ctx_index * span_dev + jnp.arange(span_dev * group_size, dtype=jnp.int32) // group_size
    )
    causal = (jnp.arange(span_total, dtype=jnp.int32)[None, :] <= query_pos[:, None])[None]
    decode_five = decode_query.reshape(
        steps_count, samples_dev, kv_heads, group_size, head_depth
    ).transpose(2, 0, 1, 3, 4)
    prefill_state = empty_state(head_batch, span_dev * group_size, head_depth)
    along_x, other_core = ctx_shards(jnp.stack([local_keys, local_values]), ctx_count)
    arrived = jnp.concatenate([along_x, other_core], axis=0)
    prompt_keys_all, prompt_values_all = (
        jnp.concatenate([arrived[shard, member] for shard in range(ctx_count)], axis=2)
        for member in range(2)
    )
    prefix_len = prompt_keys_all.shape[2]
    key_rows = prompt_keys_all.reshape(head_batch, prefix_len, head_depth)
    value_rows = prompt_values_all.reshape(head_batch, prefix_len, head_depth)
    prefill_state = sweep(prefill_state, span_rows, key_rows, value_rows, 2048)
    decode_flat = decode_five.reshape(kv_heads, -1, head_depth)
    decode_batch = jnp.broadcast_to(decode_flat[None], (prompts,) + decode_flat.shape).reshape(
        head_batch, -1, head_depth
    )
    decode_state = empty_state(head_batch, decode_flat.shape[1], head_depth)
    decode_state = sweep(decode_state, decode_batch, key_rows, value_rows, 2048)
    decode_state = sweep(decode_state, decode_batch, span_key_rows, span_value_rows, span_total)
    own_prompts = lax.dynamic_slice_in_dim(sample_prompt, ctx_index * samples_dev, samples_dev)
    chosen = (
        own_prompts[None, None, None, :, None]
        == jnp.arange(prompts, dtype=jnp.int32)[:, None, None, None, None]
    )

    def select_prompt(member):
        shaped = member.reshape(
            (prompts, kv_heads, steps_count, samples_dev, group_size) + member.shape[2:]
        )
        select_mask = chosen.reshape(chosen.shape + (1,) * (shaped.ndim - 5))
        return jnp.sum(jnp.where(select_mask, shaped, 0.0), axis=0)

    decode_state = tuple((select_prompt(member) for member in decode_state))
    prefill_state = absorb(prefill_state, span_rows, span_key_rows, span_value_rows, causal)
    span_mixed = (prefill_state[2] / prefill_state[1][..., None]).astype(jnp.bfloat16)
    span_attn = (
        span_mixed.reshape(prompts, kv_heads, span_dev, group_size, head_depth)
        .transpose(0, 2, 1, 3, 4)
        .reshape(prompts * span_dev, heads_dev * head_depth)
    )
    decode_mixed = own_steps(decode_state, decode_five, decode_key, decode_value)
    decode_attn = decode_mixed.transpose(1, 2, 0, 3, 4).reshape(
        steps_count * samples_dev, heads_dev * head_depth
    )
    rows_local = jnp.concatenate([span_attn, decode_attn], axis=0)
    projected = jnp.dot(
        ctx_gather(rows_local, ctx_count).reshape(-1, rows_local.shape[-1]),
        out_weight,
        preferred_element_type=jnp.float32,
    )
    share = lax.psum_scatter(
        projected.astype(jnp.bfloat16), "head", scatter_dimension=0, tiled=True
    )
    summed = lax.all_gather(share, "head", axis=0, tiled=True)
    rows_dev = rows_local.shape[0]
    blocks_by_ctx = summed.reshape(-1, rows_dev, summed.shape[-1])
    span_out = (
        blocks_by_ctx[:, : prompts * span_dev]
        .reshape(ctx_count, prompts, span_dev, -1)
        .transpose(1, 0, 2, 3)
        .reshape(prompts, ctx_count * span_dev, -1)
    )
    decode_out = (
        blocks_by_ctx[:, prompts * span_dev :]
        .reshape(ctx_count, steps_count, samples_dev, -1)
        .transpose(1, 0, 2, 3)
        .reshape(steps_count, ctx_count * samples_dev, -1)
    )
    return (span_out, decode_out)


def solution(mesh):
    return jax.shard_map(
        shards,
        mesh=mesh,
        in_specs=(
            P("groups", "ctx", "head", None),
            P("groups", "ctx", "head", None),
            P("groups", "ctx", "head", None),
            P(("groups", "ctx"), None, "head", None),
            P(("groups", "ctx"), None, "head", None),
            P("groups", "ctx"),
            P("groups", "ctx", "head", None),
            P("groups", "ctx", "head", None),
            P("groups", "ctx", "head", None),
            P("groups"),
            P("head", "ctx"),
        ),
        out_specs=(P("groups", None, "ctx"), P("groups", None, "ctx")),
        check_vma=False,
    )
```

```python
import functools
import math

import jax
import jax.numpy as jnp
from jax import lax
from jax.sharding import PartitionSpec as P

negative_floor = -1e30


def absorb(softmax_state, queries, key_rows, value_rows, allowed):
    running_max, running_sum, weighted = softmax_state
    scores = jnp.einsum("brd,bnd->brn", queries, key_rows, preferred_element_type=jnp.float32) * (
        1.0 / math.sqrt(queries.shape[-1])
    )
    if allowed is not None:
        scores = jnp.where(allowed, scores, negative_floor)
    new_max = jnp.maximum(running_max, jnp.max(scores, axis=-1))
    factor = jnp.exp(running_max - new_max)
    weights = jnp.exp(scores - new_max[..., None])
    running_sum = running_sum * factor + jnp.sum(weights, axis=-1)
    weighted = weighted * factor[..., None] + jnp.einsum(
        "brn,bnd->brd", weights.astype(jnp.bfloat16), value_rows, preferred_element_type=jnp.float32
    )
    return (new_max, running_sum, weighted)


def sweep(softmax_state, queries, key_rows, value_rows, block_width):
    total_keys = key_rows.shape[1]
    block_width = math.gcd(total_keys, block_width)

    def one_block(state_in, block_start):
        key_block = lax.dynamic_slice_in_dim(key_rows, block_start, block_width, 1)
        value_block = lax.dynamic_slice_in_dim(value_rows, block_start, block_width, 1)
        return (absorb(state_in, queries, key_block, value_block, None), None)

    starts = jnp.arange(total_keys // block_width, dtype=jnp.int32) * block_width
    softmax_state, unused = lax.scan(one_block, softmax_state, starts)
    return softmax_state


def empty_state(head_batch, row_count, head_depth):
    return (
        jnp.full((head_batch, row_count), negative_floor, jnp.float32),
        jnp.zeros((head_batch, row_count), jnp.float32),
        jnp.zeros((head_batch, row_count, head_depth), jnp.float32),
    )


def own_steps(softmax_state, queries_five, own_key, own_value):
    running_max, running_sum, weighted = softmax_state
    key_rows = own_key.transpose(2, 1, 0, 3)
    value_rows = own_value.transpose(2, 1, 0, 3)
    scores = jnp.einsum(
        "ktsgd,ksud->ktsgu", queries_five, key_rows, preferred_element_type=jnp.float32
    ) * (1.0 / math.sqrt(queries_five.shape[-1]))
    step_total = queries_five.shape[1]
    step_ids = jnp.arange(step_total, dtype=jnp.int32)
    allowed = (step_ids[None, :] <= step_ids[:, None])[None, :, None, None, :]
    scores = jnp.where(allowed, scores, negative_floor)
    new_max = jnp.maximum(running_max, jnp.max(scores, axis=-1))
    factor = jnp.exp(running_max - new_max)
    weights = jnp.exp(scores - new_max[..., None])
    running_sum = running_sum * factor + jnp.sum(weights, axis=-1)
    weighted = weighted * factor[..., None] + jnp.einsum(
        "ktsgu,ksud->ktsgd",
        weights.astype(jnp.bfloat16),
        value_rows,
        preferred_element_type=jnp.float32,
    )
    return (weighted / running_sum[..., None]).astype(jnp.bfloat16)


def ctx_shards(block, ctx_count):
    chips = ctx_count // 2
    received = [block]
    for shift in range(1, chips):
        pairs = [(dev, (dev - 2 * shift) % ctx_count) for dev in range(ctx_count)]
        received.append(lax.ppermute(block, "ctx", pairs))
    along_x = jnp.stack(received)
    other_core = lax.ppermute(along_x, "ctx", [(dev, dev ^ 1) for dev in range(ctx_count)])
    return along_x, other_core


def ctx_gather(block, ctx_count, axis=0):
    ctx_index = lax.axis_index("ctx")
    chip, core = ctx_index // 2, ctx_index % 2
    along_x, other_core = ctx_shards(block, ctx_count)
    along_x = jnp.roll(along_x, chip, axis=0)
    other_core = jnp.roll(other_core, chip, axis=0)
    core_zero = jnp.where(core == 0, along_x, other_core)
    core_one = jnp.where(core == 0, other_core, along_x)
    joined = jnp.moveaxis(jnp.stack([core_zero, core_one], axis=1), (0, 1), (axis, axis + 1))
    return joined.reshape(block.shape[:axis] + (-1,) + block.shape[axis + 1 :])


def project(rows, out_weight):
    flat = rows.reshape(-1, rows.shape[-1])
    return jnp.dot(flat, out_weight, preferred_element_type=jnp.float32).astype(jnp.bfloat16)


def head_sum_direct(partial, lead_shape, head_count):
    head_index = lax.axis_index("head")
    blocks = partial.reshape((head_count, -1) + partial.shape[1:])
    total = lax.dynamic_index_in_dim(blocks, head_index, 0, keepdims=False).astype(jnp.float32)
    for shift in range(1, head_count):
        outgoing = lax.dynamic_index_in_dim(blocks, (head_index + shift) % head_count, 0, False)
        pairs = [(dev, (dev + shift) % head_count) for dev in range(head_count)]
        total = total + lax.ppermute(outgoing, "head", pairs).astype(jnp.float32)
    mine = total.astype(jnp.bfloat16)
    received = [mine]
    for shift in range(1, head_count):
        pairs = [(dev, (dev - shift) % head_count) for dev in range(head_count)]
        received.append(lax.ppermute(mine, "head", pairs))
    ordered = jnp.roll(jnp.stack(received), head_index, axis=0)
    return ordered.reshape(lead_shape + (partial.shape[-1],))


def head_sum(partial, lead_shape):
    share = lax.psum_scatter(partial, "head", scatter_dimension=0, tiled=True)
    summed = lax.all_gather(share, "head", axis=0, tiled=True)
    return summed.reshape(lead_shape + (partial.shape[-1],))


def shards(
    span_query,
    span_key,
    span_value,
    prefix_key,
    prefix_value,
    page_table,
    decode_query,
    decode_key,
    decode_value,
    sample_prompt,
    out_weight,
    head_count,
):
    prompts, span_dev, heads_dev, head_depth = span_query.shape
    kv_heads = span_key.shape[2]
    group_size = heads_dev // kv_heads
    steps_count = decode_query.shape[0]
    samples_dev = decode_query.shape[1]
    head_batch = prompts * kv_heads
    ctx_index = lax.axis_index("ctx")
    slot_rows = page_table.reshape(-1)
    local_keys = (
        jnp.take(prefix_key, slot_rows, axis=0)
        .reshape(prompts, -1, kv_heads, head_depth)
        .transpose(0, 2, 1, 3)
    )
    local_values = (
        jnp.take(prefix_value, slot_rows, axis=0)
        .reshape(prompts, -1, kv_heads, head_depth)
        .transpose(0, 2, 1, 3)
    )
    span_rows = (
        span_query.reshape(prompts, span_dev, kv_heads, group_size, head_depth)
        .transpose(0, 2, 1, 3, 4)
        .reshape(head_batch, span_dev * group_size, head_depth)
    )
    ctx_count = sample_prompt.shape[0] // samples_dev
    span_pair = ctx_gather(jnp.stack([span_key, span_value]), ctx_count, axis=2)
    span_keys_all, span_values_all = span_pair[0], span_pair[1]
    span_total = span_keys_all.shape[1]
    span_key_rows = span_keys_all.transpose(0, 2, 1, 3).reshape(head_batch, span_total, head_depth)
    span_value_rows = span_values_all.transpose(0, 2, 1, 3).reshape(
        head_batch, span_total, head_depth
    )
    query_pos = (
        ctx_index * span_dev + jnp.arange(span_dev * group_size, dtype=jnp.int32) // group_size
    )
    causal = (jnp.arange(span_total, dtype=jnp.int32)[None, :] <= query_pos[:, None])[None]
    decode_five = decode_query.reshape(
        steps_count, samples_dev, kv_heads, group_size, head_depth
    ).transpose(2, 0, 1, 3, 4)
    prefill_state = empty_state(head_batch, span_dev * group_size, head_depth)
    along_x, other_core = ctx_shards(jnp.stack([local_keys, local_values]), ctx_count)
    arrived = jnp.concatenate([along_x, other_core], axis=0)
    prompt_keys_all, prompt_values_all = (
        jnp.concatenate([arrived[shard, member] for shard in range(ctx_count)], axis=2)
        for member in range(2)
    )
    prefix_len = prompt_keys_all.shape[2]
    key_rows = prompt_keys_all.reshape(head_batch, prefix_len, head_depth)
    value_rows = prompt_values_all.reshape(head_batch, prefix_len, head_depth)
    decode_flat = decode_five.reshape(kv_heads, -1, head_depth)
    decode_batch = jnp.broadcast_to(decode_flat[None], (prompts,) + decode_flat.shape).reshape(
        head_batch, -1, head_depth
    )
    decode_state = empty_state(head_batch, decode_flat.shape[1], head_depth)
    decode_state = sweep(decode_state, decode_batch, key_rows, value_rows, 2048)
    decode_state = sweep(decode_state, decode_batch, span_key_rows, span_value_rows, span_total)
    own_prompts = lax.dynamic_slice_in_dim(sample_prompt, ctx_index * samples_dev, samples_dev)
    chosen = (
        own_prompts[None, None, None, :, None]
        == jnp.arange(prompts, dtype=jnp.int32)[:, None, None, None, None]
    )

    def select_prompt(member):
        shaped = member.reshape(
            (prompts, kv_heads, steps_count, samples_dev, group_size) + member.shape[2:]
        )
        select_mask = chosen.reshape(chosen.shape + (1,) * (shaped.ndim - 5))
        return jnp.sum(jnp.where(select_mask, shaped, 0.0), axis=0)

    decode_state = tuple((select_prompt(member) for member in decode_state))
    decode_mixed = own_steps(decode_state, decode_five, decode_key, decode_value)
    decode_attn = decode_mixed.transpose(1, 2, 0, 3, 4).reshape(
        steps_count, samples_dev, heads_dev * head_depth
    )
    decode_rows = ctx_gather(decode_attn, ctx_count, axis=1)
    decode_partial = project(decode_rows, out_weight)
    decode_partial, span_rows, key_rows, value_rows, span_key_rows, span_value_rows = (
        lax.optimization_barrier(
            (decode_partial, span_rows, key_rows, value_rows, span_key_rows, span_value_rows)
        )
    )
    decode_out = head_sum_direct(decode_partial, decode_rows.shape[:-1], head_count)
    prefill_state = sweep(prefill_state, span_rows, key_rows, value_rows, 2048)
    prefill_state = absorb(prefill_state, span_rows, span_key_rows, span_value_rows, causal)
    span_mixed = (prefill_state[2] / prefill_state[1][..., None]).astype(jnp.bfloat16)
    span_attn = (
        span_mixed.reshape(prompts, kv_heads, span_dev, group_size, head_depth)
        .transpose(0, 2, 1, 3, 4)
        .reshape(prompts, span_dev, heads_dev * head_depth)
    )
    span_rows_all = ctx_gather(span_attn, ctx_count, axis=1)
    span_out = head_sum(project(span_rows_all, out_weight), span_rows_all.shape[:-1])
    return (span_out, decode_out)


def solution(mesh):
    return jax.shard_map(
        functools.partial(shards, head_count=mesh.shape["head"]),
        mesh=mesh,
        in_specs=(
            P("groups", "ctx", "head", None),
            P("groups", "ctx", "head", None),
            P("groups", "ctx", "head", None),
            P(("groups", "ctx"), None, "head", None),
            P(("groups", "ctx"), None, "head", None),
            P("groups", "ctx"),
            P("groups", "ctx", "head", None),
            P("groups", "ctx", "head", None),
            P("groups", "ctx", "head", None),
            P("groups"),
            P("head", "ctx"),
        ),
        out_specs=(P("groups", None, "ctx"), P("groups", None, "ctx")),
        check_vma=False,
    )
```

```python
import math

import jax
import jax.numpy as jnp
from jax import lax
from jax.sharding import PartitionSpec as P

negative_floor = -1e30


def absorb(softmax_state, queries, key_rows, value_rows, allowed):
    running_max, running_sum, weighted = softmax_state
    scores = jnp.einsum("brd,bnd->brn", queries, key_rows, preferred_element_type=jnp.float32) * (
        1.0 / math.sqrt(queries.shape[-1])
    )
    if allowed is not None:
        scores = jnp.where(allowed, scores, negative_floor)
    new_max = jnp.maximum(running_max, jnp.max(scores, axis=-1))
    factor = jnp.exp(running_max - new_max)
    weights = jnp.exp(scores - new_max[..., None])
    running_sum = running_sum * factor + jnp.sum(weights, axis=-1)
    weighted = weighted * factor[..., None] + jnp.einsum(
        "brn,bnd->brd", weights.astype(jnp.bfloat16), value_rows, preferred_element_type=jnp.float32
    )
    return (new_max, running_sum, weighted)


def sweep(softmax_state, queries, key_rows, value_rows, block_width):
    total_keys = key_rows.shape[1]
    block_width = math.gcd(total_keys, block_width)

    def one_block(state_in, block_start):
        key_block = lax.dynamic_slice_in_dim(key_rows, block_start, block_width, 1)
        value_block = lax.dynamic_slice_in_dim(value_rows, block_start, block_width, 1)
        return (absorb(state_in, queries, key_block, value_block, None), None)

    starts = jnp.arange(total_keys // block_width, dtype=jnp.int32) * block_width
    softmax_state, unused = lax.scan(one_block, softmax_state, starts)
    return softmax_state


def empty_state(head_batch, row_count, head_depth):
    return (
        jnp.full((head_batch, row_count), negative_floor, jnp.float32),
        jnp.zeros((head_batch, row_count), jnp.float32),
        jnp.zeros((head_batch, row_count, head_depth), jnp.float32),
    )


def own_steps(softmax_state, queries_five, own_key, own_value):
    running_max, running_sum, weighted = softmax_state
    key_rows = own_key.transpose(2, 1, 0, 3)
    value_rows = own_value.transpose(2, 1, 0, 3)
    scores = jnp.einsum(
        "ktsgd,ksud->ktsgu", queries_five, key_rows, preferred_element_type=jnp.float32
    ) * (1.0 / math.sqrt(queries_five.shape[-1]))
    step_total = queries_five.shape[1]
    step_ids = jnp.arange(step_total, dtype=jnp.int32)
    allowed = (step_ids[None, :] <= step_ids[:, None])[None, :, None, None, :]
    scores = jnp.where(allowed, scores, negative_floor)
    new_max = jnp.maximum(running_max, jnp.max(scores, axis=-1))
    factor = jnp.exp(running_max - new_max)
    weights = jnp.exp(scores - new_max[..., None])
    running_sum = running_sum * factor + jnp.sum(weights, axis=-1)
    weighted = weighted * factor[..., None] + jnp.einsum(
        "ktsgu,ksud->ktsgd",
        weights.astype(jnp.bfloat16),
        value_rows,
        preferred_element_type=jnp.float32,
    )
    return (weighted / running_sum[..., None]).astype(jnp.bfloat16)


def ctx_shards(block, ctx_count):
    chips = ctx_count // 2
    received = [block]
    for shift in range(1, chips):
        pairs = [(dev, (dev - 2 * shift) % ctx_count) for dev in range(ctx_count)]
        received.append(lax.ppermute(block, "ctx", pairs))
    along_x = jnp.stack(received)
    other_core = lax.ppermute(along_x, "ctx", [(dev, dev ^ 1) for dev in range(ctx_count)])
    return along_x, other_core


def ctx_gather(block, ctx_count, axis=0):
    ctx_index = lax.axis_index("ctx")
    chip, core = ctx_index // 2, ctx_index % 2
    along_x, other_core = ctx_shards(block, ctx_count)
    along_x = jnp.roll(along_x, chip, axis=0)
    other_core = jnp.roll(other_core, chip, axis=0)
    core_zero = jnp.where(core == 0, along_x, other_core)
    core_one = jnp.where(core == 0, other_core, along_x)
    joined = jnp.moveaxis(jnp.stack([core_zero, core_one], axis=1), (0, 1), (axis, axis + 1))
    return joined.reshape(block.shape[:axis] + (-1,) + block.shape[axis + 1 :])


def shards(
    span_query,
    span_key,
    span_value,
    prefix_key,
    prefix_value,
    page_table,
    decode_query,
    decode_key,
    decode_value,
    sample_prompt,
    out_weight,
):
    prompts, span_dev, heads_dev, head_depth = span_query.shape
    kv_heads = span_key.shape[2]
    group_size = heads_dev // kv_heads
    steps_count = decode_query.shape[0]
    samples_dev = decode_query.shape[1]
    head_batch = prompts * kv_heads
    ctx_index = lax.axis_index("ctx")
    slot_rows = page_table.reshape(-1)
    local_keys = (
        jnp.take(prefix_key, slot_rows, axis=0)
        .reshape(prompts, -1, kv_heads, head_depth)
        .transpose(0, 2, 1, 3)
    )
    local_values = (
        jnp.take(prefix_value, slot_rows, axis=0)
        .reshape(prompts, -1, kv_heads, head_depth)
        .transpose(0, 2, 1, 3)
    )
    span_rows = (
        span_query.reshape(prompts, span_dev, kv_heads, group_size, head_depth)
        .transpose(0, 2, 1, 3, 4)
        .reshape(head_batch, span_dev * group_size, head_depth)
    )
    ctx_count = sample_prompt.shape[0] // samples_dev
    span_pair = ctx_gather(jnp.stack([span_key, span_value]), ctx_count, axis=2)
    span_keys_all, span_values_all = span_pair[0], span_pair[1]
    span_total = span_keys_all.shape[1]
    span_key_rows = span_keys_all.transpose(0, 2, 1, 3).reshape(head_batch, span_total, head_depth)
    span_value_rows = span_values_all.transpose(0, 2, 1, 3).reshape(
        head_batch, span_total, head_depth
    )
    query_pos = (
        ctx_index * span_dev + jnp.arange(span_dev * group_size, dtype=jnp.int32) // group_size
    )
    causal = (jnp.arange(span_total, dtype=jnp.int32)[None, :] <= query_pos[:, None])[None]
    decode_five = decode_query.reshape(
        steps_count, samples_dev, kv_heads, group_size, head_depth
    ).transpose(2, 0, 1, 3, 4)
    prefill_state = empty_state(head_batch, span_dev * group_size, head_depth)
    along_x, other_core = ctx_shards(jnp.stack([local_keys, local_values]), ctx_count)
    arrived = jnp.concatenate([along_x, other_core], axis=0)
    prompt_keys_all, prompt_values_all = (
        jnp.concatenate([arrived[shard, member] for shard in range(ctx_count)], axis=2)
        for member in range(2)
    )
    prefix_len = prompt_keys_all.shape[2]
    key_rows = prompt_keys_all.reshape(head_batch, prefix_len, head_depth)
    value_rows = prompt_values_all.reshape(head_batch, prefix_len, head_depth)
    prefill_state = sweep(prefill_state, span_rows, key_rows, value_rows, 2048)
    decode_flat = decode_five.reshape(kv_heads, -1, head_depth)
    decode_batch = jnp.broadcast_to(decode_flat[None], (prompts,) + decode_flat.shape).reshape(
        head_batch, -1, head_depth
    )
    decode_state = empty_state(head_batch, decode_flat.shape[1], head_depth)
    decode_state = sweep(decode_state, decode_batch, key_rows, value_rows, 2048)
    decode_state = sweep(decode_state, decode_batch, span_key_rows, span_value_rows, span_total)
    own_prompts = lax.dynamic_slice_in_dim(sample_prompt, ctx_index * samples_dev, samples_dev)
    chosen = (
        own_prompts[None, None, None, :, None]
        == jnp.arange(prompts, dtype=jnp.int32)[:, None, None, None, None]
    )

    def select_prompt(member):
        shaped = member.reshape(
            (prompts, kv_heads, steps_count, samples_dev, group_size) + member.shape[2:]
        )
        select_mask = chosen.reshape(chosen.shape + (1,) * (shaped.ndim - 5))
        return jnp.sum(jnp.where(select_mask, shaped, 0.0), axis=0)

    decode_state = tuple((select_prompt(member) for member in decode_state))
    prefill_state = absorb(prefill_state, span_rows, span_key_rows, span_value_rows, causal)
    span_mixed = (prefill_state[2] / prefill_state[1][..., None]).astype(jnp.bfloat16)
    span_attn = (
        span_mixed.reshape(prompts, kv_heads, span_dev, group_size, head_depth)
        .transpose(0, 2, 1, 3, 4)
        .reshape(prompts, span_dev, heads_dev * head_depth)
    )
    decode_mixed = own_steps(decode_state, decode_five, decode_key, decode_value)
    decode_attn = decode_mixed.transpose(1, 2, 0, 3, 4).reshape(
        steps_count, samples_dev, heads_dev * head_depth
    )
    span_rows_all = ctx_gather(span_attn, ctx_count, axis=1)
    decode_rows_all = ctx_gather(decode_attn, ctx_count, axis=1)
    span_out, decode_out = lax.psum(
        tuple(
            jnp.dot(rows, out_weight, preferred_element_type=jnp.float32).astype(jnp.bfloat16)
            for rows in (span_rows_all, decode_rows_all)
        ),
        "head",
    )
    return (span_out, decode_out)


def solution(mesh):
    return jax.shard_map(
        shards,
        mesh=mesh,
        in_specs=(
            P("groups", "ctx", "head", None),
            P("groups", "ctx", "head", None),
            P("groups", "ctx", "head", None),
            P(("groups", "ctx"), None, "head", None),
            P(("groups", "ctx"), None, "head", None),
            P("groups", "ctx"),
            P("groups", "ctx", "head", None),
            P("groups", "ctx", "head", None),
            P("groups", "ctx", "head", None),
            P("groups"),
            P("head", "ctx"),
        ),
        out_specs=(P("groups", None, "ctx"), P("groups", None, "ctx")),
        check_vma=False,
    )
```

```python
import functools
import math

import jax
import jax.numpy as jnp
from jax import lax
from jax.experimental import pallas as pl
from jax.sharding import PartitionSpec as P

negative_floor = -1e30


def attend_kernel(prompt_ref, limit_ref, q_ref, kp_ref, vp_ref, ks_ref, vs_ref, max_ref, sum_ref, acc_ref):
    queries = q_ref[0]
    row_prompt = prompt_ref[0]
    row_limit = limit_ref[0]
    scale = 1.0 / math.sqrt(queries.shape[-1])
    span_pos = lax.broadcasted_iota(jnp.int32, (1, ks_ref.shape[2]), 1)
    scores, values = [], []
    for member in range(kp_ref.shape[0]):
        mine = row_prompt == member
        for key_ref, value_ref, allowed in (
            (kp_ref, vp_ref, mine),
            (ks_ref, vs_ref, mine & (span_pos <= row_limit)),
        ):
            raw = lax.dot_general(
                queries, key_ref[member, 0], (((1,), (1,)), ((), ())),
                preferred_element_type=jnp.float32,
            ) * scale
            scores.append(jnp.where(allowed, raw, negative_floor))
            values.append(value_ref[member, 0])
    row_max = functools.reduce(jnp.maximum, [s.max(axis=-1, keepdims=True) for s in scores])
    weights = [jnp.exp(s - row_max) for s in scores]
    max_ref[0] = row_max
    sum_ref[0] = functools.reduce(jnp.add, [w.sum(axis=-1, keepdims=True) for w in weights])
    acc_ref[0] = functools.reduce(jnp.add, [
        jnp.dot(w.astype(jnp.bfloat16), v, preferred_element_type=jnp.float32)
        for w, v in zip(weights, values)
    ])


def attend(queries, prefix_keys, prefix_values, span_keys, span_values, row_prompt, row_limit, per_prompt):
    grid_count, rows, depth = queries.shape
    prompts, kv_heads = prefix_keys.shape[:2]
    if per_prompt:
        kv_block, kv_map = 1, lambda g: (g // kv_heads, g % kv_heads, 0, 0)
    else:
        kv_block, kv_map = prompts, lambda g: (0, g, 0, 0)
    row_spec = pl.BlockSpec((1, rows, 1), lambda g: (g, 0, 0))
    def kv_spec(arr):
        return pl.BlockSpec((kv_block, 1) + arr.shape[2:], kv_map)
    return pl.pallas_call(
        attend_kernel,
        grid=(grid_count,),
        in_specs=[row_spec, row_spec, pl.BlockSpec((1, rows, depth), lambda g: (g, 0, 0)),
                  kv_spec(prefix_keys), kv_spec(prefix_values), kv_spec(span_keys), kv_spec(span_values)],
        out_specs=[row_spec, row_spec, pl.BlockSpec((1, rows, depth), lambda g: (g, 0, 0))],
        out_shape=[jax.ShapeDtypeStruct((grid_count, rows, 1), jnp.float32)] * 2
        + [jax.ShapeDtypeStruct((grid_count, rows, depth), jnp.float32)],
    )(row_prompt, row_limit, queries, prefix_keys, prefix_values, span_keys, span_values)


def own_steps(softmax_state, queries_five, own_key, own_value):
    running_max, running_sum, weighted = softmax_state
    key_rows = own_key.transpose(2, 1, 0, 3)
    value_rows = own_value.transpose(2, 1, 0, 3)
    scores = jnp.einsum(
        "ktsgd,ksud->ktsgu", queries_five, key_rows, preferred_element_type=jnp.float32
    ) * (1.0 / math.sqrt(queries_five.shape[-1]))
    step_total = queries_five.shape[1]
    step_ids = jnp.arange(step_total, dtype=jnp.int32)
    allowed = (step_ids[None, :] <= step_ids[:, None])[None, :, None, None, :]
    scores = jnp.where(allowed, scores, negative_floor)
    new_max = jnp.maximum(running_max, jnp.max(scores, axis=-1))
    factor = jnp.exp(running_max - new_max)
    weights = jnp.exp(scores - new_max[..., None])
    running_sum = running_sum * factor + jnp.sum(weights, axis=-1)
    weighted = weighted * factor[..., None] + jnp.einsum(
        "ktsgu,ksud->ktsgd",
        weights.astype(jnp.bfloat16),
        value_rows,
        preferred_element_type=jnp.float32,
    )
    return (weighted / running_sum[..., None]).astype(jnp.bfloat16)


def ctx_shards(block, ctx_count):
    chips = ctx_count // 2
    received = [block]
    for shift in range(1, chips):
        pairs = [(dev, (dev - 2 * shift) % ctx_count) for dev in range(ctx_count)]
        received.append(lax.ppermute(block, "ctx", pairs))
    along_x = jnp.stack(received)
    other_core = lax.ppermute(along_x, "ctx", [(dev, dev ^ 1) for dev in range(ctx_count)])
    return along_x, other_core


def ctx_gather(block, ctx_count):
    ctx_index = lax.axis_index("ctx")
    chip, core = ctx_index // 2, ctx_index % 2
    along_x, other_core = ctx_shards(block, ctx_count)
    along_x = jnp.roll(along_x, chip, axis=0)
    other_core = jnp.roll(other_core, chip, axis=0)
    core_zero = jnp.where(core == 0, along_x, other_core)
    core_one = jnp.where(core == 0, other_core, along_x)
    return jnp.stack([core_zero, core_one], axis=1).reshape((ctx_count,) + block.shape)


def shards(
    span_query,
    span_key,
    span_value,
    prefix_key,
    prefix_value,
    page_table,
    decode_query,
    decode_key,
    decode_value,
    sample_prompt,
    out_weight,
):
    prompts, span_dev, heads_dev, head_depth = span_query.shape
    kv_heads = span_key.shape[2]
    group_size = heads_dev // kv_heads
    steps_count = decode_query.shape[0]
    samples_dev = decode_query.shape[1]
    head_batch = prompts * kv_heads
    ctx_index = lax.axis_index("ctx")
    slot_rows = page_table.reshape(-1)
    local_keys = (
        jnp.take(prefix_key, slot_rows, axis=0)
        .reshape(prompts, -1, kv_heads, head_depth)
        .transpose(0, 2, 1, 3)
    )
    local_values = (
        jnp.take(prefix_value, slot_rows, axis=0)
        .reshape(prompts, -1, kv_heads, head_depth)
        .transpose(0, 2, 1, 3)
    )
    span_rows = (
        span_query.reshape(prompts, span_dev, kv_heads, group_size, head_depth)
        .transpose(0, 2, 1, 3, 4)
        .reshape(head_batch, span_dev * group_size, head_depth)
    )
    ctx_count = sample_prompt.shape[0] // samples_dev
    span_pair = ctx_gather(jnp.stack([span_key, span_value]), ctx_count)
    span_keys_all, span_values_all = (
        span_pair[:, member].transpose(1, 0, 2, 3, 4).reshape(
            (prompts, ctx_count * span_dev) + span_key.shape[2:]
        )
        for member in range(2)
    )
    span_key_rows = span_keys_all.transpose(0, 2, 1, 3)
    span_value_rows = span_values_all.transpose(0, 2, 1, 3)
    query_pos = (
        ctx_index * span_dev + jnp.arange(span_dev * group_size, dtype=jnp.int32) // group_size
    )
    decode_five = decode_query.reshape(
        steps_count, samples_dev, kv_heads, group_size, head_depth
    ).transpose(2, 0, 1, 3, 4)
    along_x, other_core = ctx_shards(jnp.stack([local_keys, local_values]), ctx_count)
    arrived = jnp.concatenate([along_x, other_core], axis=0)
    prompt_keys_all, prompt_values_all = (
        jnp.concatenate([arrived[shard, member] for shard in range(ctx_count)], axis=2)
        for member in range(2)
    )
    span_rows_count = span_dev * group_size
    span_limit = jnp.broadcast_to(query_pos[None, :, None], (head_batch, span_rows_count, 1))
    unused, span_sum, span_acc = attend(
        span_rows,
        prompt_keys_all,
        prompt_values_all,
        span_key_rows,
        span_value_rows,
        jnp.zeros_like(span_limit),
        span_limit,
        True,
    )
    span_mixed = (span_acc / span_sum).astype(jnp.bfloat16)
    own_prompts = lax.dynamic_slice_in_dim(sample_prompt, ctx_index * samples_dev, samples_dev)
    decode_rows_count = steps_count * samples_dev * group_size
    decode_prompt = jnp.broadcast_to(
        own_prompts[None, None, :, None], (kv_heads, steps_count, samples_dev, group_size)
    ).reshape(kv_heads, decode_rows_count, 1)
    decode_max, decode_sum, decode_acc = attend(
        decode_five.reshape(kv_heads, decode_rows_count, head_depth),
        prompt_keys_all,
        prompt_values_all,
        span_key_rows,
        span_value_rows,
        decode_prompt,
        jnp.full_like(decode_prompt, span_keys_all.shape[1]),
        False,
    )
    decode_state = (
        decode_max.reshape(decode_five.shape[:4]),
        decode_sum.reshape(decode_five.shape[:4]),
        decode_acc.reshape(decode_five.shape),
    )
    span_attn = (
        span_mixed.reshape(prompts, kv_heads, span_dev, group_size, head_depth)
        .transpose(0, 2, 1, 3, 4)
        .reshape(prompts * span_dev, heads_dev * head_depth)
    )
    decode_mixed = own_steps(decode_state, decode_five, decode_key, decode_value)
    decode_attn = decode_mixed.transpose(1, 2, 0, 3, 4).reshape(
        steps_count * samples_dev, heads_dev * head_depth
    )
    rows_local = jnp.concatenate([span_attn, decode_attn], axis=0)
    projected = jnp.dot(
        ctx_gather(rows_local, ctx_count).reshape(-1, rows_local.shape[-1]),
        out_weight,
        preferred_element_type=jnp.float32,
    )
    share = lax.psum_scatter(
        projected.astype(jnp.bfloat16), "head", scatter_dimension=0, tiled=True
    )
    summed = lax.all_gather(share, "head", axis=0, tiled=True)
    rows_dev = rows_local.shape[0]
    blocks_by_ctx = summed.reshape(-1, rows_dev, summed.shape[-1])
    span_out = (
        blocks_by_ctx[:, : prompts * span_dev]
        .reshape(ctx_count, prompts, span_dev, -1)
        .transpose(1, 0, 2, 3)
        .reshape(prompts, ctx_count * span_dev, -1)
    )
    decode_out = (
        blocks_by_ctx[:, prompts * span_dev :]
        .reshape(ctx_count, steps_count, samples_dev, -1)
        .transpose(1, 0, 2, 3)
        .reshape(steps_count, ctx_count * samples_dev, -1)
    )
    return (span_out, decode_out)


def solution(mesh):
    return jax.shard_map(
        shards,
        mesh=mesh,
        in_specs=(
            P("groups", "ctx", "head", None),
            P("groups", "ctx", "head", None),
            P("groups", "ctx", "head", None),
            P(("groups", "ctx"), None, "head", None),
            P(("groups", "ctx"), None, "head", None),
            P("groups", "ctx"),
            P("groups", "ctx", "head", None),
            P("groups", "ctx", "head", None),
            P("groups", "ctx", "head", None),
            P("groups"),
            P("head", "ctx"),
        ),
        out_specs=(P("groups", None, "ctx"), P("groups", None, "ctx")),
        check_vma=False,
    )
```

```python
import functools
import math

import jax
import jax.numpy as jnp
from jax import lax
from jax.sharding import PartitionSpec as P

negative_floor = -1e30


def absorb(softmax_state, queries, key_rows, value_rows, allowed):
    running_max, running_sum, weighted = softmax_state
    scores = jnp.einsum("brd,bnd->brn", queries, key_rows, preferred_element_type=jnp.float32) * (
        1.0 / math.sqrt(queries.shape[-1])
    )
    if allowed is not None:
        scores = jnp.where(allowed, scores, negative_floor)
    new_max = jnp.maximum(running_max, jnp.max(scores, axis=-1))
    factor = jnp.exp(running_max - new_max)
    weights = jnp.exp(scores - new_max[..., None])
    running_sum = running_sum * factor + jnp.sum(weights, axis=-1)
    weighted = weighted * factor[..., None] + jnp.einsum(
        "brn,bnd->brd", weights.astype(jnp.bfloat16), value_rows, preferred_element_type=jnp.float32
    )
    return (new_max, running_sum, weighted)


def sweep(softmax_state, queries, key_rows, value_rows, block_width):
    total_keys = key_rows.shape[1]
    block_width = math.gcd(total_keys, block_width)

    def one_block(state_in, block_start):
        key_block = lax.dynamic_slice_in_dim(key_rows, block_start, block_width, 1)
        value_block = lax.dynamic_slice_in_dim(value_rows, block_start, block_width, 1)
        return (absorb(state_in, queries, key_block, value_block, None), None)

    starts = jnp.arange(total_keys // block_width, dtype=jnp.int32) * block_width
    softmax_state, unused = lax.scan(one_block, softmax_state, starts)
    return softmax_state


def empty_state(head_batch, row_count, head_depth):
    return (
        jnp.full((head_batch, row_count), negative_floor, jnp.float32),
        jnp.zeros((head_batch, row_count), jnp.float32),
        jnp.zeros((head_batch, row_count, head_depth), jnp.float32),
    )


def own_steps(softmax_state, queries_five, own_key, own_value):
    running_max, running_sum, weighted = softmax_state
    key_rows = own_key.transpose(2, 1, 0, 3)
    value_rows = own_value.transpose(2, 1, 0, 3)
    scores = jnp.einsum(
        "ktsgd,ksud->ktsgu", queries_five, key_rows, preferred_element_type=jnp.float32
    ) * (1.0 / math.sqrt(queries_five.shape[-1]))
    step_total = queries_five.shape[1]
    step_ids = jnp.arange(step_total, dtype=jnp.int32)
    allowed = (step_ids[None, :] <= step_ids[:, None])[None, :, None, None, :]
    scores = jnp.where(allowed, scores, negative_floor)
    new_max = jnp.maximum(running_max, jnp.max(scores, axis=-1))
    factor = jnp.exp(running_max - new_max)
    weights = jnp.exp(scores - new_max[..., None])
    running_sum = running_sum * factor + jnp.sum(weights, axis=-1)
    weighted = weighted * factor[..., None] + jnp.einsum(
        "ktsgu,ksud->ktsgd",
        weights.astype(jnp.bfloat16),
        value_rows,
        preferred_element_type=jnp.float32,
    )
    return (weighted / running_sum[..., None]).astype(jnp.bfloat16)


def ctx_shards(block, ctx_count):
    chips = ctx_count // 2
    received = [block]
    for shift in range(1, chips):
        pairs = [(dev, (dev - 2 * shift) % ctx_count) for dev in range(ctx_count)]
        received.append(lax.ppermute(block, "ctx", pairs))
    along_x = jnp.stack(received)
    other_core = lax.ppermute(along_x, "ctx", [(dev, dev ^ 1) for dev in range(ctx_count)])
    return along_x, other_core


def ctx_gather(block, ctx_count):
    ctx_index = lax.axis_index("ctx")
    chip, core = ctx_index // 2, ctx_index % 2
    along_x, other_core = ctx_shards(block, ctx_count)
    along_x = jnp.roll(along_x, chip, axis=0)
    other_core = jnp.roll(other_core, chip, axis=0)
    core_zero = jnp.where(core == 0, along_x, other_core)
    core_one = jnp.where(core == 0, other_core, along_x)
    return jnp.stack([core_zero, core_one], axis=1).reshape((ctx_count,) + block.shape)


def head_sum_line(partial, head_count):
    last = head_count - 1
    head_index = lax.axis_index("head")
    blocks = partial.reshape((head_count, -1) + partial.shape[1:])
    rightward = [(dev, dev + 1) for dev in range(last)]
    leftward = [(dev + 1, dev) for dev in range(last)]
    from_left = from_right = None
    for step in range(1, head_count):
        right_block = jnp.clip(head_index + head_count - step, 0, last)
        left_block = jnp.clip(head_index - head_count + step, 0, last)
        going_right = lax.dynamic_index_in_dim(blocks, right_block, 0, False)
        going_left = lax.dynamic_index_in_dim(blocks, left_block, 0, False)
        if from_left is not None:
            going_right = going_right + from_left.astype(jnp.float32)
            going_left = going_left + from_right.astype(jnp.float32)
        from_left = lax.ppermute(going_right.astype(jnp.bfloat16), "head", rightward)
        from_right = lax.ppermute(going_left.astype(jnp.bfloat16), "head", leftward)
    own = lax.dynamic_index_in_dim(blocks, head_index, 0, False)
    mine = (own + from_left.astype(jnp.float32) + from_right.astype(jnp.float32)).astype(jnp.bfloat16)
    lefts, rights = [], []
    send_right = send_left = mine
    for step in range(1, head_count):
        send_right = lax.ppermute(send_right, "head", rightward)
        send_left = lax.ppermute(send_left, "head", leftward)
        lefts.append(send_right)
        rights.append(send_left)
    candidates = jnp.stack([mine] + lefts + rights)
    wanted = jnp.arange(head_count, dtype=jnp.int32)
    pick = jnp.where(
        wanted == head_index,
        0,
        jnp.where(wanted < head_index, head_index - wanted, last + wanted - head_index),
    )
    return jnp.take(candidates, pick, axis=0).reshape(partial.shape)


def shards(
    span_query,
    span_key,
    span_value,
    prefix_key,
    prefix_value,
    page_table,
    decode_query,
    decode_key,
    decode_value,
    sample_prompt,
    out_weight,
    head_count,
):
    prompts, span_dev, heads_dev, head_depth = span_query.shape
    kv_heads = span_key.shape[2]
    group_size = heads_dev // kv_heads
    steps_count = decode_query.shape[0]
    samples_dev = decode_query.shape[1]
    head_batch = prompts * kv_heads
    ctx_index = lax.axis_index("ctx")
    slot_rows = page_table.reshape(-1)
    local_keys = (
        jnp.take(prefix_key, slot_rows, axis=0)
        .reshape(prompts, -1, kv_heads, head_depth)
        .transpose(0, 2, 1, 3)
    )
    local_values = (
        jnp.take(prefix_value, slot_rows, axis=0)
        .reshape(prompts, -1, kv_heads, head_depth)
        .transpose(0, 2, 1, 3)
    )
    span_rows = (
        span_query.reshape(prompts, span_dev, kv_heads, group_size, head_depth)
        .transpose(0, 2, 1, 3, 4)
        .reshape(head_batch, span_dev * group_size, head_depth)
    )
    ctx_count = sample_prompt.shape[0] // samples_dev
    span_pair = ctx_gather(jnp.stack([span_key, span_value]), ctx_count)
    span_keys_all, span_values_all = (
        span_pair[:, member].transpose(1, 0, 2, 3, 4).reshape(
            (prompts, ctx_count * span_dev) + span_key.shape[2:]
        )
        for member in range(2)
    )
    span_total = span_keys_all.shape[1]
    span_key_rows = span_keys_all.transpose(0, 2, 1, 3).reshape(head_batch, span_total, head_depth)
    span_value_rows = span_values_all.transpose(0, 2, 1, 3).reshape(
        head_batch, span_total, head_depth
    )
    query_pos = (
        ctx_index * span_dev + jnp.arange(span_dev * group_size, dtype=jnp.int32) // group_size
    )
    causal = (jnp.arange(span_total, dtype=jnp.int32)[None, :] <= query_pos[:, None])[None]
    decode_five = decode_query.reshape(
        steps_count, samples_dev, kv_heads, group_size, head_depth
    ).transpose(2, 0, 1, 3, 4)
    prefill_state = empty_state(head_batch, span_dev * group_size, head_depth)
    along_x, other_core = ctx_shards(jnp.stack([local_keys, local_values]), ctx_count)
    arrived = jnp.concatenate([along_x, other_core], axis=0)
    prompt_keys_all, prompt_values_all = (
        jnp.concatenate([arrived[shard, member] for shard in range(ctx_count)], axis=2)
        for member in range(2)
    )
    prefix_len = prompt_keys_all.shape[2]
    key_rows = prompt_keys_all.reshape(head_batch, prefix_len, head_depth)
    value_rows = prompt_values_all.reshape(head_batch, prefix_len, head_depth)
    prefill_state = sweep(prefill_state, span_rows, key_rows, value_rows, 2048)
    decode_flat = decode_five.reshape(kv_heads, -1, head_depth)
    decode_batch = jnp.broadcast_to(decode_flat[None], (prompts,) + decode_flat.shape).reshape(
        head_batch, -1, head_depth
    )
    decode_state = empty_state(head_batch, decode_flat.shape[1], head_depth)
    decode_state = sweep(decode_state, decode_batch, key_rows, value_rows, 2048)
    decode_state = sweep(decode_state, decode_batch, span_key_rows, span_value_rows, span_total)
    own_prompts = lax.dynamic_slice_in_dim(sample_prompt, ctx_index * samples_dev, samples_dev)
    chosen = (
        own_prompts[None, None, None, :, None]
        == jnp.arange(prompts, dtype=jnp.int32)[:, None, None, None, None]
    )

    def select_prompt(member):
        shaped = member.reshape(
            (prompts, kv_heads, steps_count, samples_dev, group_size) + member.shape[2:]
        )
        select_mask = chosen.reshape(chosen.shape + (1,) * (shaped.ndim - 5))
        return jnp.sum(jnp.where(select_mask, shaped, 0.0), axis=0)

    decode_state = tuple((select_prompt(member) for member in decode_state))
    prefill_state = absorb(prefill_state, span_rows, span_key_rows, span_value_rows, causal)
    span_mixed = (prefill_state[2] / prefill_state[1][..., None]).astype(jnp.bfloat16)
    span_attn = (
        span_mixed.reshape(prompts, kv_heads, span_dev, group_size, head_depth)
        .transpose(0, 2, 1, 3, 4)
        .reshape(prompts * span_dev, heads_dev * head_depth)
    )
    decode_mixed = own_steps(decode_state, decode_five, decode_key, decode_value)
    decode_attn = decode_mixed.transpose(1, 2, 0, 3, 4).reshape(
        steps_count * samples_dev, heads_dev * head_depth
    )
    rows_local = jnp.concatenate([span_attn, decode_attn], axis=0)
    projected = jnp.dot(
        ctx_gather(rows_local, ctx_count).reshape(-1, rows_local.shape[-1]),
        out_weight,
        preferred_element_type=jnp.float32,
    )
    summed = head_sum_line(projected, head_count)
    rows_dev = rows_local.shape[0]
    blocks_by_ctx = summed.reshape(-1, rows_dev, summed.shape[-1])
    span_out = (
        blocks_by_ctx[:, : prompts * span_dev]
        .reshape(ctx_count, prompts, span_dev, -1)
        .transpose(1, 0, 2, 3)
        .reshape(prompts, ctx_count * span_dev, -1)
    )
    decode_out = (
        blocks_by_ctx[:, prompts * span_dev :]
        .reshape(ctx_count, steps_count, samples_dev, -1)
        .transpose(1, 0, 2, 3)
        .reshape(steps_count, ctx_count * samples_dev, -1)
    )
    return (span_out, decode_out)


def solution(mesh):
    return jax.shard_map(
        functools.partial(shards, head_count=mesh.shape["head"]),
        mesh=mesh,
        in_specs=(
            P("groups", "ctx", "head", None),
            P("groups", "ctx", "head", None),
            P("groups", "ctx", "head", None),
            P(("groups", "ctx"), None, "head", None),
            P(("groups", "ctx"), None, "head", None),
            P("groups", "ctx"),
            P("groups", "ctx", "head", None),
            P("groups", "ctx", "head", None),
            P("groups", "ctx", "head", None),
            P("groups"),
            P("head", "ctx"),
        ),
        out_specs=(P("groups", None, "ctx"), P("groups", None, "ctx")),
        check_vma=False,
    )
```

```python
import functools
import math

import jax
import jax.numpy as jnp
from jax import lax
from jax.sharding import PartitionSpec as P

negative_floor = -1e30


def absorb(softmax_state, queries, key_rows, value_rows, allowed):
    running_max, running_sum, weighted = softmax_state
    scores = jnp.einsum("brd,bnd->brn", queries, key_rows, preferred_element_type=jnp.float32) * (
        1.0 / math.sqrt(queries.shape[-1])
    )
    if allowed is not None:
        scores = jnp.where(allowed, scores, negative_floor)
    new_max = jnp.maximum(running_max, jnp.max(scores, axis=-1))
    factor = jnp.exp(running_max - new_max)
    weights = jnp.exp(scores - new_max[..., None])
    running_sum = running_sum * factor + jnp.sum(weights, axis=-1)
    weighted = weighted * factor[..., None] + jnp.einsum(
        "brn,bnd->brd", weights.astype(jnp.bfloat16), value_rows, preferred_element_type=jnp.float32
    )
    return (new_max, running_sum, weighted)


def sweep(softmax_state, queries, key_rows, value_rows, block_width):
    total_keys = key_rows.shape[1]
    block_width = math.gcd(total_keys, block_width)

    def one_block(state_in, block_start):
        key_block = lax.dynamic_slice_in_dim(key_rows, block_start, block_width, 1)
        value_block = lax.dynamic_slice_in_dim(value_rows, block_start, block_width, 1)
        return (absorb(state_in, queries, key_block, value_block, None), None)

    starts = jnp.arange(total_keys // block_width, dtype=jnp.int32) * block_width
    softmax_state, unused = lax.scan(one_block, softmax_state, starts)
    return softmax_state


def empty_state(head_batch, row_count, head_depth):
    return (
        jnp.full((head_batch, row_count), negative_floor, jnp.float32),
        jnp.zeros((head_batch, row_count), jnp.float32),
        jnp.zeros((head_batch, row_count, head_depth), jnp.float32),
    )


def own_steps(softmax_state, queries_five, own_key, own_value):
    running_max, running_sum, weighted = softmax_state
    key_rows = own_key.transpose(2, 1, 0, 3)
    value_rows = own_value.transpose(2, 1, 0, 3)
    scores = jnp.einsum(
        "ktsgd,ksud->ktsgu", queries_five, key_rows, preferred_element_type=jnp.float32
    ) * (1.0 / math.sqrt(queries_five.shape[-1]))
    step_total = queries_five.shape[1]
    step_ids = jnp.arange(step_total, dtype=jnp.int32)
    allowed = (step_ids[None, :] <= step_ids[:, None])[None, :, None, None, :]
    scores = jnp.where(allowed, scores, negative_floor)
    new_max = jnp.maximum(running_max, jnp.max(scores, axis=-1))
    factor = jnp.exp(running_max - new_max)
    weights = jnp.exp(scores - new_max[..., None])
    running_sum = running_sum * factor + jnp.sum(weights, axis=-1)
    weighted = weighted * factor[..., None] + jnp.einsum(
        "ktsgu,ksud->ktsgd",
        weights.astype(jnp.bfloat16),
        value_rows,
        preferred_element_type=jnp.float32,
    )
    return (weighted / running_sum[..., None]).astype(jnp.bfloat16)


def ctx_shards(block, ctx_count):
    chips = ctx_count // 2
    received = [block]
    for shift in range(1, chips):
        pairs = [(dev, (dev - 2 * shift) % ctx_count) for dev in range(ctx_count)]
        received.append(lax.ppermute(block, "ctx", pairs))
    along_x = jnp.stack(received)
    other_core = lax.ppermute(along_x, "ctx", [(dev, dev ^ 1) for dev in range(ctx_count)])
    return along_x, other_core


def ctx_gather(block, ctx_count):
    ctx_index = lax.axis_index("ctx")
    chip, core = ctx_index // 2, ctx_index % 2
    along_x, other_core = ctx_shards(block, ctx_count)
    along_x = jnp.roll(along_x, chip, axis=0)
    other_core = jnp.roll(other_core, chip, axis=0)
    core_zero = jnp.where(core == 0, along_x, other_core)
    core_one = jnp.where(core == 0, other_core, along_x)
    return jnp.stack([core_zero, core_one], axis=1).reshape((ctx_count,) + block.shape)


def head_sum_line(partial, head_count):
    last = head_count - 1
    head_index = lax.axis_index("head")
    blocks = partial.reshape((head_count, -1) + partial.shape[1:])
    rightward = [(dev, dev + 1) for dev in range(last)]
    leftward = [(dev + 1, dev) for dev in range(last)]
    from_left = from_right = None
    for step in range(1, head_count):
        right_block = jnp.clip(head_index + head_count - step, 0, last)
        left_block = jnp.clip(head_index - head_count + step, 0, last)
        going_right = lax.dynamic_index_in_dim(blocks, right_block, 0, False)
        going_left = lax.dynamic_index_in_dim(blocks, left_block, 0, False)
        if from_left is not None:
            going_right = going_right + from_left.astype(jnp.float32)
            going_left = going_left + from_right.astype(jnp.float32)
        from_left = lax.ppermute(going_right.astype(jnp.bfloat16), "head", rightward)
        from_right = lax.ppermute(going_left.astype(jnp.bfloat16), "head", leftward)
    own = lax.dynamic_index_in_dim(blocks, head_index, 0, False)
    mine = (own + from_left.astype(jnp.float32) + from_right.astype(jnp.float32)).astype(jnp.bfloat16)
    lefts, rights = [], []
    send_right = send_left = mine
    for step in range(1, head_count):
        send_right = lax.ppermute(send_right, "head", rightward)
        send_left = lax.ppermute(send_left, "head", leftward)
        lefts.append(send_right)
        rights.append(send_left)
    candidates = jnp.stack([mine] + lefts + rights)
    wanted = jnp.arange(head_count, dtype=jnp.int32)
    pick = jnp.where(
        wanted == head_index,
        0,
        jnp.where(wanted < head_index, head_index - wanted, last + wanted - head_index),
    )
    return jnp.take(candidates, pick, axis=0).reshape(partial.shape)


def shards(
    span_query,
    span_key,
    span_value,
    prefix_key,
    prefix_value,
    page_table,
    decode_query,
    decode_key,
    decode_value,
    sample_prompt,
    out_weight,
    head_count,
):
    prompts, span_dev, heads_dev, head_depth = span_query.shape
    kv_heads = span_key.shape[2]
    group_size = heads_dev // kv_heads
    steps_count = decode_query.shape[0]
    samples_dev = decode_query.shape[1]
    head_batch = prompts * kv_heads
    ctx_index = lax.axis_index("ctx")
    slot_rows = page_table.reshape(-1)
    local_keys = (
        jnp.take(prefix_key, slot_rows, axis=0)
        .reshape(prompts, -1, kv_heads, head_depth)
        .transpose(0, 2, 1, 3)
    )
    local_values = (
        jnp.take(prefix_value, slot_rows, axis=0)
        .reshape(prompts, -1, kv_heads, head_depth)
        .transpose(0, 2, 1, 3)
    )
    span_rows = (
        span_query.reshape(prompts, span_dev, kv_heads, group_size, head_depth)
        .transpose(0, 2, 1, 3, 4)
        .reshape(head_batch, span_dev * group_size, head_depth)
    )
    ctx_count = sample_prompt.shape[0] // samples_dev
    span_pair = ctx_gather(jnp.stack([span_key, span_value]), ctx_count)
    span_keys_all, span_values_all = (
        span_pair[:, member].transpose(1, 0, 2, 3, 4).reshape(
            (prompts, ctx_count * span_dev) + span_key.shape[2:]
        )
        for member in range(2)
    )
    span_total = span_keys_all.shape[1]
    span_key_rows = span_keys_all.transpose(0, 2, 1, 3).reshape(head_batch, span_total, head_depth)
    span_value_rows = span_values_all.transpose(0, 2, 1, 3).reshape(
        head_batch, span_total, head_depth
    )
    query_pos = (
        ctx_index * span_dev + jnp.arange(span_dev * group_size, dtype=jnp.int32) // group_size
    )
    causal = (jnp.arange(span_total, dtype=jnp.int32)[None, :] <= query_pos[:, None])[None]
    decode_five = decode_query.reshape(
        steps_count, samples_dev, kv_heads, group_size, head_depth
    ).transpose(2, 0, 1, 3, 4)
    prefill_state = empty_state(head_batch, span_dev * group_size, head_depth)
    own_pages = jnp.stack([local_keys, local_values])
    core_pairs = [(dev, dev ^ 1) for dev in range(ctx_count)]
    near_pages = jnp.concatenate([own_pages, lax.ppermute(own_pages, "ctx", core_pairs)], axis=3)
    along_x = [
        lax.ppermute(own_pages, "ctx", [(dev, (dev - 2 * shift) % ctx_count) for dev in range(ctx_count)])
        for shift in range(1, ctx_count // 2)
    ]
    far_pages = jnp.concatenate(along_x, axis=3)
    far_pages = jnp.concatenate([far_pages, lax.ppermute(far_pages, "ctx", core_pairs)], axis=3)
    decode_flat = decode_five.reshape(kv_heads, -1, head_depth)
    decode_batch = jnp.broadcast_to(decode_flat[None], (prompts,) + decode_flat.shape).reshape(
        head_batch, -1, head_depth
    )
    decode_state = empty_state(head_batch, decode_flat.shape[1], head_depth)
    for pages in (near_pages, far_pages):
        key_rows = pages[0].reshape(head_batch, -1, head_depth)
        value_rows = pages[1].reshape(head_batch, -1, head_depth)
        prefill_state = absorb(prefill_state, span_rows, key_rows, value_rows, None)
        decode_state = absorb(decode_state, decode_batch, key_rows, value_rows, None)
    decode_state = sweep(decode_state, decode_batch, span_key_rows, span_value_rows, span_total)
    own_prompts = lax.dynamic_slice_in_dim(sample_prompt, ctx_index * samples_dev, samples_dev)
    chosen = (
        own_prompts[None, None, None, :, None]
        == jnp.arange(prompts, dtype=jnp.int32)[:, None, None, None, None]
    )

    def select_prompt(member):
        shaped = member.reshape(
            (prompts, kv_heads, steps_count, samples_dev, group_size) + member.shape[2:]
        )
        select_mask = chosen.reshape(chosen.shape + (1,) * (shaped.ndim - 5))
        return jnp.sum(jnp.where(select_mask, shaped, 0.0), axis=0)

    decode_state = tuple((select_prompt(member) for member in decode_state))
    prefill_state = absorb(prefill_state, span_rows, span_key_rows, span_value_rows, causal)
    span_mixed = (prefill_state[2] / prefill_state[1][..., None]).astype(jnp.bfloat16)
    span_attn = (
        span_mixed.reshape(prompts, kv_heads, span_dev, group_size, head_depth)
        .transpose(0, 2, 1, 3, 4)
        .reshape(prompts * span_dev, heads_dev * head_depth)
    )
    decode_mixed = own_steps(decode_state, decode_five, decode_key, decode_value)
    decode_attn = decode_mixed.transpose(1, 2, 0, 3, 4).reshape(
        steps_count * samples_dev, heads_dev * head_depth
    )
    rows_local = jnp.concatenate([span_attn, decode_attn], axis=0)
    projected = jnp.dot(
        ctx_gather(rows_local, ctx_count).reshape(-1, rows_local.shape[-1]),
        out_weight,
        preferred_element_type=jnp.float32,
    )
    summed = head_sum_line(projected, head_count)
    rows_dev = rows_local.shape[0]
    blocks_by_ctx = summed.reshape(-1, rows_dev, summed.shape[-1])
    span_out = (
        blocks_by_ctx[:, : prompts * span_dev]
        .reshape(ctx_count, prompts, span_dev, -1)
        .transpose(1, 0, 2, 3)
        .reshape(prompts, ctx_count * span_dev, -1)
    )
    decode_out = (
        blocks_by_ctx[:, prompts * span_dev :]
        .reshape(ctx_count, steps_count, samples_dev, -1)
        .transpose(1, 0, 2, 3)
        .reshape(steps_count, ctx_count * samples_dev, -1)
    )
    return (span_out, decode_out)


def solution(mesh):
    return jax.shard_map(
        functools.partial(shards, head_count=mesh.shape["head"]),
        mesh=mesh,
        in_specs=(
            P("groups", "ctx", "head", None),
            P("groups", "ctx", "head", None),
            P("groups", "ctx", "head", None),
            P(("groups", "ctx"), None, "head", None),
            P(("groups", "ctx"), None, "head", None),
            P("groups", "ctx"),
            P("groups", "ctx", "head", None),
            P("groups", "ctx", "head", None),
            P("groups", "ctx", "head", None),
            P("groups"),
            P("head", "ctx"),
        ),
        out_specs=(P("groups", None, "ctx"), P("groups", None, "ctx")),
        check_vma=False,
    )
```

```python
import functools
import math

import jax
import jax.numpy as jnp
from jax import lax
from jax.sharding import PartitionSpec as P

negative_floor = -1e30


def absorb(softmax_state, queries, key_rows, value_rows, allowed):
    running_max, running_sum, weighted = softmax_state
    scores = jnp.einsum("brd,bnd->brn", queries, key_rows, preferred_element_type=jnp.float32) * (
        1.0 / math.sqrt(queries.shape[-1])
    )
    if allowed is not None:
        scores = jnp.where(allowed, scores, negative_floor)
    new_max = jnp.maximum(running_max, jnp.max(scores, axis=-1))
    factor = jnp.exp(running_max - new_max)
    weights = jnp.exp(scores - new_max[..., None])
    running_sum = running_sum * factor + jnp.sum(weights, axis=-1)
    weighted = weighted * factor[..., None] + jnp.einsum(
        "brn,bnd->brd", weights.astype(jnp.bfloat16), value_rows, preferred_element_type=jnp.float32
    )
    return (new_max, running_sum, weighted)


def sweep(softmax_state, queries, key_rows, value_rows, block_width):
    total_keys = key_rows.shape[1]
    block_width = math.gcd(total_keys, block_width)

    def one_block(state_in, block_start):
        key_block = lax.dynamic_slice_in_dim(key_rows, block_start, block_width, 1)
        value_block = lax.dynamic_slice_in_dim(value_rows, block_start, block_width, 1)
        return (absorb(state_in, queries, key_block, value_block, None), None)

    starts = jnp.arange(total_keys // block_width, dtype=jnp.int32) * block_width
    softmax_state, unused = lax.scan(one_block, softmax_state, starts)
    return softmax_state


def empty_state(head_batch, row_count, head_depth):
    return (
        jnp.full((head_batch, row_count), negative_floor, jnp.float32),
        jnp.zeros((head_batch, row_count), jnp.float32),
        jnp.zeros((head_batch, row_count, head_depth), jnp.float32),
    )


def own_steps(softmax_state, queries_five, own_key, own_value):
    running_max, running_sum, weighted = softmax_state
    key_rows = own_key.transpose(2, 1, 0, 3)
    value_rows = own_value.transpose(2, 1, 0, 3)
    scores = jnp.einsum(
        "ktsgd,ksud->ktsgu", queries_five, key_rows, preferred_element_type=jnp.float32
    ) * (1.0 / math.sqrt(queries_five.shape[-1]))
    step_total = queries_five.shape[1]
    step_ids = jnp.arange(step_total, dtype=jnp.int32)
    allowed = (step_ids[None, :] <= step_ids[:, None])[None, :, None, None, :]
    scores = jnp.where(allowed, scores, negative_floor)
    new_max = jnp.maximum(running_max, jnp.max(scores, axis=-1))
    factor = jnp.exp(running_max - new_max)
    weights = jnp.exp(scores - new_max[..., None])
    running_sum = running_sum * factor + jnp.sum(weights, axis=-1)
    weighted = weighted * factor[..., None] + jnp.einsum(
        "ktsgu,ksud->ktsgd",
        weights.astype(jnp.bfloat16),
        value_rows,
        preferred_element_type=jnp.float32,
    )
    return (weighted / running_sum[..., None]).astype(jnp.bfloat16)


def ctx_shards(block, ctx_count):
    chips = ctx_count // 2
    received = [block]
    for shift in range(1, chips):
        pairs = [(dev, (dev - 2 * shift) % ctx_count) for dev in range(ctx_count)]
        received.append(lax.ppermute(block, "ctx", pairs))
    along_x = jnp.stack(received)
    other_core = lax.ppermute(along_x, "ctx", [(dev, dev ^ 1) for dev in range(ctx_count)])
    return along_x, other_core


def ctx_gather(block, ctx_count):
    ctx_index = lax.axis_index("ctx")
    chip, core = ctx_index // 2, ctx_index % 2
    along_x, other_core = ctx_shards(block, ctx_count)
    along_x = jnp.roll(along_x, chip, axis=0)
    other_core = jnp.roll(other_core, chip, axis=0)
    core_zero = jnp.where(core == 0, along_x, other_core)
    core_one = jnp.where(core == 0, other_core, along_x)
    return jnp.stack([core_zero, core_one], axis=1).reshape((ctx_count,) + block.shape)


def head_sum_line(partial, head_count):
    last = head_count - 1
    head_index = lax.axis_index("head")
    blocks = partial.reshape((head_count, -1) + partial.shape[1:])
    rightward = [(dev, dev + 1) for dev in range(last)]
    leftward = [(dev + 1, dev) for dev in range(last)]
    from_left = from_right = None
    for step in range(1, head_count):
        right_block = jnp.clip(head_index + head_count - step, 0, last)
        left_block = jnp.clip(head_index - head_count + step, 0, last)
        going_right = lax.dynamic_index_in_dim(blocks, right_block, 0, False)
        going_left = lax.dynamic_index_in_dim(blocks, left_block, 0, False)
        if from_left is not None:
            going_right = going_right + from_left.astype(jnp.float32)
            going_left = going_left + from_right.astype(jnp.float32)
        from_left = lax.ppermute(going_right.astype(jnp.bfloat16), "head", rightward)
        from_right = lax.ppermute(going_left.astype(jnp.bfloat16), "head", leftward)
    own = lax.dynamic_index_in_dim(blocks, head_index, 0, False)
    mine = (own + from_left.astype(jnp.float32) + from_right.astype(jnp.float32)).astype(jnp.bfloat16)
    lefts, rights = [], []
    send_right = send_left = mine
    for step in range(1, head_count):
        send_right = lax.ppermute(send_right, "head", rightward)
        send_left = lax.ppermute(send_left, "head", leftward)
        lefts.append(send_right)
        rights.append(send_left)
    candidates = jnp.stack([mine] + lefts + rights)
    wanted = jnp.arange(head_count, dtype=jnp.int32)
    pick = jnp.where(
        wanted == head_index,
        0,
        jnp.where(wanted < head_index, head_index - wanted, last + wanted - head_index),
    )
    return jnp.take(candidates, pick, axis=0).reshape(partial.shape)


def shards(
    span_query,
    span_key,
    span_value,
    prefix_key,
    prefix_value,
    page_table,
    decode_query,
    decode_key,
    decode_value,
    sample_prompt,
    out_weight,
    head_count,
):
    prompts, span_dev, heads_dev, head_depth = span_query.shape
    kv_heads = span_key.shape[2]
    group_size = heads_dev // kv_heads
    steps_count = decode_query.shape[0]
    samples_dev = decode_query.shape[1]
    head_batch = prompts * kv_heads
    ctx_index = lax.axis_index("ctx")
    slot_pick = (
        page_table[:, :, None] == jnp.arange(prefix_key.shape[0], dtype=jnp.int32)
    ).astype(prefix_key.dtype)
    local_keys, local_values = (
        jnp.einsum("pjs,sqkd->pkjqd", slot_pick, pages, preferred_element_type=jnp.float32)
        .astype(pages.dtype)
        .reshape(prompts, kv_heads, -1, head_depth)
        for pages in (prefix_key, prefix_value)
    )
    span_rows = (
        span_query.reshape(prompts, span_dev, kv_heads, group_size, head_depth)
        .transpose(0, 2, 1, 3, 4)
        .reshape(head_batch, span_dev * group_size, head_depth)
    )
    ctx_count = sample_prompt.shape[0] // samples_dev
    span_pair = ctx_gather(jnp.stack([span_key, span_value]), ctx_count)
    span_keys_all, span_values_all = (
        span_pair[:, member].transpose(1, 0, 2, 3, 4).reshape(
            (prompts, ctx_count * span_dev) + span_key.shape[2:]
        )
        for member in range(2)
    )
    span_total = span_keys_all.shape[1]
    span_key_rows = span_keys_all.transpose(0, 2, 1, 3).reshape(head_batch, span_total, head_depth)
    span_value_rows = span_values_all.transpose(0, 2, 1, 3).reshape(
        head_batch, span_total, head_depth
    )
    query_pos = (
        ctx_index * span_dev + jnp.arange(span_dev * group_size, dtype=jnp.int32) // group_size
    )
    causal = (jnp.arange(span_total, dtype=jnp.int32)[None, :] <= query_pos[:, None])[None]
    decode_five = decode_query.reshape(
        steps_count, samples_dev, kv_heads, group_size, head_depth
    ).transpose(2, 0, 1, 3, 4)
    prefill_state = empty_state(head_batch, span_dev * group_size, head_depth)
    along_x, other_core = ctx_shards(jnp.stack([local_keys, local_values]), ctx_count)
    arrived = jnp.concatenate([along_x, other_core], axis=0)
    prompt_keys_all, prompt_values_all = (
        jnp.concatenate([arrived[shard, member] for shard in range(ctx_count)], axis=2)
        for member in range(2)
    )
    prefix_len = prompt_keys_all.shape[2]
    key_rows = prompt_keys_all.reshape(head_batch, prefix_len, head_depth)
    value_rows = prompt_values_all.reshape(head_batch, prefix_len, head_depth)
    prefill_state = sweep(prefill_state, span_rows, key_rows, value_rows, 2048)
    decode_flat = decode_five.reshape(kv_heads, -1, head_depth)
    decode_batch = jnp.broadcast_to(decode_flat[None], (prompts,) + decode_flat.shape).reshape(
        head_batch, -1, head_depth
    )
    decode_state = empty_state(head_batch, decode_flat.shape[1], head_depth)
    decode_state = sweep(decode_state, decode_batch, key_rows, value_rows, 2048)
    decode_state = sweep(decode_state, decode_batch, span_key_rows, span_value_rows, span_total)
    own_prompts = lax.dynamic_slice_in_dim(sample_prompt, ctx_index * samples_dev, samples_dev)
    chosen = (
        own_prompts[None, None, None, :, None]
        == jnp.arange(prompts, dtype=jnp.int32)[:, None, None, None, None]
    )

    def select_prompt(member):
        shaped = member.reshape(
            (prompts, kv_heads, steps_count, samples_dev, group_size) + member.shape[2:]
        )
        select_mask = chosen.reshape(chosen.shape + (1,) * (shaped.ndim - 5))
        return jnp.sum(jnp.where(select_mask, shaped, 0.0), axis=0)

    decode_state = tuple((select_prompt(member) for member in decode_state))
    prefill_state = absorb(prefill_state, span_rows, span_key_rows, span_value_rows, causal)
    span_mixed = (prefill_state[2] / prefill_state[1][..., None]).astype(jnp.bfloat16)
    span_attn = (
        span_mixed.reshape(prompts, kv_heads, span_dev, group_size, head_depth)
        .transpose(0, 2, 1, 3, 4)
        .reshape(prompts * span_dev, heads_dev * head_depth)
    )
    decode_mixed = own_steps(decode_state, decode_five, decode_key, decode_value)
    decode_attn = decode_mixed.transpose(1, 2, 0, 3, 4).reshape(
        steps_count * samples_dev, heads_dev * head_depth
    )
    rows_local = jnp.concatenate([span_attn, decode_attn], axis=0)
    projected = jnp.dot(
        ctx_gather(rows_local, ctx_count).reshape(-1, rows_local.shape[-1]),
        out_weight,
        preferred_element_type=jnp.float32,
    )
    summed = head_sum_line(projected, head_count)
    rows_dev = rows_local.shape[0]
    blocks_by_ctx = summed.reshape(-1, rows_dev, summed.shape[-1])
    span_out = (
        blocks_by_ctx[:, : prompts * span_dev]
        .reshape(ctx_count, prompts, span_dev, -1)
        .transpose(1, 0, 2, 3)
        .reshape(prompts, ctx_count * span_dev, -1)
    )
    decode_out = (
        blocks_by_ctx[:, prompts * span_dev :]
        .reshape(ctx_count, steps_count, samples_dev, -1)
        .transpose(1, 0, 2, 3)
        .reshape(steps_count, ctx_count * samples_dev, -1)
    )
    return (span_out, decode_out)


def solution(mesh):
    return jax.shard_map(
        functools.partial(shards, head_count=mesh.shape["head"]),
        mesh=mesh,
        in_specs=(
            P("groups", "ctx", "head", None),
            P("groups", "ctx", "head", None),
            P("groups", "ctx", "head", None),
            P(("groups", "ctx"), None, "head", None),
            P(("groups", "ctx"), None, "head", None),
            P("groups", "ctx"),
            P("groups", "ctx", "head", None),
            P("groups", "ctx", "head", None),
            P("groups", "ctx", "head", None),
            P("groups"),
            P("head", "ctx"),
        ),
        out_specs=(P("groups", None, "ctx"), P("groups", None, "ctx")),
        check_vma=False,
    )
```

```python
import functools
import math

import jax
import jax.numpy as jnp
from jax import lax
from jax.sharding import PartitionSpec as P

negative_floor = -1e30


def absorb(softmax_state, queries, key_rows, value_rows, allowed):
    running_max, running_sum, weighted = softmax_state
    scores = jnp.einsum("brd,bnd->brn", queries, key_rows, preferred_element_type=jnp.float32) * (
        1.0 / math.sqrt(queries.shape[-1])
    )
    if allowed is not None:
        scores = jnp.where(allowed, scores, negative_floor)
    new_max = jnp.maximum(running_max, jnp.max(scores, axis=-1))
    factor = jnp.exp(running_max - new_max)
    weights = jnp.exp(scores - new_max[..., None])
    running_sum = running_sum * factor + jnp.sum(weights, axis=-1)
    weighted = weighted * factor[..., None] + jnp.einsum(
        "brn,bnd->brd", weights.astype(jnp.bfloat16), value_rows, preferred_element_type=jnp.float32
    )
    return (new_max, running_sum, weighted)


def sweep(softmax_state, queries, key_rows, value_rows, block_width):
    total_keys = key_rows.shape[1]
    block_width = math.gcd(total_keys, block_width)

    def one_block(state_in, block_start):
        key_block = lax.dynamic_slice_in_dim(key_rows, block_start, block_width, 1)
        value_block = lax.dynamic_slice_in_dim(value_rows, block_start, block_width, 1)
        return (absorb(state_in, queries, key_block, value_block, None), None)

    starts = jnp.arange(total_keys // block_width, dtype=jnp.int32) * block_width
    softmax_state, unused = lax.scan(one_block, softmax_state, starts)
    return softmax_state


def empty_state(head_batch, row_count, head_depth):
    return (
        jnp.full((head_batch, row_count), negative_floor, jnp.float32),
        jnp.zeros((head_batch, row_count), jnp.float32),
        jnp.zeros((head_batch, row_count, head_depth), jnp.float32),
    )


def own_steps(softmax_state, queries_five, own_key, own_value):
    running_max, running_sum, weighted = softmax_state
    key_rows = own_key.transpose(2, 1, 0, 3)
    value_rows = own_value.transpose(2, 1, 0, 3)
    scores = jnp.einsum(
        "ktsgd,ksud->ktsgu", queries_five, key_rows, preferred_element_type=jnp.float32
    ) * (1.0 / math.sqrt(queries_five.shape[-1]))
    step_total = queries_five.shape[1]
    step_ids = jnp.arange(step_total, dtype=jnp.int32)
    allowed = (step_ids[None, :] <= step_ids[:, None])[None, :, None, None, :]
    scores = jnp.where(allowed, scores, negative_floor)
    new_max = jnp.maximum(running_max, jnp.max(scores, axis=-1))
    factor = jnp.exp(running_max - new_max)
    weights = jnp.exp(scores - new_max[..., None])
    running_sum = running_sum * factor + jnp.sum(weights, axis=-1)
    weighted = weighted * factor[..., None] + jnp.einsum(
        "ktsgu,ksud->ktsgd",
        weights.astype(jnp.bfloat16),
        value_rows,
        preferred_element_type=jnp.float32,
    )
    return (weighted / running_sum[..., None]).astype(jnp.bfloat16)


def ctx_shards(block, ctx_count):
    chips = ctx_count // 2
    received = [block]
    for shift in range(1, chips):
        pairs = [(dev, (dev - 2 * shift) % ctx_count) for dev in range(ctx_count)]
        received.append(lax.ppermute(block, "ctx", pairs))
    along_x = jnp.stack(received)
    other_core = lax.ppermute(along_x, "ctx", [(dev, dev ^ 1) for dev in range(ctx_count)])
    return along_x, other_core


def ctx_gather(block, ctx_count):
    ctx_index = lax.axis_index("ctx")
    chip, core = ctx_index // 2, ctx_index % 2
    along_x, other_core = ctx_shards(block, ctx_count)
    along_x = jnp.roll(along_x, chip, axis=0)
    other_core = jnp.roll(other_core, chip, axis=0)
    core_zero = jnp.where(core == 0, along_x, other_core)
    core_one = jnp.where(core == 0, other_core, along_x)
    return jnp.stack([core_zero, core_one], axis=1).reshape((ctx_count,) + block.shape)


def head_sum_line(partial, head_count):
    last = head_count - 1
    head_index = lax.axis_index("head")
    blocks = partial.reshape((head_count, -1) + partial.shape[1:])
    rightward = [(dev, dev + 1) for dev in range(last)]
    leftward = [(dev + 1, dev) for dev in range(last)]
    from_left = from_right = None
    for step in range(1, head_count):
        right_block = jnp.clip(head_index + head_count - step, 0, last)
        left_block = jnp.clip(head_index - head_count + step, 0, last)
        going_right = lax.dynamic_index_in_dim(blocks, right_block, 0, False)
        going_left = lax.dynamic_index_in_dim(blocks, left_block, 0, False)
        if from_left is not None:
            going_right = going_right + from_left.astype(jnp.float32)
            going_left = going_left + from_right.astype(jnp.float32)
        from_left = lax.ppermute(going_right.astype(jnp.bfloat16), "head", rightward)
        from_right = lax.ppermute(going_left.astype(jnp.bfloat16), "head", leftward)
    own = lax.dynamic_index_in_dim(blocks, head_index, 0, False)
    mine = (own + from_left.astype(jnp.float32) + from_right.astype(jnp.float32)).astype(jnp.bfloat16)
    lefts, rights = [], []
    send_right = send_left = mine
    for step in range(1, head_count):
        send_right = lax.ppermute(send_right, "head", rightward)
        send_left = lax.ppermute(send_left, "head", leftward)
        lefts.append(send_right)
        rights.append(send_left)
    candidates = jnp.stack([mine] + lefts + rights)
    wanted = jnp.arange(head_count, dtype=jnp.int32)
    pick = jnp.where(
        wanted == head_index,
        0,
        jnp.where(wanted < head_index, head_index - wanted, last + wanted - head_index),
    )
    return jnp.take(candidates, pick, axis=0).reshape(partial.shape)


def shards(
    span_query,
    span_key,
    span_value,
    prefix_key,
    prefix_value,
    page_table,
    decode_query,
    decode_key,
    decode_value,
    sample_prompt,
    out_weight,
    head_count,
):
    prompts, span_dev, heads_dev, head_depth = span_query.shape
    kv_heads = span_key.shape[2]
    group_size = heads_dev // kv_heads
    steps_count = decode_query.shape[0]
    samples_dev = decode_query.shape[1]
    head_batch = prompts * kv_heads
    ctx_index = lax.axis_index("ctx")
    slot_pick = (
        page_table[:, :, None] == jnp.arange(prefix_key.shape[0], dtype=jnp.int32)
    ).astype(prefix_key.dtype)
    own_pages = (
        jnp.einsum(
            "pjs,msqkd->mpkjqd",
            slot_pick,
            jnp.stack([prefix_key, prefix_value]),
            preferred_element_type=jnp.float32,
        )
        .astype(prefix_key.dtype)
        .reshape(2, prompts, kv_heads, -1, head_depth)
    )
    span_rows = (
        span_query.reshape(prompts, span_dev, kv_heads, group_size, head_depth)
        .transpose(0, 2, 1, 3, 4)
        .reshape(head_batch, span_dev * group_size, head_depth)
    )
    ctx_count = sample_prompt.shape[0] // samples_dev
    span_pair = ctx_gather(jnp.stack([span_key, span_value]), ctx_count)
    span_keys_all, span_values_all = (
        span_pair[:, member].transpose(1, 0, 2, 3, 4).reshape(
            (prompts, ctx_count * span_dev) + span_key.shape[2:]
        )
        for member in range(2)
    )
    span_total = span_keys_all.shape[1]
    span_key_rows = span_keys_all.transpose(0, 2, 1, 3).reshape(head_batch, span_total, head_depth)
    span_value_rows = span_values_all.transpose(0, 2, 1, 3).reshape(
        head_batch, span_total, head_depth
    )
    query_pos = (
        ctx_index * span_dev + jnp.arange(span_dev * group_size, dtype=jnp.int32) // group_size
    )
    causal = (jnp.arange(span_total, dtype=jnp.int32)[None, :] <= query_pos[:, None])[None]
    decode_five = decode_query.reshape(
        steps_count, samples_dev, kv_heads, group_size, head_depth
    ).transpose(2, 0, 1, 3, 4)
    prefill_state = empty_state(head_batch, span_dev * group_size, head_depth)
    along_x, other_core = ctx_shards(own_pages, ctx_count)
    arrived = jnp.concatenate([along_x, other_core], axis=0)
    prompt_keys_all, prompt_values_all = (
        jnp.concatenate([arrived[shard, member] for shard in range(ctx_count)], axis=2)
        for member in range(2)
    )
    prefix_len = prompt_keys_all.shape[2]
    key_rows = prompt_keys_all.reshape(head_batch, prefix_len, head_depth)
    value_rows = prompt_values_all.reshape(head_batch, prefix_len, head_depth)
    prefill_state = sweep(prefill_state, span_rows, key_rows, value_rows, 2048)
    decode_flat = decode_five.reshape(kv_heads, -1, head_depth)
    decode_batch = jnp.broadcast_to(decode_flat[None], (prompts,) + decode_flat.shape).reshape(
        head_batch, -1, head_depth
    )
    decode_state = empty_state(head_batch, decode_flat.shape[1], head_depth)
    decode_state = sweep(decode_state, decode_batch, key_rows, value_rows, 2048)
    decode_state = sweep(decode_state, decode_batch, span_key_rows, span_value_rows, span_total)
    own_prompts = lax.dynamic_slice_in_dim(sample_prompt, ctx_index * samples_dev, samples_dev)
    chosen = (
        own_prompts[None, None, None, :, None]
        == jnp.arange(prompts, dtype=jnp.int32)[:, None, None, None, None]
    )

    def select_prompt(member):
        shaped = member.reshape(
            (prompts, kv_heads, steps_count, samples_dev, group_size) + member.shape[2:]
        )
        select_mask = chosen.reshape(chosen.shape + (1,) * (shaped.ndim - 5))
        return jnp.sum(jnp.where(select_mask, shaped, 0.0), axis=0)

    decode_state = tuple((select_prompt(member) for member in decode_state))
    prefill_state = absorb(prefill_state, span_rows, span_key_rows, span_value_rows, causal)
    span_mixed = (prefill_state[2] / prefill_state[1][..., None]).astype(jnp.bfloat16)
    span_attn = (
        span_mixed.reshape(prompts, kv_heads, span_dev, group_size, head_depth)
        .transpose(0, 2, 1, 3, 4)
        .reshape(prompts * span_dev, heads_dev * head_depth)
    )
    decode_mixed = own_steps(decode_state, decode_five, decode_key, decode_value)
    decode_attn = decode_mixed.transpose(1, 2, 0, 3, 4).reshape(
        steps_count * samples_dev, heads_dev * head_depth
    )
    rows_local = jnp.concatenate([span_attn, decode_attn], axis=0)
    projected = jnp.dot(
        ctx_gather(rows_local, ctx_count).reshape(-1, rows_local.shape[-1]),
        out_weight,
        preferred_element_type=jnp.float32,
    )
    summed = head_sum_line(projected, head_count)
    rows_dev = rows_local.shape[0]
    blocks_by_ctx = summed.reshape(-1, rows_dev, summed.shape[-1])
    span_out = (
        blocks_by_ctx[:, : prompts * span_dev]
        .reshape(ctx_count, prompts, span_dev, -1)
        .transpose(1, 0, 2, 3)
        .reshape(prompts, ctx_count * span_dev, -1)
    )
    decode_out = (
        blocks_by_ctx[:, prompts * span_dev :]
        .reshape(ctx_count, steps_count, samples_dev, -1)
        .transpose(1, 0, 2, 3)
        .reshape(steps_count, ctx_count * samples_dev, -1)
    )
    return (span_out, decode_out)


def solution(mesh):
    return jax.shard_map(
        functools.partial(shards, head_count=mesh.shape["head"]),
        mesh=mesh,
        in_specs=(
            P("groups", "ctx", "head", None),
            P("groups", "ctx", "head", None),
            P("groups", "ctx", "head", None),
            P(("groups", "ctx"), None, "head", None),
            P(("groups", "ctx"), None, "head", None),
            P("groups", "ctx"),
            P("groups", "ctx", "head", None),
            P("groups", "ctx", "head", None),
            P("groups", "ctx", "head", None),
            P("groups"),
            P("head", "ctx"),
        ),
        out_specs=(P("groups", None, "ctx"), P("groups", None, "ctx")),
        check_vma=False,
    )
```

```python
import functools
import math

import jax
import jax.numpy as jnp
from jax import lax
from jax.sharding import PartitionSpec as P

negative_floor = -1e30


def absorb(softmax_state, queries, key_rows, value_rows, allowed):
    running_max, running_sum, weighted = softmax_state
    scores = jnp.einsum("brd,bnd->brn", queries, key_rows, preferred_element_type=jnp.float32) * (
        1.0 / math.sqrt(queries.shape[-1])
    )
    if allowed is not None:
        scores = jnp.where(allowed, scores, negative_floor)
    new_max = jnp.maximum(running_max, jnp.max(scores, axis=-1))
    factor = jnp.exp(running_max - new_max)
    weights = jnp.exp(scores - new_max[..., None])
    running_sum = running_sum * factor + jnp.sum(weights, axis=-1)
    weighted = weighted * factor[..., None] + jnp.einsum(
        "brn,bnd->brd", weights.astype(jnp.bfloat16), value_rows, preferred_element_type=jnp.float32
    )
    return (new_max, running_sum, weighted)


def sweep(softmax_state, queries, key_rows, value_rows, block_width):
    total_keys = key_rows.shape[1]
    block_width = math.gcd(total_keys, block_width)

    def one_block(state_in, block_start):
        key_block = lax.dynamic_slice_in_dim(key_rows, block_start, block_width, 1)
        value_block = lax.dynamic_slice_in_dim(value_rows, block_start, block_width, 1)
        return (absorb(state_in, queries, key_block, value_block, None), None)

    starts = jnp.arange(total_keys // block_width, dtype=jnp.int32) * block_width
    softmax_state, unused = lax.scan(one_block, softmax_state, starts)
    return softmax_state


def empty_state(head_batch, row_count, head_depth):
    return (
        jnp.full((head_batch, row_count), negative_floor, jnp.float32),
        jnp.zeros((head_batch, row_count), jnp.float32),
        jnp.zeros((head_batch, row_count, head_depth), jnp.float32),
    )


def own_steps(softmax_state, queries_five, own_key, own_value):
    running_max, running_sum, weighted = softmax_state
    key_rows = own_key.transpose(2, 1, 0, 3)
    value_rows = own_value.transpose(2, 1, 0, 3)
    scores = jnp.einsum(
        "ktsgd,ksud->ktsgu", queries_five, key_rows, preferred_element_type=jnp.float32
    ) * (1.0 / math.sqrt(queries_five.shape[-1]))
    step_total = queries_five.shape[1]
    step_ids = jnp.arange(step_total, dtype=jnp.int32)
    allowed = (step_ids[None, :] <= step_ids[:, None])[None, :, None, None, :]
    scores = jnp.where(allowed, scores, negative_floor)
    new_max = jnp.maximum(running_max, jnp.max(scores, axis=-1))
    factor = jnp.exp(running_max - new_max)
    weights = jnp.exp(scores - new_max[..., None])
    running_sum = running_sum * factor + jnp.sum(weights, axis=-1)
    weighted = weighted * factor[..., None] + jnp.einsum(
        "ktsgu,ksud->ktsgd",
        weights.astype(jnp.bfloat16),
        value_rows,
        preferred_element_type=jnp.float32,
    )
    return (weighted / running_sum[..., None]).astype(jnp.bfloat16)


def ctx_shards(block, ctx_count):
    chips = ctx_count // 2
    received = [block]
    for shift in range(1, chips):
        pairs = [(dev, (dev - 2 * shift) % ctx_count) for dev in range(ctx_count)]
        received.append(lax.ppermute(block, "ctx", pairs))
    along_x = jnp.stack(received)
    other_core = lax.ppermute(along_x, "ctx", [(dev, dev ^ 1) for dev in range(ctx_count)])
    return along_x, other_core


def ctx_gather(block, ctx_count):
    ctx_index = lax.axis_index("ctx")
    chip, core = ctx_index // 2, ctx_index % 2
    along_x, other_core = ctx_shards(block, ctx_count)
    along_x = jnp.roll(along_x, chip, axis=0)
    other_core = jnp.roll(other_core, chip, axis=0)
    core_zero = jnp.where(core == 0, along_x, other_core)
    core_one = jnp.where(core == 0, other_core, along_x)
    return jnp.stack([core_zero, core_one], axis=1).reshape((ctx_count,) + block.shape)


def head_sum_line(partial, head_count):
    last = head_count - 1
    head_index = lax.axis_index("head")
    blocks = partial.reshape((head_count, -1) + partial.shape[1:])
    rightward = [(dev, dev + 1) for dev in range(last)]
    leftward = [(dev + 1, dev) for dev in range(last)]
    from_left = from_right = None
    for step in range(1, head_count):
        right_block = jnp.clip(head_index + head_count - step, 0, last)
        left_block = jnp.clip(head_index - head_count + step, 0, last)
        going_right = lax.dynamic_index_in_dim(blocks, right_block, 0, False)
        going_left = lax.dynamic_index_in_dim(blocks, left_block, 0, False)
        if from_left is not None:
            going_right = going_right + from_left.astype(jnp.float32)
            going_left = going_left + from_right.astype(jnp.float32)
        from_left = lax.ppermute(going_right.astype(jnp.bfloat16), "head", rightward)
        from_right = lax.ppermute(going_left.astype(jnp.bfloat16), "head", leftward)
    own = lax.dynamic_index_in_dim(blocks, head_index, 0, False)
    mine = (own + from_left.astype(jnp.float32) + from_right.astype(jnp.float32)).astype(jnp.bfloat16)
    lefts, rights = [], []
    send_right = send_left = mine
    for step in range(1, head_count):
        send_right = lax.ppermute(send_right, "head", rightward)
        send_left = lax.ppermute(send_left, "head", leftward)
        lefts.append(send_right)
        rights.append(send_left)
    candidates = jnp.stack([mine] + lefts + rights)
    wanted = jnp.arange(head_count, dtype=jnp.int32)
    pick = jnp.where(
        wanted == head_index,
        0,
        jnp.where(wanted < head_index, head_index - wanted, last + wanted - head_index),
    )
    return jnp.take(candidates, pick, axis=0).reshape(partial.shape)


def shards(
    span_query,
    span_key,
    span_value,
    prefix_key,
    prefix_value,
    page_table,
    decode_query,
    decode_key,
    decode_value,
    sample_prompt,
    out_weight,
    head_count,
):
    prompts, span_dev, heads_dev, head_depth = span_query.shape
    kv_heads = span_key.shape[2]
    group_size = heads_dev // kv_heads
    steps_count = decode_query.shape[0]
    samples_dev = decode_query.shape[1]
    head_batch = prompts * kv_heads
    ctx_index = lax.axis_index("ctx")
    slot_pick = (
        page_table[:, :, None] == jnp.arange(prefix_key.shape[0], dtype=jnp.int32)
    ).astype(prefix_key.dtype)
    local_keys, local_values = (
        jnp.einsum("pjs,sqkd->pkjqd", slot_pick, pages, preferred_element_type=jnp.float32)
        .astype(pages.dtype)
        .reshape(prompts, kv_heads, -1, head_depth)
        for pages in (prefix_key, prefix_value)
    )
    span_rows = (
        span_query.reshape(prompts, span_dev, kv_heads, group_size, head_depth)
        .transpose(0, 2, 1, 3, 4)
        .reshape(head_batch, span_dev * group_size, head_depth)
    )
    ctx_count = sample_prompt.shape[0] // samples_dev
    span_pair = ctx_gather(jnp.stack([span_key, span_value]), ctx_count)
    span_keys_all, span_values_all = (
        span_pair[:, member].transpose(1, 0, 2, 3, 4).reshape(
            (prompts, ctx_count * span_dev) + span_key.shape[2:]
        )
        for member in range(2)
    )
    span_total = span_keys_all.shape[1]
    span_key_rows = span_keys_all.transpose(0, 2, 1, 3).reshape(head_batch, span_total, head_depth)
    span_value_rows = span_values_all.transpose(0, 2, 1, 3).reshape(
        head_batch, span_total, head_depth
    )
    query_pos = (
        ctx_index * span_dev + jnp.arange(span_dev * group_size, dtype=jnp.int32) // group_size
    )
    causal = (jnp.arange(span_total, dtype=jnp.int32)[None, :] <= query_pos[:, None])[None]
    decode_five = decode_query.reshape(
        steps_count, samples_dev, kv_heads, group_size, head_depth
    ).transpose(2, 0, 1, 3, 4)
    prefill_state = empty_state(head_batch, span_dev * group_size, head_depth)
    own_pages = jnp.stack([local_keys, local_values])
    core_pairs = [(dev, dev ^ 1) for dev in range(ctx_count)]
    along_x = [
        lax.ppermute(own_pages, "ctx", [(dev, (dev - 2 * shift) % ctx_count) for dev in range(ctx_count)])
        for shift in range(1, ctx_count // 2)
    ]
    arrived = [own_pages, lax.ppermute(own_pages, "ctx", core_pairs)] + along_x
    arrived += [lax.ppermute(pages, "ctx", core_pairs) for pages in along_x]
    prompt_keys_all, prompt_values_all = (
        jnp.concatenate([pages[member] for pages in arrived], axis=2) for member in range(2)
    )
    prefix_len = prompt_keys_all.shape[2]
    key_rows = prompt_keys_all.reshape(head_batch, prefix_len, head_depth)
    value_rows = prompt_values_all.reshape(head_batch, prefix_len, head_depth)
    prefill_state = sweep(prefill_state, span_rows, key_rows, value_rows, 2048)
    decode_flat = decode_five.reshape(kv_heads, -1, head_depth)
    decode_batch = jnp.broadcast_to(decode_flat[None], (prompts,) + decode_flat.shape).reshape(
        head_batch, -1, head_depth
    )
    decode_state = empty_state(head_batch, decode_flat.shape[1], head_depth)
    decode_state = sweep(decode_state, decode_batch, key_rows, value_rows, 2048)
    decode_state = sweep(decode_state, decode_batch, span_key_rows, span_value_rows, span_total)
    own_prompts = lax.dynamic_slice_in_dim(sample_prompt, ctx_index * samples_dev, samples_dev)
    chosen = (
        own_prompts[None, None, None, :, None]
        == jnp.arange(prompts, dtype=jnp.int32)[:, None, None, None, None]
    )

    def select_prompt(member):
        shaped = member.reshape(
            (prompts, kv_heads, steps_count, samples_dev, group_size) + member.shape[2:]
        )
        select_mask = chosen.reshape(chosen.shape + (1,) * (shaped.ndim - 5))
        return jnp.sum(jnp.where(select_mask, shaped, 0.0), axis=0)

    decode_state = tuple((select_prompt(member) for member in decode_state))
    prefill_state = absorb(prefill_state, span_rows, span_key_rows, span_value_rows, causal)
    span_mixed = (prefill_state[2] / prefill_state[1][..., None]).astype(jnp.bfloat16)
    span_attn = (
        span_mixed.reshape(prompts, kv_heads, span_dev, group_size, head_depth)
        .transpose(0, 2, 1, 3, 4)
        .reshape(prompts * span_dev, heads_dev * head_depth)
    )
    decode_mixed = own_steps(decode_state, decode_five, decode_key, decode_value)
    decode_attn = decode_mixed.transpose(1, 2, 0, 3, 4).reshape(
        steps_count * samples_dev, heads_dev * head_depth
    )
    rows_local = jnp.concatenate([span_attn, decode_attn], axis=0)
    projected = jnp.dot(
        ctx_gather(rows_local, ctx_count).reshape(-1, rows_local.shape[-1]),
        out_weight,
        preferred_element_type=jnp.float32,
    )
    summed = head_sum_line(projected, head_count)
    rows_dev = rows_local.shape[0]
    blocks_by_ctx = summed.reshape(-1, rows_dev, summed.shape[-1])
    span_out = (
        blocks_by_ctx[:, : prompts * span_dev]
        .reshape(ctx_count, prompts, span_dev, -1)
        .transpose(1, 0, 2, 3)
        .reshape(prompts, ctx_count * span_dev, -1)
    )
    decode_out = (
        blocks_by_ctx[:, prompts * span_dev :]
        .reshape(ctx_count, steps_count, samples_dev, -1)
        .transpose(1, 0, 2, 3)
        .reshape(steps_count, ctx_count * samples_dev, -1)
    )
    return (span_out, decode_out)


def solution(mesh):
    return jax.shard_map(
        functools.partial(shards, head_count=mesh.shape["head"]),
        mesh=mesh,
        in_specs=(
            P("groups", "ctx", "head", None),
            P("groups", "ctx", "head", None),
            P("groups", "ctx", "head", None),
            P(("groups", "ctx"), None, "head", None),
            P(("groups", "ctx"), None, "head", None),
            P("groups", "ctx"),
            P("groups", "ctx", "head", None),
            P("groups", "ctx", "head", None),
            P("groups", "ctx", "head", None),
            P("groups"),
            P("head", "ctx"),
        ),
        out_specs=(P("groups", None, "ctx"), P("groups", None, "ctx")),
        check_vma=False,
    )
```

```python
import functools
import math

import jax
import jax.numpy as jnp
from jax import lax
from jax.sharding import PartitionSpec as P

negative_floor = -1e30


def absorb(softmax_state, queries, key_rows, value_rows, allowed):
    running_max, running_sum, weighted = softmax_state
    scores = jnp.einsum("brd,bnd->brn", queries, key_rows, preferred_element_type=jnp.float32) * (
        1.0 / math.sqrt(queries.shape[-1])
    )
    if allowed is not None:
        scores = jnp.where(allowed, scores, negative_floor)
    new_max = jnp.maximum(running_max, jnp.max(scores, axis=-1))
    factor = jnp.exp(running_max - new_max)
    weights = jnp.exp(scores - new_max[..., None])
    running_sum = running_sum * factor + jnp.sum(weights, axis=-1)
    weighted = weighted * factor[..., None] + jnp.einsum(
        "brn,bnd->brd", weights.astype(jnp.bfloat16), value_rows, preferred_element_type=jnp.float32
    )
    return (new_max, running_sum, weighted)


def sweep(softmax_state, queries, key_rows, value_rows, block_width):
    total_keys = key_rows.shape[1]
    block_width = math.gcd(total_keys, block_width)

    def one_block(state_in, block_start):
        key_block = lax.dynamic_slice_in_dim(key_rows, block_start, block_width, 1)
        value_block = lax.dynamic_slice_in_dim(value_rows, block_start, block_width, 1)
        return (absorb(state_in, queries, key_block, value_block, None), None)

    starts = jnp.arange(total_keys // block_width, dtype=jnp.int32) * block_width
    softmax_state, unused = lax.scan(one_block, softmax_state, starts)
    return softmax_state


def empty_state(head_batch, row_count, head_depth):
    return (
        jnp.full((head_batch, row_count), negative_floor, jnp.float32),
        jnp.zeros((head_batch, row_count), jnp.float32),
        jnp.zeros((head_batch, row_count, head_depth), jnp.float32),
    )


def own_steps(softmax_state, queries_five, own_key, own_value):
    running_max, running_sum, weighted = softmax_state
    key_rows = own_key.transpose(2, 1, 0, 3)
    value_rows = own_value.transpose(2, 1, 0, 3)
    scores = jnp.einsum(
        "ktsgd,ksud->ktsgu", queries_five, key_rows, preferred_element_type=jnp.float32
    ) * (1.0 / math.sqrt(queries_five.shape[-1]))
    step_total = queries_five.shape[1]
    step_ids = jnp.arange(step_total, dtype=jnp.int32)
    allowed = (step_ids[None, :] <= step_ids[:, None])[None, :, None, None, :]
    scores = jnp.where(allowed, scores, negative_floor)
    new_max = jnp.maximum(running_max, jnp.max(scores, axis=-1))
    factor = jnp.exp(running_max - new_max)
    weights = jnp.exp(scores - new_max[..., None])
    running_sum = running_sum * factor + jnp.sum(weights, axis=-1)
    weighted = weighted * factor[..., None] + jnp.einsum(
        "ktsgu,ksud->ktsgd",
        weights.astype(jnp.bfloat16),
        value_rows,
        preferred_element_type=jnp.float32,
    )
    return (weighted / running_sum[..., None]).astype(jnp.bfloat16)


def ctx_shards(block, ctx_count):
    chips = ctx_count // 2
    received = [block]
    for shift in range(1, chips):
        pairs = [(dev, (dev - 2 * shift) % ctx_count) for dev in range(ctx_count)]
        received.append(lax.ppermute(block, "ctx", pairs))
    along_x = jnp.stack(received)
    other_core = lax.ppermute(along_x, "ctx", [(dev, dev ^ 1) for dev in range(ctx_count)])
    return along_x, other_core


def ctx_gather(block, ctx_count, axis=0):
    ctx_index = lax.axis_index("ctx")
    chip, core = ctx_index // 2, ctx_index % 2
    along_x, other_core = ctx_shards(block, ctx_count)
    along_x = jnp.roll(along_x, chip, axis=0)
    other_core = jnp.roll(other_core, chip, axis=0)
    core_zero = jnp.where(core == 0, along_x, other_core)
    core_one = jnp.where(core == 0, other_core, along_x)
    joined = jnp.moveaxis(jnp.stack([core_zero, core_one], axis=1), (0, 1), (axis, axis + 1))
    return joined.reshape(block.shape[:axis] + (-1,) + block.shape[axis + 1 :])


def head_sum_line(partials, head_count):
    last = head_count - 1
    head_index = lax.axis_index("head")
    pieces = [part.reshape((head_count, -1) + part.shape[1:]) for part in partials]

    def take_block(index):
        return jnp.concatenate(
            [lax.dynamic_index_in_dim(piece, index, 0, False) for piece in pieces], axis=0
        )

    rightward = [(dev, dev + 1) for dev in range(last)]
    leftward = [(dev + 1, dev) for dev in range(last)]
    from_left = from_right = None
    for step in range(1, head_count):
        right_block = jnp.clip(head_index + head_count - step, 0, last)
        left_block = jnp.clip(head_index - head_count + step, 0, last)
        going_right = take_block(right_block)
        going_left = take_block(left_block)
        if from_left is not None:
            going_right = going_right + from_left.astype(jnp.float32)
            going_left = going_left + from_right.astype(jnp.float32)
        from_left = lax.ppermute(going_right.astype(jnp.bfloat16), "head", rightward)
        from_right = lax.ppermute(going_left.astype(jnp.bfloat16), "head", leftward)
    own = take_block(head_index)
    mine = (own + from_left.astype(jnp.float32) + from_right.astype(jnp.float32)).astype(jnp.bfloat16)
    lefts, rights = [], []
    send_right = send_left = mine
    for step in range(1, head_count):
        send_right = lax.ppermute(send_right, "head", rightward)
        send_left = lax.ppermute(send_left, "head", leftward)
        lefts.append(send_right)
        rights.append(send_left)
    candidates = jnp.stack([mine] + lefts + rights)
    wanted = jnp.arange(head_count, dtype=jnp.int32)
    pick = jnp.where(
        wanted == head_index,
        0,
        jnp.where(wanted < head_index, head_index - wanted, last + wanted - head_index),
    )
    return jnp.take(candidates, pick, axis=0)


def shards(
    span_query,
    span_key,
    span_value,
    prefix_key,
    prefix_value,
    page_table,
    decode_query,
    decode_key,
    decode_value,
    sample_prompt,
    out_weight,
    head_count,
):
    prompts, span_dev, heads_dev, head_depth = span_query.shape
    kv_heads = span_key.shape[2]
    group_size = heads_dev // kv_heads
    steps_count = decode_query.shape[0]
    samples_dev = decode_query.shape[1]
    head_batch = prompts * kv_heads
    ctx_index = lax.axis_index("ctx")
    slot_pick = (
        page_table[:, :, None] == jnp.arange(prefix_key.shape[0], dtype=jnp.int32)
    ).astype(prefix_key.dtype)
    local_keys, local_values = (
        jnp.einsum("pjs,sqkd->pkjqd", slot_pick, pages, preferred_element_type=jnp.float32)
        .astype(pages.dtype)
        .reshape(prompts, kv_heads, -1, head_depth)
        for pages in (prefix_key, prefix_value)
    )
    span_rows = (
        span_query.reshape(prompts, span_dev, kv_heads, group_size, head_depth)
        .transpose(0, 2, 1, 3, 4)
        .reshape(head_batch, span_dev * group_size, head_depth)
    )
    ctx_count = sample_prompt.shape[0] // samples_dev
    span_pair = ctx_gather(jnp.stack([span_key, span_value]), ctx_count, axis=2)
    span_keys_all, span_values_all = span_pair[0], span_pair[1]
    span_total = span_keys_all.shape[1]
    span_key_rows = span_keys_all.transpose(0, 2, 1, 3).reshape(head_batch, span_total, head_depth)
    span_value_rows = span_values_all.transpose(0, 2, 1, 3).reshape(
        head_batch, span_total, head_depth
    )
    query_pos = (
        ctx_index * span_dev + jnp.arange(span_dev * group_size, dtype=jnp.int32) // group_size
    )
    causal = (jnp.arange(span_total, dtype=jnp.int32)[None, :] <= query_pos[:, None])[None]
    decode_five = decode_query.reshape(
        steps_count, samples_dev, kv_heads, group_size, head_depth
    ).transpose(2, 0, 1, 3, 4)
    prefill_state = empty_state(head_batch, span_dev * group_size, head_depth)
    own_pages = jnp.stack([local_keys, local_values])
    core_pairs = [(dev, dev ^ 1) for dev in range(ctx_count)]
    along_x = [
        lax.ppermute(own_pages, "ctx", [(dev, (dev - 2 * shift) % ctx_count) for dev in range(ctx_count)])
        for shift in range(1, ctx_count // 2)
    ]
    arrived = [own_pages, lax.ppermute(own_pages, "ctx", core_pairs)] + along_x
    arrived += [lax.ppermute(pages, "ctx", core_pairs) for pages in along_x]
    prompt_keys_all, prompt_values_all = (
        jnp.concatenate([pages[member] for pages in arrived], axis=2) for member in range(2)
    )
    prefix_len = prompt_keys_all.shape[2]
    key_rows = prompt_keys_all.reshape(head_batch, prefix_len, head_depth)
    value_rows = prompt_values_all.reshape(head_batch, prefix_len, head_depth)
    prefill_state = sweep(prefill_state, span_rows, key_rows, value_rows, 2048)
    decode_flat = decode_five.reshape(kv_heads, -1, head_depth)
    decode_batch = jnp.broadcast_to(decode_flat[None], (prompts,) + decode_flat.shape).reshape(
        head_batch, -1, head_depth
    )
    decode_state = empty_state(head_batch, decode_flat.shape[1], head_depth)
    decode_state = sweep(decode_state, decode_batch, key_rows, value_rows, 2048)
    decode_state = sweep(decode_state, decode_batch, span_key_rows, span_value_rows, span_total)
    own_prompts = lax.dynamic_slice_in_dim(sample_prompt, ctx_index * samples_dev, samples_dev)
    chosen = (
        own_prompts[None, None, None, :, None]
        == jnp.arange(prompts, dtype=jnp.int32)[:, None, None, None, None]
    )

    def select_prompt(member):
        shaped = member.reshape(
            (prompts, kv_heads, steps_count, samples_dev, group_size) + member.shape[2:]
        )
        select_mask = chosen.reshape(chosen.shape + (1,) * (shaped.ndim - 5))
        return jnp.sum(jnp.where(select_mask, shaped, 0.0), axis=0)

    decode_state = tuple((select_prompt(member) for member in decode_state))
    prefill_state = absorb(prefill_state, span_rows, span_key_rows, span_value_rows, causal)
    span_mixed = (prefill_state[2] / prefill_state[1][..., None]).astype(jnp.bfloat16)
    span_attn = (
        span_mixed.reshape(prompts, kv_heads, span_dev, group_size, head_depth)
        .transpose(0, 2, 1, 3, 4)
        .reshape(prompts, span_dev, heads_dev * head_depth)
    )
    span_rows_all = ctx_gather(span_attn, ctx_count, axis=1)
    span_partial = jnp.dot(
        span_rows_all.reshape(-1, span_rows_all.shape[-1]), out_weight, preferred_element_type=jnp.float32
    )
    decode_mixed = own_steps(decode_state, decode_five, decode_key, decode_value)
    decode_attn = decode_mixed.transpose(1, 2, 0, 3, 4).reshape(
        steps_count, samples_dev, heads_dev * head_depth
    )
    decode_rows_all = ctx_gather(decode_attn, ctx_count, axis=1)
    decode_partial = jnp.dot(
        decode_rows_all.reshape(-1, decode_rows_all.shape[-1]), out_weight, preferred_element_type=jnp.float32
    )
    summed = head_sum_line((span_partial, decode_partial), head_count)
    span_block = span_partial.shape[0] // head_count
    span_out = summed[:, :span_block].reshape(span_rows_all.shape[:-1] + (-1,))
    decode_out = summed[:, span_block:].reshape(decode_rows_all.shape[:-1] + (-1,))
    return (span_out, decode_out)


def solution(mesh):
    return jax.shard_map(
        functools.partial(shards, head_count=mesh.shape["head"]),
        mesh=mesh,
        in_specs=(
            P("groups", "ctx", "head", None),
            P("groups", "ctx", "head", None),
            P("groups", "ctx", "head", None),
            P(("groups", "ctx"), None, "head", None),
            P(("groups", "ctx"), None, "head", None),
            P("groups", "ctx"),
            P("groups", "ctx", "head", None),
            P("groups", "ctx", "head", None),
            P("groups", "ctx", "head", None),
            P("groups"),
            P("head", "ctx"),
        ),
        out_specs=(P("groups", None, "ctx"), P("groups", None, "ctx")),
        check_vma=False,
    )
```

```python
import functools
import math

import jax
import jax.numpy as jnp
from jax import lax
from jax.sharding import PartitionSpec as P

negative_floor = -1e30


def absorb(softmax_state, queries, key_rows, value_rows, allowed):
    running_max, running_sum, weighted = softmax_state
    scores = jnp.einsum("brd,bnd->brn", queries, key_rows, preferred_element_type=jnp.float32) * (
        1.0 / math.sqrt(queries.shape[-1])
    )
    if allowed is not None:
        scores = jnp.where(allowed, scores, negative_floor)
    new_max = jnp.maximum(running_max, jnp.max(scores, axis=-1))
    factor = jnp.exp(running_max - new_max)
    weights = jnp.exp(scores - new_max[..., None])
    running_sum = running_sum * factor + jnp.sum(weights, axis=-1)
    weighted = weighted * factor[..., None] + jnp.einsum(
        "brn,bnd->brd", weights.astype(jnp.bfloat16), value_rows, preferred_element_type=jnp.float32
    )
    return (new_max, running_sum, weighted)


def sweep(softmax_state, queries, key_rows, value_rows, block_width):
    total_keys = key_rows.shape[1]
    block_width = math.gcd(total_keys, block_width)

    def one_block(state_in, block_start):
        key_block = lax.dynamic_slice_in_dim(key_rows, block_start, block_width, 1)
        value_block = lax.dynamic_slice_in_dim(value_rows, block_start, block_width, 1)
        return (absorb(state_in, queries, key_block, value_block, None), None)

    starts = jnp.arange(total_keys // block_width, dtype=jnp.int32) * block_width
    softmax_state, unused = lax.scan(one_block, softmax_state, starts)
    return softmax_state


def empty_state(head_batch, row_count, head_depth):
    return (
        jnp.full((head_batch, row_count), negative_floor, jnp.float32),
        jnp.zeros((head_batch, row_count), jnp.float32),
        jnp.zeros((head_batch, row_count, head_depth), jnp.float32),
    )


def own_steps(softmax_state, queries_five, own_key, own_value):
    running_max, running_sum, weighted = softmax_state
    key_rows = own_key.transpose(2, 1, 0, 3)
    value_rows = own_value.transpose(2, 1, 0, 3)
    scores = jnp.einsum(
        "ktsgd,ksud->ktsgu", queries_five, key_rows, preferred_element_type=jnp.float32
    ) * (1.0 / math.sqrt(queries_five.shape[-1]))
    step_total = queries_five.shape[1]
    step_ids = jnp.arange(step_total, dtype=jnp.int32)
    allowed = (step_ids[None, :] <= step_ids[:, None])[None, :, None, None, :]
    scores = jnp.where(allowed, scores, negative_floor)
    new_max = jnp.maximum(running_max, jnp.max(scores, axis=-1))
    factor = jnp.exp(running_max - new_max)
    weights = jnp.exp(scores - new_max[..., None])
    running_sum = running_sum * factor + jnp.sum(weights, axis=-1)
    weighted = weighted * factor[..., None] + jnp.einsum(
        "ktsgu,ksud->ktsgd",
        weights.astype(jnp.bfloat16),
        value_rows,
        preferred_element_type=jnp.float32,
    )
    return (weighted / running_sum[..., None]).astype(jnp.bfloat16)


def ctx_shards(block, ctx_count):
    chips = ctx_count // 2
    received = [block]
    for shift in range(1, chips):
        pairs = [(dev, (dev - 2 * shift) % ctx_count) for dev in range(ctx_count)]
        received.append(lax.ppermute(block, "ctx", pairs))
    along_x = jnp.stack(received)
    other_core = lax.ppermute(along_x, "ctx", [(dev, dev ^ 1) for dev in range(ctx_count)])
    return along_x, other_core


def ctx_gather(block, ctx_count, axis=0):
    ctx_index = lax.axis_index("ctx")
    chip, core = ctx_index // 2, ctx_index % 2
    along_x, other_core = ctx_shards(block, ctx_count)
    along_x = jnp.roll(along_x, chip, axis=0)
    other_core = jnp.roll(other_core, chip, axis=0)
    core_zero = jnp.where(core == 0, along_x, other_core)
    core_one = jnp.where(core == 0, other_core, along_x)
    joined = jnp.moveaxis(jnp.stack([core_zero, core_one], axis=1), (0, 1), (axis, axis + 1))
    return joined.reshape(block.shape[:axis] + (-1,) + block.shape[axis + 1 :])


def head_sum_line(partials, head_count):
    last = head_count - 1
    head_index = lax.axis_index("head")
    pieces = [part.reshape((head_count, -1) + part.shape[1:]) for part in partials]

    def take_block(index):
        return jnp.concatenate(
            [lax.dynamic_index_in_dim(piece, index, 0, False) for piece in pieces], axis=0
        )

    rightward = [(dev, dev + 1) for dev in range(last)]
    leftward = [(dev + 1, dev) for dev in range(last)]
    from_left = from_right = None
    for step in range(1, head_count):
        right_block = jnp.clip(head_index + head_count - step, 0, last)
        left_block = jnp.clip(head_index - head_count + step, 0, last)
        going_right = take_block(right_block)
        going_left = take_block(left_block)
        if from_left is not None:
            going_right = going_right + from_left.astype(jnp.float32)
            going_left = going_left + from_right.astype(jnp.float32)
        from_left = lax.ppermute(going_right.astype(jnp.bfloat16), "head", rightward)
        from_right = lax.ppermute(going_left.astype(jnp.bfloat16), "head", leftward)
    own = take_block(head_index)
    mine = (own + from_left.astype(jnp.float32) + from_right.astype(jnp.float32)).astype(jnp.bfloat16)
    sizes = [piece.shape[1] for piece in pieces]
    outs = [jnp.zeros((head_count,) + piece.shape[1:], mine.dtype) for piece in pieces]

    def place(outs, block, index, valid):
        safe = jnp.clip(index, 0, last)
        placed, start = [], 0
        for out, size in zip(outs, sizes):
            part = block[start : start + size]
            start += size
            current = lax.dynamic_index_in_dim(out, safe, 0, False)
            placed.append(lax.dynamic_update_index_in_dim(out, jnp.where(valid, part, current), safe, 0))
        return placed

    outs = place(outs, mine, head_index, True)
    send_right = send_left = mine
    for step in range(1, head_count):
        send_right = lax.ppermute(send_right, "head", rightward)
        send_left = lax.ppermute(send_left, "head", leftward)
        outs = place(outs, send_right, head_index - step, head_index >= step)
        outs = place(outs, send_left, head_index + step, head_index + step <= last)
    return outs


def shards(
    span_query,
    span_key,
    span_value,
    prefix_key,
    prefix_value,
    page_table,
    decode_query,
    decode_key,
    decode_value,
    sample_prompt,
    out_weight,
    head_count,
):
    prompts, span_dev, heads_dev, head_depth = span_query.shape
    kv_heads = span_key.shape[2]
    group_size = heads_dev // kv_heads
    steps_count = decode_query.shape[0]
    samples_dev = decode_query.shape[1]
    head_batch = prompts * kv_heads
    ctx_index = lax.axis_index("ctx")
    slot_pick = (
        page_table[:, :, None] == jnp.arange(prefix_key.shape[0], dtype=jnp.int32)
    ).astype(prefix_key.dtype)
    local_keys, local_values = (
        jnp.einsum("pjs,sqkd->pkjqd", slot_pick, pages, preferred_element_type=jnp.float32)
        .astype(pages.dtype)
        .reshape(prompts, kv_heads, -1, head_depth)
        for pages in (prefix_key, prefix_value)
    )
    span_rows = (
        span_query.reshape(prompts, span_dev, kv_heads, group_size, head_depth)
        .transpose(0, 2, 1, 3, 4)
        .reshape(head_batch, span_dev * group_size, head_depth)
    )
    ctx_count = sample_prompt.shape[0] // samples_dev
    span_pair = ctx_gather(jnp.stack([span_key, span_value]), ctx_count, axis=2)
    span_keys_all, span_values_all = span_pair[0], span_pair[1]
    span_total = span_keys_all.shape[1]
    span_key_rows = span_keys_all.transpose(0, 2, 1, 3).reshape(head_batch, span_total, head_depth)
    span_value_rows = span_values_all.transpose(0, 2, 1, 3).reshape(
        head_batch, span_total, head_depth
    )
    query_pos = (
        ctx_index * span_dev + jnp.arange(span_dev * group_size, dtype=jnp.int32) // group_size
    )
    causal = (jnp.arange(span_total, dtype=jnp.int32)[None, :] <= query_pos[:, None])[None]
    decode_five = decode_query.reshape(
        steps_count, samples_dev, kv_heads, group_size, head_depth
    ).transpose(2, 0, 1, 3, 4)
    prefill_state = empty_state(head_batch, span_dev * group_size, head_depth)
    own_pages = jnp.stack([local_keys, local_values])
    core_pairs = [(dev, dev ^ 1) for dev in range(ctx_count)]
    along_x = [
        lax.ppermute(own_pages, "ctx", [(dev, (dev - 2 * shift) % ctx_count) for dev in range(ctx_count)])
        for shift in range(1, ctx_count // 2)
    ]
    arrived = [own_pages, lax.ppermute(own_pages, "ctx", core_pairs)] + along_x
    arrived += [lax.ppermute(pages, "ctx", core_pairs) for pages in along_x]
    prompt_keys_all, prompt_values_all = (
        jnp.concatenate([pages[member] for pages in arrived], axis=2) for member in range(2)
    )
    prefix_len = prompt_keys_all.shape[2]
    key_rows = prompt_keys_all.reshape(head_batch, prefix_len, head_depth)
    value_rows = prompt_values_all.reshape(head_batch, prefix_len, head_depth)
    prefill_state = sweep(prefill_state, span_rows, key_rows, value_rows, 2048)
    decode_flat = decode_five.reshape(kv_heads, -1, head_depth)
    decode_batch = jnp.broadcast_to(decode_flat[None], (prompts,) + decode_flat.shape).reshape(
        head_batch, -1, head_depth
    )
    decode_state = empty_state(head_batch, decode_flat.shape[1], head_depth)
    decode_state = sweep(decode_state, decode_batch, key_rows, value_rows, 2048)
    decode_state = sweep(decode_state, decode_batch, span_key_rows, span_value_rows, span_total)
    own_prompts = lax.dynamic_slice_in_dim(sample_prompt, ctx_index * samples_dev, samples_dev)
    chosen = (
        own_prompts[None, None, None, :, None]
        == jnp.arange(prompts, dtype=jnp.int32)[:, None, None, None, None]
    )

    def select_prompt(member):
        shaped = member.reshape(
            (prompts, kv_heads, steps_count, samples_dev, group_size) + member.shape[2:]
        )
        select_mask = chosen.reshape(chosen.shape + (1,) * (shaped.ndim - 5))
        return jnp.sum(jnp.where(select_mask, shaped, 0.0), axis=0)

    decode_state = tuple((select_prompt(member) for member in decode_state))
    prefill_state = absorb(prefill_state, span_rows, span_key_rows, span_value_rows, causal)
    span_mixed = (prefill_state[2] / prefill_state[1][..., None]).astype(jnp.bfloat16)
    span_attn = (
        span_mixed.reshape(prompts, kv_heads, span_dev, group_size, head_depth)
        .transpose(0, 2, 1, 3, 4)
        .reshape(prompts, span_dev, heads_dev * head_depth)
    )
    span_rows_all = ctx_gather(span_attn, ctx_count, axis=1)
    span_partial = jnp.dot(
        span_rows_all.reshape(-1, span_rows_all.shape[-1]), out_weight, preferred_element_type=jnp.float32
    )
    decode_mixed = own_steps(decode_state, decode_five, decode_key, decode_value)
    decode_attn = decode_mixed.transpose(1, 2, 0, 3, 4).reshape(
        steps_count, samples_dev, heads_dev * head_depth
    )
    decode_rows_all = ctx_gather(decode_attn, ctx_count, axis=1)
    decode_partial = jnp.dot(
        decode_rows_all.reshape(-1, decode_rows_all.shape[-1]), out_weight, preferred_element_type=jnp.float32
    )
    span_sum, decode_sum = head_sum_line((span_partial, decode_partial), head_count)
    span_out = span_sum.reshape(span_rows_all.shape[:-1] + (-1,))
    decode_out = decode_sum.reshape(decode_rows_all.shape[:-1] + (-1,))
    return (span_out, decode_out)


def solution(mesh):
    return jax.shard_map(
        functools.partial(shards, head_count=mesh.shape["head"]),
        mesh=mesh,
        in_specs=(
            P("groups", "ctx", "head", None),
            P("groups", "ctx", "head", None),
            P("groups", "ctx", "head", None),
            P(("groups", "ctx"), None, "head", None),
            P(("groups", "ctx"), None, "head", None),
            P("groups", "ctx"),
            P("groups", "ctx", "head", None),
            P("groups", "ctx", "head", None),
            P("groups", "ctx", "head", None),
            P("groups"),
            P("head", "ctx"),
        ),
        out_specs=(P("groups", None, "ctx"), P("groups", None, "ctx")),
        check_vma=False,
    )
```

```python
import functools
import math

import jax
import jax.numpy as jnp
from jax import lax
from jax.sharding import PartitionSpec as P

negative_floor = -1e30


def absorb(softmax_state, queries, key_rows, value_rows, allowed):
    running_max, running_sum, weighted = softmax_state
    scores = jnp.einsum("brd,bnd->brn", queries, key_rows, preferred_element_type=jnp.float32) * (
        1.0 / math.sqrt(queries.shape[-1])
    )
    if allowed is not None:
        scores = jnp.where(allowed, scores, negative_floor)
    new_max = jnp.maximum(running_max, jnp.max(scores, axis=-1))
    factor = jnp.exp(running_max - new_max)
    weights = jnp.exp(scores - new_max[..., None])
    running_sum = running_sum * factor + jnp.sum(weights, axis=-1)
    weighted = weighted * factor[..., None] + jnp.einsum(
        "brn,bnd->brd", weights.astype(jnp.bfloat16), value_rows, preferred_element_type=jnp.float32
    )
    return (new_max, running_sum, weighted)


def sweep(softmax_state, queries, key_rows, value_rows, block_width):
    total_keys = key_rows.shape[1]
    block_width = math.gcd(total_keys, block_width)

    def one_block(state_in, block_start):
        key_block = lax.dynamic_slice_in_dim(key_rows, block_start, block_width, 1)
        value_block = lax.dynamic_slice_in_dim(value_rows, block_start, block_width, 1)
        return (absorb(state_in, queries, key_block, value_block, None), None)

    starts = jnp.arange(total_keys // block_width, dtype=jnp.int32) * block_width
    softmax_state, unused = lax.scan(one_block, softmax_state, starts)
    return softmax_state


def empty_state(head_batch, row_count, head_depth):
    return (
        jnp.full((head_batch, row_count), negative_floor, jnp.float32),
        jnp.zeros((head_batch, row_count), jnp.float32),
        jnp.zeros((head_batch, row_count, head_depth), jnp.float32),
    )


def own_steps(softmax_state, queries_five, own_key, own_value):
    running_max, running_sum, weighted = softmax_state
    key_rows = own_key.transpose(2, 1, 0, 3)
    value_rows = own_value.transpose(2, 1, 0, 3)
    scores = jnp.einsum(
        "ktsgd,ksud->ktsgu", queries_five, key_rows, preferred_element_type=jnp.float32
    ) * (1.0 / math.sqrt(queries_five.shape[-1]))
    step_total = queries_five.shape[1]
    step_ids = jnp.arange(step_total, dtype=jnp.int32)
    allowed = (step_ids[None, :] <= step_ids[:, None])[None, :, None, None, :]
    scores = jnp.where(allowed, scores, negative_floor)
    new_max = jnp.maximum(running_max, jnp.max(scores, axis=-1))
    factor = jnp.exp(running_max - new_max)
    weights = jnp.exp(scores - new_max[..., None])
    running_sum = running_sum * factor + jnp.sum(weights, axis=-1)
    weighted = weighted * factor[..., None] + jnp.einsum(
        "ktsgu,ksud->ktsgd",
        weights.astype(jnp.bfloat16),
        value_rows,
        preferred_element_type=jnp.float32,
    )
    return (weighted / running_sum[..., None]).astype(jnp.bfloat16)


def ctx_shards(block, ctx_count):
    chips = ctx_count // 2
    received = [block]
    for shift in range(1, chips):
        pairs = [(dev, (dev - 2 * shift) % ctx_count) for dev in range(ctx_count)]
        received.append(lax.ppermute(block, "ctx", pairs))
    along_x = jnp.stack(received)
    other_core = lax.ppermute(along_x, "ctx", [(dev, dev ^ 1) for dev in range(ctx_count)])
    return along_x, other_core


def ctx_gather(block, ctx_count, axis=0):
    ctx_index = lax.axis_index("ctx")
    chip, core = ctx_index // 2, ctx_index % 2
    along_x, other_core = ctx_shards(block, ctx_count)
    along_x = jnp.roll(along_x, chip, axis=0)
    other_core = jnp.roll(other_core, chip, axis=0)
    core_zero = jnp.where(core == 0, along_x, other_core)
    core_one = jnp.where(core == 0, other_core, along_x)
    joined = jnp.moveaxis(jnp.stack([core_zero, core_one], axis=1), (0, 1), (axis, axis + 1))
    return joined.reshape(block.shape[:axis] + (-1,) + block.shape[axis + 1 :])


def head_sum_line(partials, head_count):
    last = head_count - 1
    head_index = lax.axis_index("head")
    pieces = [part.reshape((head_count, -1) + part.shape[1:]) for part in partials]

    def take_block(index):
        return jnp.concatenate(
            [lax.dynamic_index_in_dim(piece, index, 0, False) for piece in pieces], axis=0
        )

    rightward = [(dev, dev + 1) for dev in range(last)]
    leftward = [(dev + 1, dev) for dev in range(last)]
    total = take_block(head_index)
    for offset in [step for step in range(1, head_count)] + [-step for step in range(1, head_count)]:
        pairs = [(dev, dev + offset) for dev in range(head_count) if 0 <= dev + offset <= last]
        outgoing = take_block(jnp.clip(head_index + offset, 0, last)).astype(jnp.bfloat16)
        total = total + lax.ppermute(outgoing, "head", pairs).astype(jnp.float32)
    mine = total.astype(jnp.bfloat16)
    lefts, rights = [], []
    send_right = send_left = mine
    for step in range(1, head_count):
        send_right = lax.ppermute(send_right, "head", rightward)
        send_left = lax.ppermute(send_left, "head", leftward)
        lefts.append(send_right)
        rights.append(send_left)
    candidates = jnp.stack([mine] + lefts + rights)
    wanted = jnp.arange(head_count, dtype=jnp.int32)
    pick = jnp.where(
        wanted == head_index,
        0,
        jnp.where(wanted < head_index, head_index - wanted, last + wanted - head_index),
    )
    return jnp.take(candidates, pick, axis=0)


def shards(
    span_query,
    span_key,
    span_value,
    prefix_key,
    prefix_value,
    page_table,
    decode_query,
    decode_key,
    decode_value,
    sample_prompt,
    out_weight,
    head_count,
):
    prompts, span_dev, heads_dev, head_depth = span_query.shape
    kv_heads = span_key.shape[2]
    group_size = heads_dev // kv_heads
    steps_count = decode_query.shape[0]
    samples_dev = decode_query.shape[1]
    head_batch = prompts * kv_heads
    ctx_index = lax.axis_index("ctx")
    slot_pick = (
        page_table[:, :, None] == jnp.arange(prefix_key.shape[0], dtype=jnp.int32)
    ).astype(prefix_key.dtype)
    local_keys, local_values = (
        jnp.einsum("pjs,sqkd->pkjqd", slot_pick, pages, preferred_element_type=jnp.float32)
        .astype(pages.dtype)
        .reshape(prompts, kv_heads, -1, head_depth)
        for pages in (prefix_key, prefix_value)
    )
    span_rows = (
        span_query.reshape(prompts, span_dev, kv_heads, group_size, head_depth)
        .transpose(0, 2, 1, 3, 4)
        .reshape(head_batch, span_dev * group_size, head_depth)
    )
    ctx_count = sample_prompt.shape[0] // samples_dev
    span_pair = ctx_gather(jnp.stack([span_key, span_value]), ctx_count, axis=2)
    span_keys_all, span_values_all = span_pair[0], span_pair[1]
    span_total = span_keys_all.shape[1]
    span_key_rows = span_keys_all.transpose(0, 2, 1, 3).reshape(head_batch, span_total, head_depth)
    span_value_rows = span_values_all.transpose(0, 2, 1, 3).reshape(
        head_batch, span_total, head_depth
    )
    query_pos = (
        ctx_index * span_dev + jnp.arange(span_dev * group_size, dtype=jnp.int32) // group_size
    )
    causal = (jnp.arange(span_total, dtype=jnp.int32)[None, :] <= query_pos[:, None])[None]
    decode_five = decode_query.reshape(
        steps_count, samples_dev, kv_heads, group_size, head_depth
    ).transpose(2, 0, 1, 3, 4)
    prefill_state = empty_state(head_batch, span_dev * group_size, head_depth)
    own_pages = jnp.stack([local_keys, local_values])
    core_pairs = [(dev, dev ^ 1) for dev in range(ctx_count)]
    along_x = [
        lax.ppermute(own_pages, "ctx", [(dev, (dev - 2 * shift) % ctx_count) for dev in range(ctx_count)])
        for shift in range(1, ctx_count // 2)
    ]
    arrived = [own_pages, lax.ppermute(own_pages, "ctx", core_pairs)] + along_x
    arrived += [lax.ppermute(pages, "ctx", core_pairs) for pages in along_x]
    prompt_keys_all, prompt_values_all = (
        jnp.concatenate([pages[member] for pages in arrived], axis=2) for member in range(2)
    )
    prefix_len = prompt_keys_all.shape[2]
    key_rows = prompt_keys_all.reshape(head_batch, prefix_len, head_depth)
    value_rows = prompt_values_all.reshape(head_batch, prefix_len, head_depth)
    prefill_state = sweep(prefill_state, span_rows, key_rows, value_rows, 2048)
    decode_flat = decode_five.reshape(kv_heads, -1, head_depth)
    decode_batch = jnp.broadcast_to(decode_flat[None], (prompts,) + decode_flat.shape).reshape(
        head_batch, -1, head_depth
    )
    decode_state = empty_state(head_batch, decode_flat.shape[1], head_depth)
    decode_state = sweep(decode_state, decode_batch, key_rows, value_rows, 2048)
    decode_state = sweep(decode_state, decode_batch, span_key_rows, span_value_rows, span_total)
    own_prompts = lax.dynamic_slice_in_dim(sample_prompt, ctx_index * samples_dev, samples_dev)
    chosen = (
        own_prompts[None, None, None, :, None]
        == jnp.arange(prompts, dtype=jnp.int32)[:, None, None, None, None]
    )

    def select_prompt(member):
        shaped = member.reshape(
            (prompts, kv_heads, steps_count, samples_dev, group_size) + member.shape[2:]
        )
        select_mask = chosen.reshape(chosen.shape + (1,) * (shaped.ndim - 5))
        return jnp.sum(jnp.where(select_mask, shaped, 0.0), axis=0)

    decode_state = tuple((select_prompt(member) for member in decode_state))
    prefill_state = absorb(prefill_state, span_rows, span_key_rows, span_value_rows, causal)
    span_mixed = (prefill_state[2] / prefill_state[1][..., None]).astype(jnp.bfloat16)
    span_attn = (
        span_mixed.reshape(prompts, kv_heads, span_dev, group_size, head_depth)
        .transpose(0, 2, 1, 3, 4)
        .reshape(prompts, span_dev, heads_dev * head_depth)
    )
    span_rows_all = ctx_gather(span_attn, ctx_count, axis=1)
    span_partial = jnp.dot(
        span_rows_all.reshape(-1, span_rows_all.shape[-1]), out_weight, preferred_element_type=jnp.float32
    )
    decode_mixed = own_steps(decode_state, decode_five, decode_key, decode_value)
    decode_attn = decode_mixed.transpose(1, 2, 0, 3, 4).reshape(
        steps_count, samples_dev, heads_dev * head_depth
    )
    decode_rows_all = ctx_gather(decode_attn, ctx_count, axis=1)
    decode_partial = jnp.dot(
        decode_rows_all.reshape(-1, decode_rows_all.shape[-1]), out_weight, preferred_element_type=jnp.float32
    )
    summed = head_sum_line((span_partial, decode_partial), head_count)
    span_block = span_partial.shape[0] // head_count
    span_out = summed[:, :span_block].reshape(span_rows_all.shape[:-1] + (-1,))
    decode_out = summed[:, span_block:].reshape(decode_rows_all.shape[:-1] + (-1,))
    return (span_out, decode_out)


def solution(mesh):
    return jax.shard_map(
        functools.partial(shards, head_count=mesh.shape["head"]),
        mesh=mesh,
        in_specs=(
            P("groups", "ctx", "head", None),
            P("groups", "ctx", "head", None),
            P("groups", "ctx", "head", None),
            P(("groups", "ctx"), None, "head", None),
            P(("groups", "ctx"), None, "head", None),
            P("groups", "ctx"),
            P("groups", "ctx", "head", None),
            P("groups", "ctx", "head", None),
            P("groups", "ctx", "head", None),
            P("groups"),
            P("head", "ctx"),
        ),
        out_specs=(P("groups", None, "ctx"), P("groups", None, "ctx")),
        check_vma=False,
    )
```

```python
import functools
import math

import jax
import jax.numpy as jnp
from jax import lax
from jax.sharding import PartitionSpec as P

negative_floor = -1e30


def absorb(softmax_state, queries, key_rows, value_rows, allowed):
    running_max, running_sum, weighted = softmax_state
    scores = jnp.einsum("brd,bnd->brn", queries, key_rows, preferred_element_type=jnp.float32) * (
        1.0 / math.sqrt(queries.shape[-1])
    )
    if allowed is not None:
        scores = jnp.where(allowed, scores, negative_floor)
    new_max = jnp.maximum(running_max, jnp.max(scores, axis=-1))
    factor = jnp.exp(running_max - new_max)
    weights = jnp.exp(scores - new_max[..., None])
    running_sum = running_sum * factor + jnp.sum(weights, axis=-1)
    weighted = weighted * factor[..., None] + jnp.einsum(
        "brn,bnd->brd", weights.astype(jnp.bfloat16), value_rows, preferred_element_type=jnp.float32
    )
    return (new_max, running_sum, weighted)


def sweep(softmax_state, queries, key_rows, value_rows, block_width):
    total_keys = key_rows.shape[1]
    block_width = math.gcd(total_keys, block_width)

    def one_block(state_in, block_start):
        key_block = lax.dynamic_slice_in_dim(key_rows, block_start, block_width, 1)
        value_block = lax.dynamic_slice_in_dim(value_rows, block_start, block_width, 1)
        return (absorb(state_in, queries, key_block, value_block, None), None)

    starts = jnp.arange(total_keys // block_width, dtype=jnp.int32) * block_width
    softmax_state, unused = lax.scan(one_block, softmax_state, starts)
    return softmax_state


def empty_state(head_batch, row_count, head_depth):
    return (
        jnp.full((head_batch, row_count), negative_floor, jnp.float32),
        jnp.zeros((head_batch, row_count), jnp.float32),
        jnp.zeros((head_batch, row_count, head_depth), jnp.float32),
    )


def own_steps(softmax_state, queries_five, own_key, own_value):
    running_max, running_sum, weighted = softmax_state
    key_rows = own_key.transpose(2, 1, 0, 3)
    value_rows = own_value.transpose(2, 1, 0, 3)
    scores = jnp.einsum(
        "ktsgd,ksud->ktsgu", queries_five, key_rows, preferred_element_type=jnp.float32
    ) * (1.0 / math.sqrt(queries_five.shape[-1]))
    step_total = queries_five.shape[1]
    step_ids = jnp.arange(step_total, dtype=jnp.int32)
    allowed = (step_ids[None, :] <= step_ids[:, None])[None, :, None, None, :]
    scores = jnp.where(allowed, scores, negative_floor)
    new_max = jnp.maximum(running_max, jnp.max(scores, axis=-1))
    factor = jnp.exp(running_max - new_max)
    weights = jnp.exp(scores - new_max[..., None])
    running_sum = running_sum * factor + jnp.sum(weights, axis=-1)
    weighted = weighted * factor[..., None] + jnp.einsum(
        "ktsgu,ksud->ktsgd",
        weights.astype(jnp.bfloat16),
        value_rows,
        preferred_element_type=jnp.float32,
    )
    return (weighted / running_sum[..., None]).astype(jnp.bfloat16)


def ctx_shards(block, ctx_count):
    chips = ctx_count // 2
    received = [block]
    for shift in range(1, chips):
        pairs = [(dev, (dev - 2 * shift) % ctx_count) for dev in range(ctx_count)]
        received.append(lax.ppermute(block, "ctx", pairs))
    along_x = jnp.stack(received)
    other_core = lax.ppermute(along_x, "ctx", [(dev, dev ^ 1) for dev in range(ctx_count)])
    return along_x, other_core


def ctx_gather(block, ctx_count, axis=0):
    ctx_index = lax.axis_index("ctx")
    chip, core = ctx_index // 2, ctx_index % 2
    along_x, other_core = ctx_shards(block, ctx_count)
    along_x = jnp.roll(along_x, chip, axis=0)
    other_core = jnp.roll(other_core, chip, axis=0)
    core_zero = jnp.where(core == 0, along_x, other_core)
    core_one = jnp.where(core == 0, other_core, along_x)
    joined = jnp.moveaxis(jnp.stack([core_zero, core_one], axis=1), (0, 1), (axis, axis + 1))
    return joined.reshape(block.shape[:axis] + (-1,) + block.shape[axis + 1 :])


def head_sum_line(partials, head_count):
    last = head_count - 1
    head_index = lax.axis_index("head")
    pieces = [part.reshape((head_count, -1) + part.shape[1:]) for part in partials]

    def take_block(index):
        return jnp.concatenate(
            [lax.dynamic_index_in_dim(piece, index, 0, False) for piece in pieces], axis=0
        )

    rightward = [(dev, dev + 1) for dev in range(last)]
    leftward = [(dev + 1, dev) for dev in range(last)]
    from_left = from_right = None
    for step in range(1, head_count):
        right_block = jnp.clip(head_index + head_count - step, 0, last)
        left_block = jnp.clip(head_index - head_count + step, 0, last)
        going_right = take_block(right_block)
        going_left = take_block(left_block)
        if from_left is not None:
            going_right = going_right + from_left.astype(jnp.float32)
            going_left = going_left + from_right.astype(jnp.float32)
        from_left = lax.ppermute(going_right.astype(jnp.bfloat16), "head", rightward)
        from_right = lax.ppermute(going_left.astype(jnp.bfloat16), "head", leftward)
    own = take_block(head_index)
    mine = (own + from_left.astype(jnp.float32) + from_right.astype(jnp.float32)).astype(jnp.bfloat16)
    lefts, rights = [], []
    send_right = send_left = mine
    for step in range(1, head_count):
        send_right = lax.ppermute(send_right, "head", rightward)
        send_left = lax.ppermute(send_left, "head", leftward)
        lefts.append(send_right)
        rights.append(send_left)
    candidates = jnp.stack([mine] + lefts + rights)
    wanted = jnp.arange(head_count, dtype=jnp.int32)
    pick = jnp.where(
        wanted == head_index,
        0,
        jnp.where(wanted < head_index, head_index - wanted, last + wanted - head_index),
    )
    return jnp.take(candidates, pick, axis=0)


def shards(
    span_query,
    span_key,
    span_value,
    prefix_key,
    prefix_value,
    page_table,
    decode_query,
    decode_key,
    decode_value,
    sample_prompt,
    out_weight,
    head_count,
):
    prompts, span_dev, heads_dev, head_depth = span_query.shape
    kv_heads = span_key.shape[2]
    group_size = heads_dev // kv_heads
    steps_count = decode_query.shape[0]
    samples_dev = decode_query.shape[1]
    head_batch = prompts * kv_heads
    ctx_index = lax.axis_index("ctx")
    slot_pick = (
        page_table[:, :, None] == jnp.arange(prefix_key.shape[0], dtype=jnp.int32)
    ).astype(prefix_key.dtype)
    local_keys, local_values = (
        jnp.einsum("pjs,sqkd->pkjqd", slot_pick, pages, preferred_element_type=jnp.float32)
        .astype(pages.dtype)
        .reshape(prompts, kv_heads, -1, head_depth)
        for pages in (prefix_key, prefix_value)
    )
    span_rows = (
        span_query.reshape(prompts, span_dev, kv_heads, group_size, head_depth)
        .transpose(0, 2, 1, 3, 4)
        .reshape(head_batch, span_dev * group_size, head_depth)
    )
    ctx_count = sample_prompt.shape[0] // samples_dev
    span_pair = ctx_gather(jnp.stack([span_key, span_value]), ctx_count, axis=2)
    span_keys_all, span_values_all = span_pair[0], span_pair[1]
    span_total = span_keys_all.shape[1]
    span_key_rows = span_keys_all.transpose(0, 2, 1, 3).reshape(head_batch, span_total, head_depth)
    span_value_rows = span_values_all.transpose(0, 2, 1, 3).reshape(
        head_batch, span_total, head_depth
    )
    query_pos = (
        ctx_index * span_dev + jnp.arange(span_dev * group_size, dtype=jnp.int32) // group_size
    )
    causal = (jnp.arange(span_total, dtype=jnp.int32)[None, :] <= query_pos[:, None])[None]
    decode_five = decode_query.reshape(
        steps_count, samples_dev, kv_heads, group_size, head_depth
    ).transpose(2, 0, 1, 3, 4)
    prefill_state = empty_state(head_batch, span_dev * group_size, head_depth)
    own_pages = (local_keys, local_values)
    core_pairs = [(dev, dev ^ 1) for dev in range(ctx_count)]
    along_x = [
        lax.ppermute(own_pages, "ctx", [(dev, (dev - 2 * shift) % ctx_count) for dev in range(ctx_count)])
        for shift in range(1, ctx_count // 2)
    ]
    arrived = [own_pages, lax.ppermute(own_pages, "ctx", core_pairs)] + along_x
    arrived += [lax.ppermute(pages, "ctx", core_pairs) for pages in along_x]
    prompt_keys_all, prompt_values_all = (
        jnp.concatenate([pages[member] for pages in arrived], axis=2) for member in range(2)
    )
    prefix_len = prompt_keys_all.shape[2]
    key_rows = prompt_keys_all.reshape(head_batch, prefix_len, head_depth)
    value_rows = prompt_values_all.reshape(head_batch, prefix_len, head_depth)
    prefill_state = sweep(prefill_state, span_rows, key_rows, value_rows, 2048)
    decode_flat = decode_five.reshape(kv_heads, -1, head_depth)
    decode_batch = jnp.broadcast_to(decode_flat[None], (prompts,) + decode_flat.shape).reshape(
        head_batch, -1, head_depth
    )
    decode_state = empty_state(head_batch, decode_flat.shape[1], head_depth)
    decode_state = sweep(decode_state, decode_batch, key_rows, value_rows, 2048)
    decode_state = sweep(decode_state, decode_batch, span_key_rows, span_value_rows, span_total)
    own_prompts = lax.dynamic_slice_in_dim(sample_prompt, ctx_index * samples_dev, samples_dev)
    chosen = (
        own_prompts[None, None, None, :, None]
        == jnp.arange(prompts, dtype=jnp.int32)[:, None, None, None, None]
    )

    def select_prompt(member):
        shaped = member.reshape(
            (prompts, kv_heads, steps_count, samples_dev, group_size) + member.shape[2:]
        )
        select_mask = chosen.reshape(chosen.shape + (1,) * (shaped.ndim - 5))
        return jnp.sum(jnp.where(select_mask, shaped, 0.0), axis=0)

    decode_state = tuple((select_prompt(member) for member in decode_state))
    prefill_state = absorb(prefill_state, span_rows, span_key_rows, span_value_rows, causal)
    span_mixed = (prefill_state[2] / prefill_state[1][..., None]).astype(jnp.bfloat16)
    span_attn = (
        span_mixed.reshape(prompts, kv_heads, span_dev, group_size, head_depth)
        .transpose(0, 2, 1, 3, 4)
        .reshape(prompts, span_dev, heads_dev * head_depth)
    )
    span_rows_all = ctx_gather(span_attn, ctx_count, axis=1)
    span_partial = jnp.dot(
        span_rows_all.reshape(-1, span_rows_all.shape[-1]), out_weight, preferred_element_type=jnp.float32
    )
    decode_mixed = own_steps(decode_state, decode_five, decode_key, decode_value)
    decode_attn = decode_mixed.transpose(1, 2, 0, 3, 4).reshape(
        steps_count, samples_dev, heads_dev * head_depth
    )
    decode_rows_all = ctx_gather(decode_attn, ctx_count, axis=1)
    decode_partial = jnp.dot(
        decode_rows_all.reshape(-1, decode_rows_all.shape[-1]), out_weight, preferred_element_type=jnp.float32
    )
    summed = head_sum_line((span_partial, decode_partial), head_count)
    span_block = span_partial.shape[0] // head_count
    span_out = summed[:, :span_block].reshape(span_rows_all.shape[:-1] + (-1,))
    decode_out = summed[:, span_block:].reshape(decode_rows_all.shape[:-1] + (-1,))
    return (span_out, decode_out)


def solution(mesh):
    return jax.shard_map(
        functools.partial(shards, head_count=mesh.shape["head"]),
        mesh=mesh,
        in_specs=(
            P("groups", "ctx", "head", None),
            P("groups", "ctx", "head", None),
            P("groups", "ctx", "head", None),
            P(("groups", "ctx"), None, "head", None),
            P(("groups", "ctx"), None, "head", None),
            P("groups", "ctx"),
            P("groups", "ctx", "head", None),
            P("groups", "ctx", "head", None),
            P("groups", "ctx", "head", None),
            P("groups"),
            P("head", "ctx"),
        ),
        out_specs=(P("groups", None, "ctx"), P("groups", None, "ctx")),
        check_vma=False,
    )
```

```python
import functools
import math

import jax
import jax.numpy as jnp
from jax import lax
from jax.sharding import PartitionSpec as P

negative_floor = -1e30


def absorb(softmax_state, queries, key_rows, value_rows, allowed):
    running_max, running_sum, weighted = softmax_state
    scores = jnp.einsum("brd,bnd->brn", queries, key_rows, preferred_element_type=jnp.float32) * (
        1.0 / math.sqrt(queries.shape[-1])
    )
    if allowed is not None:
        scores = jnp.where(allowed, scores, negative_floor)
    new_max = jnp.maximum(running_max, jnp.max(scores, axis=-1))
    factor = jnp.exp(running_max - new_max)
    weights = jnp.exp(scores - new_max[..., None])
    running_sum = running_sum * factor + jnp.sum(weights, axis=-1)
    weighted = weighted * factor[..., None] + jnp.einsum(
        "brn,bnd->brd", weights.astype(jnp.bfloat16), value_rows, preferred_element_type=jnp.float32
    )
    return (new_max, running_sum, weighted)


def sweep(softmax_state, queries, key_rows, value_rows, block_width):
    total_keys = key_rows.shape[1]
    block_width = math.gcd(total_keys, block_width)

    def one_block(state_in, block_start):
        key_block = lax.dynamic_slice_in_dim(key_rows, block_start, block_width, 1)
        value_block = lax.dynamic_slice_in_dim(value_rows, block_start, block_width, 1)
        return (absorb(state_in, queries, key_block, value_block, None), None)

    starts = jnp.arange(total_keys // block_width, dtype=jnp.int32) * block_width
    softmax_state, unused = lax.scan(one_block, softmax_state, starts)
    return softmax_state


def empty_state(head_batch, row_count, head_depth):
    return (
        jnp.full((head_batch, row_count), negative_floor, jnp.float32),
        jnp.zeros((head_batch, row_count), jnp.float32),
        jnp.zeros((head_batch, row_count, head_depth), jnp.float32),
    )


def own_steps(softmax_state, queries_five, own_key, own_value):
    running_max, running_sum, weighted = softmax_state
    key_rows = own_key.transpose(2, 1, 0, 3)
    value_rows = own_value.transpose(2, 1, 0, 3)
    scores = jnp.einsum(
        "ktsgd,ksud->ktsgu", queries_five, key_rows, preferred_element_type=jnp.float32
    ) * (1.0 / math.sqrt(queries_five.shape[-1]))
    step_total = queries_five.shape[1]
    step_ids = jnp.arange(step_total, dtype=jnp.int32)
    allowed = (step_ids[None, :] <= step_ids[:, None])[None, :, None, None, :]
    scores = jnp.where(allowed, scores, negative_floor)
    new_max = jnp.maximum(running_max, jnp.max(scores, axis=-1))
    factor = jnp.exp(running_max - new_max)
    weights = jnp.exp(scores - new_max[..., None])
    running_sum = running_sum * factor + jnp.sum(weights, axis=-1)
    weighted = weighted * factor[..., None] + jnp.einsum(
        "ktsgu,ksud->ktsgd",
        weights.astype(jnp.bfloat16),
        value_rows,
        preferred_element_type=jnp.float32,
    )
    return (weighted / running_sum[..., None]).astype(jnp.bfloat16)


def ctx_shards(block, ctx_count):
    chips = ctx_count // 2
    halves = tuple(jnp.split(block, 2)) if block.shape[0] % 2 == 0 else (block,)
    received = [halves]
    for shift in range(1, chips):
        pairs = [(dev, (dev - 2 * shift) % ctx_count) for dev in range(ctx_count)]
        received.append(lax.ppermute(halves, "ctx", pairs))
    along_x = tuple(jnp.stack([parts[half] for parts in received]) for half in range(len(halves)))
    other_core = lax.ppermute(along_x, "ctx", [(dev, dev ^ 1) for dev in range(ctx_count)])
    return jnp.concatenate(along_x, axis=1), jnp.concatenate(other_core, axis=1)


def ctx_gather(block, ctx_count, axis=0):
    ctx_index = lax.axis_index("ctx")
    chip, core = ctx_index // 2, ctx_index % 2
    along_x, other_core = ctx_shards(block, ctx_count)
    along_x = jnp.roll(along_x, chip, axis=0)
    other_core = jnp.roll(other_core, chip, axis=0)
    core_zero = jnp.where(core == 0, along_x, other_core)
    core_one = jnp.where(core == 0, other_core, along_x)
    joined = jnp.moveaxis(jnp.stack([core_zero, core_one], axis=1), (0, 1), (axis, axis + 1))
    return joined.reshape(block.shape[:axis] + (-1,) + block.shape[axis + 1 :])


def head_sum_line(partials, head_count):
    last = head_count - 1
    head_index = lax.axis_index("head")
    pieces = [part.reshape((head_count, -1) + part.shape[1:]) for part in partials]

    def take_block(index):
        return jnp.concatenate(
            [lax.dynamic_index_in_dim(piece, index, 0, False) for piece in pieces], axis=0
        )

    rightward = [(dev, dev + 1) for dev in range(last)]
    leftward = [(dev + 1, dev) for dev in range(last)]
    from_left = from_right = None
    for step in range(1, head_count):
        right_block = jnp.clip(head_index + head_count - step, 0, last)
        left_block = jnp.clip(head_index - head_count + step, 0, last)
        going_right = take_block(right_block)
        going_left = take_block(left_block)
        if from_left is not None:
            going_right = going_right + from_left.astype(jnp.float32)
            going_left = going_left + from_right.astype(jnp.float32)
        from_left = lax.ppermute(going_right.astype(jnp.bfloat16), "head", rightward)
        from_right = lax.ppermute(going_left.astype(jnp.bfloat16), "head", leftward)
    own = take_block(head_index)
    mine = (own + from_left.astype(jnp.float32) + from_right.astype(jnp.float32)).astype(jnp.bfloat16)
    lefts, rights = [], []
    send_right = send_left = mine
    for step in range(1, head_count):
        send_right = lax.ppermute(send_right, "head", rightward)
        send_left = lax.ppermute(send_left, "head", leftward)
        lefts.append(send_right)
        rights.append(send_left)
    candidates = jnp.stack([mine] + lefts + rights)
    wanted = jnp.arange(head_count, dtype=jnp.int32)
    pick = jnp.where(
        wanted == head_index,
        0,
        jnp.where(wanted < head_index, head_index - wanted, last + wanted - head_index),
    )
    return jnp.take(candidates, pick, axis=0)


def shards(
    span_query,
    span_key,
    span_value,
    prefix_key,
    prefix_value,
    page_table,
    decode_query,
    decode_key,
    decode_value,
    sample_prompt,
    out_weight,
    head_count,
):
    prompts, span_dev, heads_dev, head_depth = span_query.shape
    kv_heads = span_key.shape[2]
    group_size = heads_dev // kv_heads
    steps_count = decode_query.shape[0]
    samples_dev = decode_query.shape[1]
    head_batch = prompts * kv_heads
    ctx_index = lax.axis_index("ctx")
    slot_pick = (
        page_table[:, :, None] == jnp.arange(prefix_key.shape[0], dtype=jnp.int32)
    ).astype(prefix_key.dtype)
    local_keys, local_values = (
        jnp.einsum("pjs,sqkd->pkjqd", slot_pick, pages, preferred_element_type=jnp.float32)
        .astype(pages.dtype)
        .reshape(prompts, kv_heads, -1, head_depth)
        for pages in (prefix_key, prefix_value)
    )
    span_rows = (
        span_query.reshape(prompts, span_dev, kv_heads, group_size, head_depth)
        .transpose(0, 2, 1, 3, 4)
        .reshape(head_batch, span_dev * group_size, head_depth)
    )
    ctx_count = sample_prompt.shape[0] // samples_dev
    span_pair = ctx_gather(jnp.stack([span_key, span_value]), ctx_count, axis=2)
    span_keys_all, span_values_all = span_pair[0], span_pair[1]
    span_total = span_keys_all.shape[1]
    span_key_rows = span_keys_all.transpose(0, 2, 1, 3).reshape(head_batch, span_total, head_depth)
    span_value_rows = span_values_all.transpose(0, 2, 1, 3).reshape(
        head_batch, span_total, head_depth
    )
    query_pos = (
        ctx_index * span_dev + jnp.arange(span_dev * group_size, dtype=jnp.int32) // group_size
    )
    causal = (jnp.arange(span_total, dtype=jnp.int32)[None, :] <= query_pos[:, None])[None]
    decode_five = decode_query.reshape(
        steps_count, samples_dev, kv_heads, group_size, head_depth
    ).transpose(2, 0, 1, 3, 4)
    prefill_state = empty_state(head_batch, span_dev * group_size, head_depth)
    own_pages = (local_keys, local_values)
    core_pairs = [(dev, dev ^ 1) for dev in range(ctx_count)]
    along_x = [
        lax.ppermute(own_pages, "ctx", [(dev, (dev - 2 * shift) % ctx_count) for dev in range(ctx_count)])
        for shift in range(1, ctx_count // 2)
    ]
    arrived = [own_pages, lax.ppermute(own_pages, "ctx", core_pairs)] + along_x
    arrived += [lax.ppermute(pages, "ctx", core_pairs) for pages in along_x]
    prompt_keys_all, prompt_values_all = (
        jnp.concatenate([pages[member] for pages in arrived], axis=2) for member in range(2)
    )
    prefix_len = prompt_keys_all.shape[2]
    key_rows = prompt_keys_all.reshape(head_batch, prefix_len, head_depth)
    value_rows = prompt_values_all.reshape(head_batch, prefix_len, head_depth)
    prefill_state = sweep(prefill_state, span_rows, key_rows, value_rows, 2048)
    decode_flat = decode_five.reshape(kv_heads, -1, head_depth)
    decode_batch = jnp.broadcast_to(decode_flat[None], (prompts,) + decode_flat.shape).reshape(
        head_batch, -1, head_depth
    )
    decode_state = empty_state(head_batch, decode_flat.shape[1], head_depth)
    decode_state = sweep(decode_state, decode_batch, key_rows, value_rows, 2048)
    decode_state = sweep(decode_state, decode_batch, span_key_rows, span_value_rows, span_total)
    own_prompts = lax.dynamic_slice_in_dim(sample_prompt, ctx_index * samples_dev, samples_dev)
    chosen = (
        own_prompts[None, None, None, :, None]
        == jnp.arange(prompts, dtype=jnp.int32)[:, None, None, None, None]
    )

    def select_prompt(member):
        shaped = member.reshape(
            (prompts, kv_heads, steps_count, samples_dev, group_size) + member.shape[2:]
        )
        select_mask = chosen.reshape(chosen.shape + (1,) * (shaped.ndim - 5))
        return jnp.sum(jnp.where(select_mask, shaped, 0.0), axis=0)

    decode_state = tuple((select_prompt(member) for member in decode_state))
    prefill_state = absorb(prefill_state, span_rows, span_key_rows, span_value_rows, causal)
    span_mixed = (prefill_state[2] / prefill_state[1][..., None]).astype(jnp.bfloat16)
    span_attn = (
        span_mixed.reshape(prompts, kv_heads, span_dev, group_size, head_depth)
        .transpose(0, 2, 1, 3, 4)
        .reshape(prompts, span_dev, heads_dev * head_depth)
    )
    span_rows_all = ctx_gather(span_attn, ctx_count, axis=1)
    span_partial = jnp.dot(
        span_rows_all.reshape(-1, span_rows_all.shape[-1]), out_weight, preferred_element_type=jnp.float32
    )
    decode_mixed = own_steps(decode_state, decode_five, decode_key, decode_value)
    decode_attn = decode_mixed.transpose(1, 2, 0, 3, 4).reshape(
        steps_count, samples_dev, heads_dev * head_depth
    )
    decode_rows_all = ctx_gather(decode_attn, ctx_count, axis=1)
    decode_partial = jnp.dot(
        decode_rows_all.reshape(-1, decode_rows_all.shape[-1]), out_weight, preferred_element_type=jnp.float32
    )
    summed = head_sum_line((span_partial, decode_partial), head_count)
    span_block = span_partial.shape[0] // head_count
    span_out = summed[:, :span_block].reshape(span_rows_all.shape[:-1] + (-1,))
    decode_out = summed[:, span_block:].reshape(decode_rows_all.shape[:-1] + (-1,))
    return (span_out, decode_out)


def solution(mesh):
    return jax.shard_map(
        functools.partial(shards, head_count=mesh.shape["head"]),
        mesh=mesh,
        in_specs=(
            P("groups", "ctx", "head", None),
            P("groups", "ctx", "head", None),
            P("groups", "ctx", "head", None),
            P(("groups", "ctx"), None, "head", None),
            P(("groups", "ctx"), None, "head", None),
            P("groups", "ctx"),
            P("groups", "ctx", "head", None),
            P("groups", "ctx", "head", None),
            P("groups", "ctx", "head", None),
            P("groups"),
            P("head", "ctx"),
        ),
        out_specs=(P("groups", None, "ctx"), P("groups", None, "ctx")),
        check_vma=False,
    )
```

```python
import functools
import math

import jax
import jax.numpy as jnp
from jax import lax
from jax.sharding import PartitionSpec as P

negative_floor = -1e30


def absorb(softmax_state, queries, key_rows, value_rows, allowed):
    running_max, running_sum, weighted = softmax_state
    scores = jnp.einsum("brd,bnd->brn", queries, key_rows, preferred_element_type=jnp.float32) * (
        1.0 / math.sqrt(queries.shape[-1])
    )
    if allowed is not None:
        scores = jnp.where(allowed, scores, negative_floor)
    new_max = jnp.maximum(running_max, jnp.max(scores, axis=-1))
    factor = jnp.exp(running_max - new_max)
    weights = jnp.exp(scores - new_max[..., None])
    running_sum = running_sum * factor + jnp.sum(weights, axis=-1)
    weighted = weighted * factor[..., None] + jnp.einsum(
        "brn,bnd->brd", weights.astype(jnp.bfloat16), value_rows, preferred_element_type=jnp.float32
    )
    return (new_max, running_sum, weighted)


def sweep(softmax_state, queries, key_rows, value_rows, block_width):
    total_keys = key_rows.shape[1]
    block_width = math.gcd(total_keys, block_width)

    def one_block(state_in, block_start):
        key_block = lax.dynamic_slice_in_dim(key_rows, block_start, block_width, 1)
        value_block = lax.dynamic_slice_in_dim(value_rows, block_start, block_width, 1)
        return (absorb(state_in, queries, key_block, value_block, None), None)

    starts = jnp.arange(total_keys // block_width, dtype=jnp.int32) * block_width
    softmax_state, unused = lax.scan(one_block, softmax_state, starts)
    return softmax_state


def empty_state(head_batch, row_count, head_depth):
    return (
        jnp.full((head_batch, row_count), negative_floor, jnp.float32),
        jnp.zeros((head_batch, row_count), jnp.float32),
        jnp.zeros((head_batch, row_count, head_depth), jnp.float32),
    )


def own_steps(softmax_state, queries_five, own_key, own_value):
    running_max, running_sum, weighted = softmax_state
    key_rows = own_key.transpose(2, 1, 0, 3)
    value_rows = own_value.transpose(2, 1, 0, 3)
    scores = jnp.einsum(
        "ktsgd,ksud->ktsgu", queries_five, key_rows, preferred_element_type=jnp.float32
    ) * (1.0 / math.sqrt(queries_five.shape[-1]))
    step_total = queries_five.shape[1]
    step_ids = jnp.arange(step_total, dtype=jnp.int32)
    allowed = (step_ids[None, :] <= step_ids[:, None])[None, :, None, None, :]
    scores = jnp.where(allowed, scores, negative_floor)
    new_max = jnp.maximum(running_max, jnp.max(scores, axis=-1))
    factor = jnp.exp(running_max - new_max)
    weights = jnp.exp(scores - new_max[..., None])
    running_sum = running_sum * factor + jnp.sum(weights, axis=-1)
    weighted = weighted * factor[..., None] + jnp.einsum(
        "ktsgu,ksud->ktsgd",
        weights.astype(jnp.bfloat16),
        value_rows,
        preferred_element_type=jnp.float32,
    )
    return (weighted / running_sum[..., None]).astype(jnp.bfloat16)


def ctx_shards(block, ctx_count):
    chips = ctx_count // 2
    received = [block]
    for shift in range(1, chips):
        pairs = [(dev, (dev - 2 * shift) % ctx_count) for dev in range(ctx_count)]
        received.append(lax.ppermute(block, "ctx", pairs))
    along_x = jnp.stack(received)
    other_core = lax.ppermute(along_x, "ctx", [(dev, dev ^ 1) for dev in range(ctx_count)])
    return along_x, other_core


def ctx_gather(block, ctx_count, axis=0):
    ctx_index = lax.axis_index("ctx")
    chip, core = ctx_index // 2, ctx_index % 2
    along_x, other_core = ctx_shards(block, ctx_count)
    along_x = jnp.roll(along_x, chip, axis=0)
    other_core = jnp.roll(other_core, chip, axis=0)
    core_zero = jnp.where(core == 0, along_x, other_core)
    core_one = jnp.where(core == 0, other_core, along_x)
    joined = jnp.moveaxis(jnp.stack([core_zero, core_one], axis=1), (0, 1), (axis, axis + 1))
    return joined.reshape(block.shape[:axis] + (-1,) + block.shape[axis + 1 :])


def head_sum_line(partials, head_count):
    last = head_count - 1
    head_index = lax.axis_index("head")
    pieces = [part.reshape((head_count, -1) + part.shape[1:]) for part in partials]

    def take_block(index):
        return jnp.concatenate(
            [lax.dynamic_index_in_dim(piece, index, 0, False) for piece in pieces], axis=0
        )

    rightward = [(dev, dev + 1) for dev in range(last)]
    leftward = [(dev + 1, dev) for dev in range(last)]
    from_left = from_right = None
    for step in range(1, head_count):
        right_block = jnp.clip(head_index + head_count - step, 0, last)
        left_block = jnp.clip(head_index - head_count + step, 0, last)
        going_right = take_block(right_block)
        going_left = take_block(left_block)
        if from_left is not None:
            going_right = going_right + from_left.astype(jnp.float32)
            going_left = going_left + from_right.astype(jnp.float32)
        from_left = lax.ppermute(going_right.astype(jnp.bfloat16), "head", rightward)
        from_right = lax.ppermute(going_left.astype(jnp.bfloat16), "head", leftward)
    own = take_block(head_index)
    mine = (own + from_left.astype(jnp.float32) + from_right.astype(jnp.float32)).astype(jnp.bfloat16)
    lefts, rights = [], []
    send_right = send_left = mine
    for step in range(1, head_count):
        send_right = lax.ppermute(send_right, "head", rightward)
        send_left = lax.ppermute(send_left, "head", leftward)
        lefts.append(send_right)
        rights.append(send_left)
    candidates = jnp.stack([mine] + lefts + rights)
    wanted = jnp.arange(head_count, dtype=jnp.int32)
    pick = jnp.where(
        wanted == head_index,
        0,
        jnp.where(wanted < head_index, head_index - wanted, last + wanted - head_index),
    )
    return jnp.take(candidates, pick, axis=0)


def shards(
    span_query,
    span_key,
    span_value,
    prefix_key,
    prefix_value,
    page_table,
    decode_query,
    decode_key,
    decode_value,
    sample_prompt,
    out_weight,
    head_count,
):
    prompts, span_dev, heads_dev, head_depth = span_query.shape
    kv_heads = span_key.shape[2]
    group_size = heads_dev // kv_heads
    steps_count = decode_query.shape[0]
    samples_dev = decode_query.shape[1]
    head_batch = prompts * kv_heads
    ctx_index = lax.axis_index("ctx")
    slot_pick = (
        page_table[:, :, None] == jnp.arange(prefix_key.shape[0], dtype=jnp.int32)
    ).astype(prefix_key.dtype)
    local_keys, local_values = (
        jnp.einsum("pjs,sqkd->pkjqd", slot_pick, pages, preferred_element_type=jnp.float32)
        .astype(pages.dtype)
        .reshape(prompts, kv_heads, -1, head_depth)
        for pages in (prefix_key, prefix_value)
    )
    span_rows = (
        span_query.reshape(prompts, span_dev, kv_heads, group_size, head_depth)
        .transpose(0, 2, 1, 3, 4)
        .reshape(head_batch, span_dev * group_size, head_depth)
    )
    ctx_count = sample_prompt.shape[0] // samples_dev
    span_pair = ctx_gather(jnp.stack([span_key, span_value]), ctx_count, axis=2)
    span_keys_all, span_values_all = span_pair[0], span_pair[1]
    span_total = span_keys_all.shape[1]
    span_key_rows = span_keys_all.transpose(0, 2, 1, 3).reshape(head_batch, span_total, head_depth)
    span_value_rows = span_values_all.transpose(0, 2, 1, 3).reshape(
        head_batch, span_total, head_depth
    )
    query_pos = (
        ctx_index * span_dev + jnp.arange(span_dev * group_size, dtype=jnp.int32) // group_size
    )
    causal = (jnp.arange(span_total, dtype=jnp.int32)[None, :] <= query_pos[:, None])[None]
    decode_five = decode_query.reshape(
        steps_count, samples_dev, kv_heads, group_size, head_depth
    ).transpose(2, 0, 1, 3, 4)
    prefill_state = empty_state(head_batch, span_dev * group_size, head_depth)
    own_pages = (local_keys, local_values)
    core_pairs = [(dev, dev ^ 1) for dev in range(ctx_count)]
    x_pairs = [
        [(dev, (dev - 2 * shift) % ctx_count) for dev in range(ctx_count)]
        for shift in range(1, ctx_count // 2)
    ]
    keys_x = [lax.ppermute(local_keys, "ctx", pairs) for pairs in x_pairs]
    values_after_keys, keys_x = lax.optimization_barrier((local_values, keys_x))
    values_x = [lax.ppermute(values_after_keys, "ctx", pairs) for pairs in x_pairs]
    along_x = list(zip(keys_x, values_x))
    arrived = [own_pages, lax.ppermute(own_pages, "ctx", core_pairs)] + along_x
    arrived += [lax.ppermute(pages, "ctx", core_pairs) for pages in along_x]
    prompt_keys_all, prompt_values_all = (
        jnp.concatenate([pages[member] for pages in arrived], axis=2) for member in range(2)
    )
    prefix_len = prompt_keys_all.shape[2]
    key_rows = prompt_keys_all.reshape(head_batch, prefix_len, head_depth)
    value_rows = prompt_values_all.reshape(head_batch, prefix_len, head_depth)
    prefill_state = sweep(prefill_state, span_rows, key_rows, value_rows, 2048)
    decode_flat = decode_five.reshape(kv_heads, -1, head_depth)
    decode_batch = jnp.broadcast_to(decode_flat[None], (prompts,) + decode_flat.shape).reshape(
        head_batch, -1, head_depth
    )
    decode_state = empty_state(head_batch, decode_flat.shape[1], head_depth)
    decode_state = sweep(decode_state, decode_batch, key_rows, value_rows, 2048)
    decode_state = sweep(decode_state, decode_batch, span_key_rows, span_value_rows, span_total)
    own_prompts = lax.dynamic_slice_in_dim(sample_prompt, ctx_index * samples_dev, samples_dev)
    chosen = (
        own_prompts[None, None, None, :, None]
        == jnp.arange(prompts, dtype=jnp.int32)[:, None, None, None, None]
    )

    def select_prompt(member):
        shaped = member.reshape(
            (prompts, kv_heads, steps_count, samples_dev, group_size) + member.shape[2:]
        )
        select_mask = chosen.reshape(chosen.shape + (1,) * (shaped.ndim - 5))
        return jnp.sum(jnp.where(select_mask, shaped, 0.0), axis=0)

    decode_state = tuple((select_prompt(member) for member in decode_state))
    prefill_state = absorb(prefill_state, span_rows, span_key_rows, span_value_rows, causal)
    span_mixed = (prefill_state[2] / prefill_state[1][..., None]).astype(jnp.bfloat16)
    span_attn = (
        span_mixed.reshape(prompts, kv_heads, span_dev, group_size, head_depth)
        .transpose(0, 2, 1, 3, 4)
        .reshape(prompts, span_dev, heads_dev * head_depth)
    )
    span_rows_all = ctx_gather(span_attn, ctx_count, axis=1)
    span_partial = jnp.dot(
        span_rows_all.reshape(-1, span_rows_all.shape[-1]), out_weight, preferred_element_type=jnp.float32
    )
    decode_mixed = own_steps(decode_state, decode_five, decode_key, decode_value)
    decode_attn = decode_mixed.transpose(1, 2, 0, 3, 4).reshape(
        steps_count, samples_dev, heads_dev * head_depth
    )
    decode_rows_all = ctx_gather(decode_attn, ctx_count, axis=1)
    decode_partial = jnp.dot(
        decode_rows_all.reshape(-1, decode_rows_all.shape[-1]), out_weight, preferred_element_type=jnp.float32
    )
    summed = head_sum_line((span_partial, decode_partial), head_count)
    span_block = span_partial.shape[0] // head_count
    span_out = summed[:, :span_block].reshape(span_rows_all.shape[:-1] + (-1,))
    decode_out = summed[:, span_block:].reshape(decode_rows_all.shape[:-1] + (-1,))
    return (span_out, decode_out)


def solution(mesh):
    return jax.shard_map(
        functools.partial(shards, head_count=mesh.shape["head"]),
        mesh=mesh,
        in_specs=(
            P("groups", "ctx", "head", None),
            P("groups", "ctx", "head", None),
            P("groups", "ctx", "head", None),
            P(("groups", "ctx"), None, "head", None),
            P(("groups", "ctx"), None, "head", None),
            P("groups", "ctx"),
            P("groups", "ctx", "head", None),
            P("groups", "ctx", "head", None),
            P("groups", "ctx", "head", None),
            P("groups"),
            P("head", "ctx"),
        ),
        out_specs=(P("groups", None, "ctx"), P("groups", None, "ctx")),
        check_vma=False,
    )
```

```python
import functools
import math

import jax
import jax.numpy as jnp
from jax import lax
from jax.sharding import PartitionSpec as P

negative_floor = -1e30


def absorb(softmax_state, queries, key_rows, value_rows, allowed):
    running_max, running_sum, weighted = softmax_state
    scores = jnp.einsum("brd,bnd->brn", queries, key_rows, preferred_element_type=jnp.float32) * (
        1.0 / math.sqrt(queries.shape[-1])
    )
    if allowed is not None:
        scores = jnp.where(allowed, scores, negative_floor)
    new_max = jnp.maximum(running_max, jnp.max(scores, axis=-1))
    factor = jnp.exp(running_max - new_max)
    weights = jnp.exp(scores - new_max[..., None])
    running_sum = running_sum * factor + jnp.sum(weights, axis=-1)
    weighted = weighted * factor[..., None] + jnp.einsum(
        "brn,bnd->brd", weights.astype(jnp.bfloat16), value_rows, preferred_element_type=jnp.float32
    )
    return (new_max, running_sum, weighted)


def sweep(softmax_state, queries, key_rows, value_rows, block_width):
    total_keys = key_rows.shape[1]
    block_width = math.gcd(total_keys, block_width)

    def one_block(state_in, block_start):
        key_block = lax.dynamic_slice_in_dim(key_rows, block_start, block_width, 1)
        value_block = lax.dynamic_slice_in_dim(value_rows, block_start, block_width, 1)
        return (absorb(state_in, queries, key_block, value_block, None), None)

    starts = jnp.arange(total_keys // block_width, dtype=jnp.int32) * block_width
    softmax_state, unused = lax.scan(one_block, softmax_state, starts)
    return softmax_state


def empty_state(head_batch, row_count, head_depth):
    return (
        jnp.full((head_batch, row_count), negative_floor, jnp.float32),
        jnp.zeros((head_batch, row_count), jnp.float32),
        jnp.zeros((head_batch, row_count, head_depth), jnp.float32),
    )


def own_steps(softmax_state, queries_five, own_key, own_value):
    running_max, running_sum, weighted = softmax_state
    key_rows = own_key.transpose(2, 1, 0, 3)
    value_rows = own_value.transpose(2, 1, 0, 3)
    scores = jnp.einsum(
        "ktsgd,ksud->ktsgu", queries_five, key_rows, preferred_element_type=jnp.float32
    ) * (1.0 / math.sqrt(queries_five.shape[-1]))
    step_total = queries_five.shape[1]
    step_ids = jnp.arange(step_total, dtype=jnp.int32)
    allowed = (step_ids[None, :] <= step_ids[:, None])[None, :, None, None, :]
    scores = jnp.where(allowed, scores, negative_floor)
    new_max = jnp.maximum(running_max, jnp.max(scores, axis=-1))
    factor = jnp.exp(running_max - new_max)
    weights = jnp.exp(scores - new_max[..., None])
    running_sum = running_sum * factor + jnp.sum(weights, axis=-1)
    weighted = weighted * factor[..., None] + jnp.einsum(
        "ktsgu,ksud->ktsgd",
        weights.astype(jnp.bfloat16),
        value_rows,
        preferred_element_type=jnp.float32,
    )
    return (weighted / running_sum[..., None]).astype(jnp.bfloat16)


def ctx_shards(block, ctx_count):
    chips = ctx_count // 2
    received = [block]
    for shift in range(1, chips):
        pairs = [(dev, (dev - 2 * shift) % ctx_count) for dev in range(ctx_count)]
        received.append(lax.ppermute(block, "ctx", pairs))
    along_x = jnp.stack(received)
    other_core = lax.ppermute(along_x, "ctx", [(dev, dev ^ 1) for dev in range(ctx_count)])
    return along_x, other_core


def ctx_gather(block, ctx_count, axis=0):
    ctx_index = lax.axis_index("ctx")
    chip, core = ctx_index // 2, ctx_index % 2
    along_x, other_core = ctx_shards(block, ctx_count)
    along_x = jnp.roll(along_x, chip, axis=0)
    other_core = jnp.roll(other_core, chip, axis=0)
    core_zero = jnp.where(core == 0, along_x, other_core)
    core_one = jnp.where(core == 0, other_core, along_x)
    joined = jnp.moveaxis(jnp.stack([core_zero, core_one], axis=1), (0, 1), (axis, axis + 1))
    return joined.reshape(block.shape[:axis] + (-1,) + block.shape[axis + 1 :])


def head_sum_line(partials, head_count):
    last = head_count - 1
    head_index = lax.axis_index("head")
    pieces = [part.reshape((head_count, -1) + part.shape[1:]) for part in partials]

    def take_block(index):
        return jnp.concatenate(
            [lax.dynamic_index_in_dim(piece, index, 0, False) for piece in pieces], axis=0
        )

    rightward = [(dev, dev + 1) for dev in range(last)]
    leftward = [(dev + 1, dev) for dev in range(last)]
    from_left = from_right = None
    for step in range(1, head_count):
        right_block = jnp.clip(head_index + head_count - step, 0, last)
        left_block = jnp.clip(head_index - head_count + step, 0, last)
        going_right = take_block(right_block)
        going_left = take_block(left_block)
        if from_left is not None:
            going_right = going_right + from_left.astype(jnp.float32)
            going_left = going_left + from_right.astype(jnp.float32)
        from_left = lax.ppermute(going_right.astype(jnp.bfloat16), "head", rightward)
        from_right = lax.ppermute(going_left.astype(jnp.bfloat16), "head", leftward)
    own = take_block(head_index)
    mine = (own + from_left.astype(jnp.float32) + from_right.astype(jnp.float32)).astype(jnp.bfloat16)
    lefts, rights = [], []
    send_right = send_left = mine
    for step in range(1, head_count):
        send_right = lax.ppermute(send_right, "head", rightward)
        send_left = lax.ppermute(send_left, "head", leftward)
        lefts.append(send_right)
        rights.append(send_left)
    candidates = jnp.stack([mine] + lefts + rights)
    wanted = jnp.arange(head_count, dtype=jnp.int32)
    pick = jnp.where(
        wanted == head_index,
        0,
        jnp.where(wanted < head_index, head_index - wanted, last + wanted - head_index),
    )
    return jnp.take(candidates, pick, axis=0)


def shards(
    span_query,
    span_key,
    span_value,
    prefix_key,
    prefix_value,
    page_table,
    decode_query,
    decode_key,
    decode_value,
    sample_prompt,
    out_weight,
    head_count,
):
    prompts, span_dev, heads_dev, head_depth = span_query.shape
    kv_heads = span_key.shape[2]
    group_size = heads_dev // kv_heads
    steps_count = decode_query.shape[0]
    samples_dev = decode_query.shape[1]
    head_batch = prompts * kv_heads
    ctx_index = lax.axis_index("ctx")
    slot_pick = (
        page_table[:, :, None] == jnp.arange(prefix_key.shape[0], dtype=jnp.int32)
    ).astype(prefix_key.dtype)
    local_keys, local_values = (
        jnp.einsum("pjs,sqkd->pkjqd", slot_pick, pages, preferred_element_type=jnp.float32)
        .astype(pages.dtype)
        .reshape(prompts, kv_heads, -1, head_depth)
        for pages in (prefix_key, prefix_value)
    )
    span_rows = (
        span_query.reshape(prompts, span_dev, kv_heads, group_size, head_depth)
        .transpose(0, 2, 1, 3, 4)
        .reshape(head_batch, span_dev * group_size, head_depth)
    )
    ctx_count = sample_prompt.shape[0] // samples_dev
    span_pair = ctx_gather(jnp.stack([span_key, span_value]), ctx_count, axis=2)
    span_keys_all, span_values_all = span_pair[0], span_pair[1]
    span_total = span_keys_all.shape[1]
    span_key_rows = span_keys_all.transpose(0, 2, 1, 3).reshape(head_batch, span_total, head_depth)
    span_value_rows = span_values_all.transpose(0, 2, 1, 3).reshape(
        head_batch, span_total, head_depth
    )
    query_pos = (
        ctx_index * span_dev + jnp.arange(span_dev * group_size, dtype=jnp.int32) // group_size
    )
    causal = (jnp.arange(span_total, dtype=jnp.int32)[None, :] <= query_pos[:, None])[None]
    decode_five = decode_query.reshape(
        steps_count, samples_dev, kv_heads, group_size, head_depth
    ).transpose(2, 0, 1, 3, 4)
    prefill_state = empty_state(head_batch, span_dev * group_size, head_depth)
    own_pages = (local_keys, local_values)
    core_pairs = [(dev, dev ^ 1) for dev in range(ctx_count)]
    x_pairs = [
        [(dev, (dev - 2 * shift) % ctx_count) for dev in range(ctx_count)]
        for shift in range(1, ctx_count // 2)
    ]
    keys_x = [lax.ppermute(local_keys, "ctx", pairs) for pairs in x_pairs]
    values_after_keys, keys_x = lax.optimization_barrier((local_values, keys_x))
    values_x = [lax.ppermute(values_after_keys, "ctx", pairs) for pairs in x_pairs]
    along_x = list(zip(keys_x, values_x))
    near = [own_pages, lax.ppermute(own_pages, "ctx", core_pairs)]
    far = along_x + [lax.ppermute(pages, "ctx", core_pairs) for pages in along_x]
    decode_flat = decode_five.reshape(kv_heads, -1, head_depth)
    decode_batch = jnp.broadcast_to(decode_flat[None], (prompts,) + decode_flat.shape).reshape(
        head_batch, -1, head_depth
    )
    decode_state = empty_state(head_batch, decode_flat.shape[1], head_depth)
    for group in (near, far):
        key_rows, value_rows = (
            jnp.concatenate([pages[member] for pages in group], axis=2).reshape(
                head_batch, -1, head_depth
            )
            for member in range(2)
        )
        prefill_state = absorb(prefill_state, span_rows, key_rows, value_rows, None)
        decode_state = absorb(decode_state, decode_batch, key_rows, value_rows, None)
    decode_state = sweep(decode_state, decode_batch, span_key_rows, span_value_rows, span_total)
    own_prompts = lax.dynamic_slice_in_dim(sample_prompt, ctx_index * samples_dev, samples_dev)
    chosen = (
        own_prompts[None, None, None, :, None]
        == jnp.arange(prompts, dtype=jnp.int32)[:, None, None, None, None]
    )

    def select_prompt(member):
        shaped = member.reshape(
            (prompts, kv_heads, steps_count, samples_dev, group_size) + member.shape[2:]
        )
        select_mask = chosen.reshape(chosen.shape + (1,) * (shaped.ndim - 5))
        return jnp.sum(jnp.where(select_mask, shaped, 0.0), axis=0)

    decode_state = tuple((select_prompt(member) for member in decode_state))
    prefill_state = absorb(prefill_state, span_rows, span_key_rows, span_value_rows, causal)
    span_mixed = (prefill_state[2] / prefill_state[1][..., None]).astype(jnp.bfloat16)
    span_attn = (
        span_mixed.reshape(prompts, kv_heads, span_dev, group_size, head_depth)
        .transpose(0, 2, 1, 3, 4)
        .reshape(prompts, span_dev, heads_dev * head_depth)
    )
    span_rows_all = ctx_gather(span_attn, ctx_count, axis=1)
    span_partial = jnp.dot(
        span_rows_all.reshape(-1, span_rows_all.shape[-1]), out_weight, preferred_element_type=jnp.float32
    )
    decode_mixed = own_steps(decode_state, decode_five, decode_key, decode_value)
    decode_attn = decode_mixed.transpose(1, 2, 0, 3, 4).reshape(
        steps_count, samples_dev, heads_dev * head_depth
    )
    decode_rows_all = ctx_gather(decode_attn, ctx_count, axis=1)
    decode_partial = jnp.dot(
        decode_rows_all.reshape(-1, decode_rows_all.shape[-1]), out_weight, preferred_element_type=jnp.float32
    )
    summed = head_sum_line((span_partial, decode_partial), head_count)
    span_block = span_partial.shape[0] // head_count
    span_out = summed[:, :span_block].reshape(span_rows_all.shape[:-1] + (-1,))
    decode_out = summed[:, span_block:].reshape(decode_rows_all.shape[:-1] + (-1,))
    return (span_out, decode_out)


def solution(mesh):
    return jax.shard_map(
        functools.partial(shards, head_count=mesh.shape["head"]),
        mesh=mesh,
        in_specs=(
            P("groups", "ctx", "head", None),
            P("groups", "ctx", "head", None),
            P("groups", "ctx", "head", None),
            P(("groups", "ctx"), None, "head", None),
            P(("groups", "ctx"), None, "head", None),
            P("groups", "ctx"),
            P("groups", "ctx", "head", None),
            P("groups", "ctx", "head", None),
            P("groups", "ctx", "head", None),
            P("groups"),
            P("head", "ctx"),
        ),
        out_specs=(P("groups", None, "ctx"), P("groups", None, "ctx")),
        check_vma=False,
    )
```

```python
import functools
import math

import jax
import jax.numpy as jnp
from jax import lax
from jax.sharding import PartitionSpec as P

negative_floor = -1e30


def absorb(softmax_state, queries, key_rows, value_rows, allowed):
    running_max, running_sum, weighted = softmax_state
    scores = jnp.einsum("brd,bnd->brn", queries, key_rows, preferred_element_type=jnp.float32) * (
        1.0 / math.sqrt(queries.shape[-1])
    )
    if allowed is not None:
        scores = jnp.where(allowed, scores, negative_floor)
    new_max = jnp.maximum(running_max, jnp.max(scores, axis=-1))
    factor = jnp.exp(running_max - new_max)
    weights = jnp.exp(scores - new_max[..., None])
    running_sum = running_sum * factor + jnp.sum(weights, axis=-1)
    weighted = weighted * factor[..., None] + jnp.einsum(
        "brn,bnd->brd", weights.astype(jnp.bfloat16), value_rows, preferred_element_type=jnp.float32
    )
    return (new_max, running_sum, weighted)


def sweep(softmax_state, queries, key_rows, value_rows, block_width):
    total_keys = key_rows.shape[1]
    block_width = math.gcd(total_keys, block_width)

    def one_block(state_in, block_start):
        key_block = lax.dynamic_slice_in_dim(key_rows, block_start, block_width, 1)
        value_block = lax.dynamic_slice_in_dim(value_rows, block_start, block_width, 1)
        return (absorb(state_in, queries, key_block, value_block, None), None)

    starts = jnp.arange(total_keys // block_width, dtype=jnp.int32) * block_width
    softmax_state, unused = lax.scan(one_block, softmax_state, starts)
    return softmax_state


def empty_state(head_batch, row_count, head_depth):
    return (
        jnp.full((head_batch, row_count), negative_floor, jnp.float32),
        jnp.zeros((head_batch, row_count), jnp.float32),
        jnp.zeros((head_batch, row_count, head_depth), jnp.float32),
    )


def own_steps(softmax_state, queries_five, own_key, own_value):
    running_max, running_sum, weighted = softmax_state
    key_rows = own_key.transpose(2, 1, 0, 3)
    value_rows = own_value.transpose(2, 1, 0, 3)
    scores = jnp.einsum(
        "ktsgd,ksud->ktsgu", queries_five, key_rows, preferred_element_type=jnp.float32
    ) * (1.0 / math.sqrt(queries_five.shape[-1]))
    step_total = queries_five.shape[1]
    step_ids = jnp.arange(step_total, dtype=jnp.int32)
    allowed = (step_ids[None, :] <= step_ids[:, None])[None, :, None, None, :]
    scores = jnp.where(allowed, scores, negative_floor)
    new_max = jnp.maximum(running_max, jnp.max(scores, axis=-1))
    factor = jnp.exp(running_max - new_max)
    weights = jnp.exp(scores - new_max[..., None])
    running_sum = running_sum * factor + jnp.sum(weights, axis=-1)
    weighted = weighted * factor[..., None] + jnp.einsum(
        "ktsgu,ksud->ktsgd",
        weights.astype(jnp.bfloat16),
        value_rows,
        preferred_element_type=jnp.float32,
    )
    return (weighted / running_sum[..., None]).astype(jnp.bfloat16)


def ctx_shards(block, ctx_count):
    chips = ctx_count // 2
    received = [block]
    for shift in range(1, chips):
        pairs = [(dev, (dev - 2 * shift) % ctx_count) for dev in range(ctx_count)]
        received.append(lax.ppermute(block, "ctx", pairs))
    along_x = jnp.stack(received)
    other_core = lax.ppermute(along_x, "ctx", [(dev, dev ^ 1) for dev in range(ctx_count)])
    return along_x, other_core


def ctx_gather(block, ctx_count, axis=0):
    ctx_index = lax.axis_index("ctx")
    chip, core = ctx_index // 2, ctx_index % 2
    along_x, other_core = ctx_shards(block, ctx_count)
    along_x = jnp.roll(along_x, chip, axis=0)
    other_core = jnp.roll(other_core, chip, axis=0)
    core_zero = jnp.where(core == 0, along_x, other_core)
    core_one = jnp.where(core == 0, other_core, along_x)
    joined = jnp.moveaxis(jnp.stack([core_zero, core_one], axis=1), (0, 1), (axis, axis + 1))
    return joined.reshape(block.shape[:axis] + (-1,) + block.shape[axis + 1 :])


def head_sum_line(partials, head_count):
    last = head_count - 1
    head_index = lax.axis_index("head")
    pieces = [part.reshape((head_count, -1) + part.shape[1:]) for part in partials]

    def take_block(index):
        return jnp.concatenate(
            [lax.dynamic_index_in_dim(piece, index, 0, False) for piece in pieces], axis=0
        )

    rightward = [(dev, dev + 1) for dev in range(last)]
    leftward = [(dev + 1, dev) for dev in range(last)]
    from_left = from_right = None
    for step in range(1, head_count):
        right_block = jnp.clip(head_index + head_count - step, 0, last)
        left_block = jnp.clip(head_index - head_count + step, 0, last)
        going_right = take_block(right_block)
        going_left = take_block(left_block)
        if from_left is not None:
            going_right = going_right + from_left.astype(jnp.float32)
            going_left = going_left + from_right.astype(jnp.float32)
        from_left = lax.ppermute(going_right.astype(jnp.bfloat16), "head", rightward)
        from_right = lax.ppermute(going_left.astype(jnp.bfloat16), "head", leftward)
    own = take_block(head_index)
    mine = (own + from_left.astype(jnp.float32) + from_right.astype(jnp.float32)).astype(jnp.bfloat16)
    lefts, rights = [], []
    send_right = send_left = mine
    for step in range(1, head_count):
        send_right = lax.ppermute(send_right, "head", rightward)
        send_left = lax.ppermute(send_left, "head", leftward)
        lefts.append(send_right)
        rights.append(send_left)
    candidates = jnp.stack([mine] + lefts + rights)
    wanted = jnp.arange(head_count, dtype=jnp.int32)
    pick = jnp.where(
        wanted == head_index,
        0,
        jnp.where(wanted < head_index, head_index - wanted, last + wanted - head_index),
    )
    return jnp.take(candidates, pick, axis=0)


def shards(
    span_query,
    span_key,
    span_value,
    prefix_key,
    prefix_value,
    page_table,
    decode_query,
    decode_key,
    decode_value,
    sample_prompt,
    out_weight,
    head_count,
):
    prompts, span_dev, heads_dev, head_depth = span_query.shape
    kv_heads = span_key.shape[2]
    group_size = heads_dev // kv_heads
    steps_count = decode_query.shape[0]
    samples_dev = decode_query.shape[1]
    head_batch = prompts * kv_heads
    ctx_index = lax.axis_index("ctx")
    slot_pick = (
        page_table[:, :, None] == jnp.arange(prefix_key.shape[0], dtype=jnp.int32)
    ).astype(prefix_key.dtype)
    local_keys, local_values = (
        jnp.einsum("pjs,sqkd->pkjqd", slot_pick, pages, preferred_element_type=jnp.float32)
        .astype(pages.dtype)
        .reshape(prompts, kv_heads, -1, head_depth)
        for pages in (prefix_key, prefix_value)
    )
    span_rows = (
        span_query.reshape(prompts, span_dev, kv_heads, group_size, head_depth)
        .transpose(0, 2, 1, 3, 4)
        .reshape(head_batch, span_dev * group_size, head_depth)
    )
    ctx_count = sample_prompt.shape[0] // samples_dev
    span_pair = ctx_gather(jnp.stack([span_key, span_value]), ctx_count, axis=2)
    span_keys_all, span_values_all = span_pair[0], span_pair[1]
    span_total = span_keys_all.shape[1]
    span_key_rows = span_keys_all.transpose(0, 2, 1, 3).reshape(head_batch, span_total, head_depth)
    span_value_rows = span_values_all.transpose(0, 2, 1, 3).reshape(
        head_batch, span_total, head_depth
    )
    query_pos = (
        ctx_index * span_dev + jnp.arange(span_dev * group_size, dtype=jnp.int32) // group_size
    )
    causal = (jnp.arange(span_total, dtype=jnp.int32)[None, :] <= query_pos[:, None])[None]
    decode_five = decode_query.reshape(
        steps_count, samples_dev, kv_heads, group_size, head_depth
    ).transpose(2, 0, 1, 3, 4)
    prefill_state = empty_state(head_batch, span_dev * group_size, head_depth)
    own_pages = (local_keys, local_values)
    core_pairs = [(dev, dev ^ 1) for dev in range(ctx_count)]
    x_pairs = [
        [(dev, (dev - 2 * shift) % ctx_count) for dev in range(ctx_count)]
        for shift in range(1, ctx_count // 2)
    ]
    keys_x = [lax.ppermute(local_keys, "ctx", pairs) for pairs in x_pairs]
    values_after_keys, keys_x = lax.optimization_barrier((local_values, keys_x))
    values_x = [lax.ppermute(values_after_keys, "ctx", pairs) for pairs in x_pairs]
    along_x = list(zip(keys_x, values_x))
    near = [own_pages, lax.ppermute(own_pages, "ctx", core_pairs)]
    forwarded = [lax.ppermute(pages, "ctx", core_pairs) for pages in along_x]
    decode_flat = decode_five.reshape(kv_heads, -1, head_depth)
    decode_batch = jnp.broadcast_to(decode_flat[None], (prompts,) + decode_flat.shape).reshape(
        head_batch, -1, head_depth
    )
    decode_state = empty_state(head_batch, decode_flat.shape[1], head_depth)
    for group in (near, along_x, forwarded):
        key_rows, value_rows = (
            jnp.concatenate([pages[member] for pages in group], axis=2).reshape(
                head_batch, -1, head_depth
            )
            for member in range(2)
        )
        prefill_state = absorb(prefill_state, span_rows, key_rows, value_rows, None)
        decode_state = absorb(decode_state, decode_batch, key_rows, value_rows, None)
    decode_state = sweep(decode_state, decode_batch, span_key_rows, span_value_rows, span_total)
    own_prompts = lax.dynamic_slice_in_dim(sample_prompt, ctx_index * samples_dev, samples_dev)
    chosen = (
        own_prompts[None, None, None, :, None]
        == jnp.arange(prompts, dtype=jnp.int32)[:, None, None, None, None]
    )

    def select_prompt(member):
        shaped = member.reshape(
            (prompts, kv_heads, steps_count, samples_dev, group_size) + member.shape[2:]
        )
        select_mask = chosen.reshape(chosen.shape + (1,) * (shaped.ndim - 5))
        return jnp.sum(jnp.where(select_mask, shaped, 0.0), axis=0)

    decode_state = tuple((select_prompt(member) for member in decode_state))
    prefill_state = absorb(prefill_state, span_rows, span_key_rows, span_value_rows, causal)
    span_mixed = (prefill_state[2] / prefill_state[1][..., None]).astype(jnp.bfloat16)
    span_attn = (
        span_mixed.reshape(prompts, kv_heads, span_dev, group_size, head_depth)
        .transpose(0, 2, 1, 3, 4)
        .reshape(prompts, span_dev, heads_dev * head_depth)
    )
    span_rows_all = ctx_gather(span_attn, ctx_count, axis=1)
    span_partial = jnp.dot(
        span_rows_all.reshape(-1, span_rows_all.shape[-1]), out_weight, preferred_element_type=jnp.float32
    )
    decode_mixed = own_steps(decode_state, decode_five, decode_key, decode_value)
    decode_attn = decode_mixed.transpose(1, 2, 0, 3, 4).reshape(
        steps_count, samples_dev, heads_dev * head_depth
    )
    decode_rows_all = ctx_gather(decode_attn, ctx_count, axis=1)
    decode_partial = jnp.dot(
        decode_rows_all.reshape(-1, decode_rows_all.shape[-1]), out_weight, preferred_element_type=jnp.float32
    )
    summed = head_sum_line((span_partial, decode_partial), head_count)
    span_block = span_partial.shape[0] // head_count
    span_out = summed[:, :span_block].reshape(span_rows_all.shape[:-1] + (-1,))
    decode_out = summed[:, span_block:].reshape(decode_rows_all.shape[:-1] + (-1,))
    return (span_out, decode_out)


def solution(mesh):
    return jax.shard_map(
        functools.partial(shards, head_count=mesh.shape["head"]),
        mesh=mesh,
        in_specs=(
            P("groups", "ctx", "head", None),
            P("groups", "ctx", "head", None),
            P("groups", "ctx", "head", None),
            P(("groups", "ctx"), None, "head", None),
            P(("groups", "ctx"), None, "head", None),
            P("groups", "ctx"),
            P("groups", "ctx", "head", None),
            P("groups", "ctx", "head", None),
            P("groups", "ctx", "head", None),
            P("groups"),
            P("head", "ctx"),
        ),
        out_specs=(P("groups", None, "ctx"), P("groups", None, "ctx")),
        check_vma=False,
    )
```
